32 devices in a mesh: fsdp: 8 (over y, x, core), tp: 4 (over z).
Axes of the slice: x: 2, y: 2, z: 4, core: 2. Of those that a mesh axis runs over, the one named last changes fastest.
Arguments:
- layer_in: bfloat16 [8192, 2048], P(('fsdp', 'tp')), may hold values from -8 to 8
- query_proj: bfloat16 [2048, 4096], P('fsdp', 'tp'), may hold values from -0.125 to 0.125
- key_proj: bfloat16 [2048, 512], P(('fsdp', 'tp')), may hold values from -0.125 to 0.125
- value_proj: bfloat16 [2048, 512], P(('fsdp', 'tp')), may hold values from -0.125 to 0.125
- output_proj: bfloat16 [4096, 2048], P('tp', 'fsdp'), may hold values from -0.75 to 0.75
- attn_gain: bfloat16 [2048], P(('fsdp', 'tp')), may hold values from 0.25 to 1.75
- query_gain: bfloat16 [128], P(('fsdp', 'tp')), may hold values from 0.25 to 1.75
- key_gain: bfloat16 [128], P(('fsdp', 'tp')), may hold values from 0.25 to 1.75
- ffn_gain: bfloat16 [2048], P(('fsdp', 'tp')), may hold values from 0.25 to 1.75
- expert_gate: bfloat16 [16, 2048, 768], P('fsdp', None, 'tp'), may hold values from -0.125 to 0.125
- expert_up: bfloat16 [16, 2048, 768], P('fsdp', None, 'tp'), may hold values from -0.125 to 0.125
- expert_down: bfloat16 [16, 768, 2048], P('fsdp', 'tp'), may hold values from -0.21875 to 0.21875
- routes: int32 [8192, 8], P('fsdp'), may hold values from 0 to 15, all different within a row; in each aligned block of 1024 rows (0 to 1023, 1024 to 2047, ...) at most 576 rows name the same one
- route_weights: float32 [8192, 8], P('fsdp'), may hold values from 0.05 to 0.3
- prefix_len: int32 [8], P('fsdp'), may hold values from 1 to 512
- out_grad: bfloat16 [8192, 2048], P(('fsdp', 'tp')), may hold values from -12 to 12
Outputs:
- layer_out: bfloat16 [8192, 2048], P(('fsdp', 'tp'))
- in_grad: float32 [8192, 2048], P(('fsdp', 'tp'))
- query_proj_grad: float32 [2048, 4096], P('fsdp', 'tp')
- key_proj_grad: float32 [2048, 512], P(('fsdp', 'tp'))
- value_proj_grad: float32 [2048, 512], P(('fsdp', 'tp'))
- output_proj_grad: float32 [4096, 2048], P('tp', 'fsdp')
- attn_gain_grad: float32 [2048], P(('fsdp', 'tp'))
- query_gain_grad: float32 [128], P(('fsdp', 'tp'))
- key_gain_grad: float32 [128], P(('fsdp', 'tp'))
- ffn_gain_grad: float32 [2048], P(('fsdp', 'tp'))
- gate_grad: float32 [16, 2048, 768], P('fsdp', None, 'tp')
- up_grad: float32 [16, 2048, 768], P('fsdp', None, 'tp')
- down_grad: float32 [16, 768, 2048], P('fsdp', 'tp')
The draws below stay inside these ranges and needn't reach their ends.
Inputs may be any that keep to these rules, and one draw needn't show every extreme that they name: `routes`: the 8 experts of a token differ. Within each aligned block of 1024 rows (the tokens of one index of fsdp) no expert is chosen by more than 576 tokens, and in every draw some expert of some block is chosen by exactly 576.
All inputs are finite; a program needn't handle non-finite values.
Results may differ from the reference program's by a relative error of at most 0.019.
Values may be sent and summed in bfloat16 or wider, within the bound.
No kernel may reach another device: no remote copies, remote signals or barrier semaphores. Data moves between devices by JAX's collectives and lax.ppermute only.
A program may use at most 448 MiB of HBM per device.

```python
import math
import jax
import jax.numpy as jnp
import numpy as np
from jax import lax

D = 2048
HQ = 32
HK = 4
HD = 128
FE = 768
TOP = 8
SEQ = 1024
EXPERTS = 16
GROUP = 1024
TOKENS = 8192
NSEQ = 8
CAP = 576
N_TP = 4


def scaled_rows(key, rising_factor, clip_bound):
    first_key, second_key, third_key = jax.random.split(key, 3)
    base = jax.random.normal(first_key, (TOKENS, D), jnp.float32)
    row_scale = jnp.exp(jax.random.uniform(second_key, (TOKENS, 1), jnp.float32, math.log(0.5), math.log(2.0)))
    column_scale = jnp.exp(jax.random.uniform(third_key, (1, D), jnp.float32, math.log(0.5), math.log(2.0)))
    rising = 1.0 + rising_factor * jnp.arange(TOKENS, dtype=jnp.float32)[:, None] / TOKENS
    values = base * column_scale * row_scale * rising
    return jnp.clip(values, -clip_bound, clip_bound)


def draw_layer_in(key, part):
    return scaled_rows(jax.random.fold_in(key, 11), 0.0, 8.0).astype(jnp.bfloat16)


def draw_out_grad(key, part):
    return scaled_rows(jax.random.fold_in(key, 23), 2.0, 12.0).astype(jnp.bfloat16)


def with_ends(values, key, least, largest):
    longest = values.shape.index(max(values.shape))
    spots = []
    for shift in (0, 1):
        where = [jax.random.randint(jax.random.fold_in(key, axis), (), 0, length) for axis, length in enumerate(values.shape)]
        where[longest] = (where[longest] + shift) % values.shape[longest]
        spots.append(tuple(where))
    return values.at[spots[0]].set(least).at[spots[1]].set(largest)


def shard_levels(rng, extent, cuts, least, top_value):
    loudness = 1.0
    for dim, shards_of in cuts:
        steps = jax.random.uniform(jax.random.fold_in(jax.random.fold_in(rng, 6), dim), (shards_of,), jnp.float32, least / len(cuts), top_value / len(cuts))
        loudness = loudness * jnp.repeat(jnp.exp(steps), extent[dim] // shards_of).reshape((-1,) + (1,) * (len(extent) - 1 - dim))
    return loudness


def shared_out(key, own, number, rows, count, top, bound, lean):
    sequence = jax.random.permutation(key, count)
    crowded, ordinary = load_shares(count, rows * top, bound, lean, True), load_shares(count, rows * top, bound, lean, False)
    places = jnp.arange(count)

    def named(sizes, offset_by):
        used = int((sizes > 0).sum())
        fixed = max(1, used // 4)
        moved = fixed + (places - fixed + offset_by * (used - fixed)) % max(1, count - fixed)
        return jnp.zeros((count,), jnp.int32).at[sequence[jnp.where(places < fixed, places, moved)]].set(jnp.asarray(sizes, jnp.int32))

    sizes = jnp.where(number % 4 == 0, named(crowded, number // 4), named(ordinary, number - number // 4 - 1))
    mixed = jax.random.permutation(jax.random.fold_in(own, 3), count)
    donor, receiver = mixed[0:count // 2 * 2:2], mixed[1:count // 2 * 2:2]
    slack = jnp.minimum(sizes[donor] - 1, bound - sizes[receiver]) // 2
    slack = jnp.where((donor == sequence[0]) | (receiver == sequence[0]) | (sizes[receiver] == 0), 0, jnp.maximum(slack, 0))
    moved = jax.random.randint(jax.random.fold_in(own, 4), (count // 2,), 0, 1 << 20) % (slack + 1)
    sizes = sizes.at[donor].add(-moved).at[receiver].add(moved)
    labels = jnp.searchsorted(jnp.cumsum(sizes), jnp.arange(rows * top), side="right").astype(jnp.int32)
    listing = labels.reshape(top, rows).T
    listing = listing[jax.random.permutation(jax.random.fold_in(own, 1), rows)]
    offset_by = jax.random.randint(jax.random.fold_in(own, 2), (rows, 1), 0, top)
    return jnp.take_along_axis(listing, (jnp.arange(top)[None, :] + offset_by) % top, axis=1)


def load_shares(amount, total, most, slope, full):
    loads = [(1 << 20) // math.isqrt(grade ** slope) + 1 for grade in range(1, amount + 1)]
    largest = most if full else min(most, max(-(-total // amount), total * loads[0] // sum(loads)))
    least = 1 if total - largest >= amount - 1 else 0
    holding, rest = [largest] + [least] * (amount - 1), total - largest - least * (amount - 1)
    while rest > 0:
        candidates = [i for i in range(1, amount) if holding[i] < largest] or [i for i in range(1, amount) if holding[i] < most]
        pool, remaining = sum([loads[i] for i in candidates]), rest
        for i in candidates:
            addition = min(most - holding[i], max(1, remaining * loads[i] // pool), rest)
            holding[i] = holding[i] + addition
            rest = rest - addition
    return np.array(holding)


def gaussian(own_key, extent, scale, reach, cuts=(), held_as=jnp.bfloat16):
    values = scale * jax.random.normal(own_key, extent, jnp.float32)
    if cuts:
        values = values * shard_levels(own_key, extent, cuts, -0.22, 0.18)
    return jnp.clip(values, -reach, reach).astype(held_as)


def setup_inputs(seed: int = 0) -> dict:
    arg_keys = jax.random.split(jax.random.key(seed), 17)
    layer_in = draw_layer_in(jax.random.fold_in(arg_keys[16], 71), 0)
    query_proj = gaussian(arg_keys[1], (D, HQ * HD), D ** -0.5, 0.125, ((0, 8), (1, 4)))
    key_proj = gaussian(arg_keys[2], (D, HK * HD), D ** -0.5, 0.125, ((0, 32),))
    value_proj = gaussian(arg_keys[3], (D, HK * HD), D ** -0.5, 0.125, ((0, 32),))
    output_proj = gaussian(arg_keys[4], (HQ * HD, D), (HQ * HD // 64) ** -0.5, 0.75, ((0, 4), (1, 8)))
    attn_gain = jnp.clip(1.0 + 0.15 * jax.random.normal(arg_keys[5], (D,), jnp.float32), 0.25, 1.75).astype(jnp.bfloat16)
    query_gain = jnp.clip(1.0 + 0.15 * jax.random.normal(arg_keys[6], (HD,), jnp.float32), 0.25, 1.75).astype(jnp.bfloat16)
    key_gain = jnp.clip(1.0 + 0.15 * jax.random.normal(arg_keys[7], (HD,), jnp.float32), 0.25, 1.75).astype(jnp.bfloat16)
    ffn_gain = jnp.clip(1.0 + 0.15 * jax.random.normal(arg_keys[8], (D,), jnp.float32), 0.25, 1.75).astype(jnp.bfloat16)
    expert_gate = gaussian(arg_keys[9], (EXPERTS, D, FE), D ** -0.5, 0.125, ((0, 8), (2, 4)))
    expert_up = gaussian(arg_keys[10], (EXPERTS, D, FE), D ** -0.5, 0.125, ((0, 8), (2, 4)))
    expert_down = gaussian(arg_keys[11], (EXPERTS, FE, D), FE ** -0.5, 0.21875, ((0, 8), (1, 4)))
    routes_keys = jax.random.split(jax.random.fold_in(arg_keys[12], 1), TOKENS // GROUP)
    routes_turns = jax.random.permutation(jax.random.fold_in(arg_keys[12], 3), TOKENS // GROUP)
    routes = jax.vmap(lambda own, number: shared_out(jax.random.fold_in(arg_keys[12], 2), own, number, GROUP, EXPERTS, TOP, CAP, 0))(routes_keys, routes_turns).reshape((TOKENS, TOP))
    route_weights = jnp.clip(jnp.exp(math.log(0.3) - 1.7917595 * jax.random.uniform(arg_keys[13], (TOKENS, TOP), jnp.float32) ** shard_levels(arg_keys[13], (TOKENS, TOP), ((0, 8),), -0.2, 0.2)), 0.05, 0.3)
    prefix_len = with_ends(jax.random.randint(arg_keys[14], (NSEQ,), 1, SEQ // 2 + 1), jax.random.fold_in(arg_keys[14], 1), 1, (SEQ // 2 + 1) - 1).astype(jnp.int32)
    out_grad = draw_out_grad(jax.random.fold_in(arg_keys[16], 71), 0)
    return dict(layer_in=layer_in, query_proj=query_proj, key_proj=key_proj, value_proj=value_proj, output_proj=output_proj, attn_gain=attn_gain, query_gain=query_gain, key_gain=key_gain, ffn_gain=ffn_gain, expert_gate=expert_gate, expert_up=expert_up, expert_down=expert_down, routes=routes, route_weights=route_weights, prefix_len=prefix_len, out_grad=out_grad)


EPSILON = 1e-06
PRECISE = lax.Precision.HIGHEST

@jax.custom_vjp
def low(v):
    return lax.optimization_barrier(v.astype(jnp.bfloat16)).astype(jnp.float32)

@jax.custom_vjp
def low_back(v):
    return v

def low_keep(v):
    return (low(v), None)

def low_pass(kept, grad):
    return (grad,)

def back_keep(v):
    return (v, None)

def back_low(kept, grad):
    return (low(grad),)
low.defvjp(low_keep, low_pass)
low_back.defvjp(back_keep, back_low)

def rms_norm(values, weight):
    return values * lax.rsqrt(lax.optimization_barrier(jnp.mean(values * values, axis=-1, keepdims=True)) + EPSILON) * weight

def rotate(values, cosine, sine):
    half_width = values.shape[-1] // 2
    first_half = values[..., :half_width]
    second_half = values[..., half_width:]
    return jnp.concatenate([first_half * cosine - second_half * sine, second_half * cosine + first_half * sine], axis=-1)

def rotary_tables(positions, width):
    half_width = width // 2
    inverse = jnp.exp(-math.log(1000000.0) * 2.0 * jnp.arange(half_width, dtype=jnp.float32) / width)
    angles = positions[:, None] * inverse[None, :]
    return (jnp.cos(angles), jnp.sin(angles))

def matmul_high(left, right):
    return jnp.dot(left, right, precision=PRECISE)

def attend(operands):
    queries, keys_rep, values_rep, prefix_end = operands
    scores = low_back(jnp.einsum('qhd,khd->hqk', queries, keys_rep, precision=PRECISE) * (1.0 / math.sqrt(HD)))
    position = jnp.arange(SEQ, dtype=jnp.int32)
    allowed = (position[None, :] <= position[:, None]) | (position[None, :] < prefix_end)
    scores = jnp.where(allowed[None], scores, -1e+30)
    attn_probs = low(jax.nn.softmax(scores, axis=-1))
    return jnp.einsum('hqk,khd->qhd', attn_probs, values_rep, precision=PRECISE)

def forward_block(params, tokens_in, route_ids, route_share, prefix_ends):
    query_w, key_w, value_w, out_w, gain_attn, gain_query, gain_key, gain_ffn, gate_w, up_w, down_w = params
    row_count = tokens_in.shape[0]
    seq_count = row_count // SEQ
    per_group = HQ // N_TP
    attn_in = low(rms_norm(tokens_in, gain_attn))
    query_raw = low_back(matmul_high(attn_in, query_w)).reshape(seq_count, SEQ, HQ, HD)
    copy_heads = jnp.arange(N_TP, dtype=jnp.int32) * per_group // (HQ // HK)
    key_all = matmul_high(attn_in, key_w).reshape(seq_count, SEQ, HK, HD)
    value_all = matmul_high(attn_in, value_w).reshape(seq_count, SEQ, HK, HD)
    key_copy = low_back(jnp.take(key_all, copy_heads, axis=2))
    value_copy = low(low_back(jnp.take(value_all, copy_heads, axis=2)))
    cosine, sine = rotary_tables(jnp.arange(SEQ, dtype=jnp.float32), HD)
    cosine = cosine[:, None, :]
    sine = sine[:, None, :]
    query_norm = low(rotate(rms_norm(query_raw, gain_query), cosine, sine))
    key_norm = low(rotate(rms_norm(key_copy, gain_key), cosine, sine))
    keys_rep = jnp.repeat(key_norm, per_group, axis=2)
    values_rep = jnp.repeat(value_copy, per_group, axis=2)
    context = lax.map(jax.checkpoint(attend), (query_norm, keys_rep, values_rep, prefix_ends))
    context = low(low_back(context)).reshape(row_count, HQ * HD)
    attn_out = low_back(matmul_high(context, out_w))
    residual = tokens_in + attn_out
    ffn_in = low(rms_norm(residual, gain_ffn))
    chosen = (route_ids[:, :, None] == jnp.arange(EXPERTS, dtype=jnp.int32)[None, None, :]).astype(jnp.float32)
    shares = lax.optimization_barrier(jnp.sum(route_share[:, :, None] * chosen, axis=1))

    def expert_step(carried, operands):
        gate_e, up_e, down_e, share_e = operands
        gate_val = low_back(matmul_high(ffn_in, gate_e))
        up_val = low_back(matmul_high(ffn_in, up_e))
        hidden = low(jax.nn.silu(gate_val) * up_val)
        expert_out = low_back(matmul_high(hidden, down_e))
        return (carried + share_e[:, None] * expert_out, None)
    mixture, _ = lax.scan(jax.checkpoint(expert_step), jnp.zeros_like(residual), (gate_w, up_w, down_w, shares.T))
    return residual + low_back(mixture)

def reference(layer_in, query_proj, key_proj, value_proj, output_proj, attn_gain, query_gain, key_gain, ffn_gain, expert_gate, expert_up, expert_down, routes, route_weights, prefix_len, out_grad):
    params = (query_proj.astype(jnp.float32), key_proj.astype(jnp.float32), value_proj.astype(jnp.float32), output_proj.astype(jnp.float32), attn_gain.astype(jnp.float32), query_gain.astype(jnp.float32), key_gain.astype(jnp.float32), ffn_gain.astype(jnp.float32), expert_gate.astype(jnp.float32), expert_up.astype(jnp.float32), expert_down.astype(jnp.float32))
    block_rows = math.gcd(TOKENS, SEQ * max(1, 4096 // SEQ))
    block_count = TOKENS // block_rows

    def block_step(accum, operands):
        tokens_in, route_ids, route_share, prefix_ends, cotangent = operands

        def forward_only(inputs_f, weights_f):
            return forward_block(weights_f, inputs_f, route_ids, route_share, prefix_ends)
        result, backward = jax.vjp(forward_only, tokens_in, params)
        in_part, weight_parts = backward(cotangent)
        accum = jax.tree.map(lambda left, right: left + right, accum, weight_parts)
        return (accum, (result.astype(jnp.bfloat16), in_part))
    starting = jax.tree.map(jnp.zeros_like, params)
    operands = (layer_in.astype(jnp.float32).reshape(block_count, block_rows, D), routes.reshape(block_count, block_rows, TOP), route_weights.astype(jnp.float32).reshape(block_count, block_rows, TOP), prefix_len.reshape(block_count, block_rows // SEQ), out_grad.astype(jnp.float32).reshape(block_count, block_rows, D))
    grads, (outputs, in_grads) = lax.scan(block_step, starting, operands)
    return (outputs.reshape(TOKENS, D), in_grads.reshape(TOKENS, D), grads[0], grads[1], grads[2], grads[3], grads[4], grads[5], grads[6], grads[7], grads[8], grads[9], grads[10])
```

```python
import math

import jax
import jax.numpy as jnp
from jax import lax
from jax.sharding import PartitionSpec as P

HQ = 32
HK = 4
HD = 128
TOP = 8
SEQ = 1024


EPSILON = 1e-06


def rms_norm(values, weight):
    return values * lax.rsqrt(jnp.mean(values * values, axis=-1, keepdims=True) + EPSILON) * weight


def rotate(values, cosine, sine):
    half_width = values.shape[-1] // 2
    first_half = values[..., :half_width]
    second_half = values[..., half_width:]
    return jnp.concatenate(
        [first_half * cosine - second_half * sine, second_half * cosine + first_half * sine],
        axis=-1,
    )


def rotary_tables(positions, width):
    half_width = width // 2
    inverse = jnp.exp(
        -math.log(1000000.0) * 2.0 * jnp.arange(half_width, dtype=jnp.float32) / width
    )
    angles = positions[:, None] * inverse[None, :]
    return (jnp.cos(angles), jnp.sin(angles))


def masked_scores(queries, keys_b, prefix_end, factor):
    scores = jnp.einsum("qhd,kd->hqk", queries, keys_b, preferred_element_type=jnp.float32) * factor
    position = lax.iota(jnp.int32, queries.shape[0])
    allowed = (position[None, :] <= position[:, None]) | (position[None, :] < prefix_end)
    return jnp.where(allowed[None], scores, -1e30)


def body(
    layer_in,
    query_proj,
    key_proj,
    value_proj,
    output_proj,
    attn_gain,
    query_gain,
    key_gain,
    ffn_gain,
    expert_gate,
    expert_up,
    expert_down,
    routes,
    route_weights,
    prefix_len,
    out_grad,
):
    tok_rows = layer_in.shape[0]
    width = layer_in.shape[1]
    group_rows = tok_rows * lax.axis_size("tp")
    seq_count = group_rows // SEQ
    factor = 1.0 / math.sqrt(HD)
    gain_sizes = (attn_gain.shape[0], query_gain.shape[0], key_gain.shape[0], ffn_gain.shape[0])
    kv_rows, kv_width = key_proj.shape
    gain_row = jnp.concatenate([attn_gain, query_gain, key_gain, ffn_gain])
    gain_block = jnp.zeros((8, 2 * kv_width), jnp.bfloat16).at[0, : gain_row.shape[0]].set(gain_row)
    packed = jnp.concatenate(
        [jnp.concatenate([key_proj, value_proj], axis=1), gain_block], axis=0
    )
    packed_all = lax.all_gather(packed, ("fsdp", "tp"), axis=0, tiled=False)
    kv_all = packed_all[:, :kv_rows].reshape(-1, 2 * kv_width)
    key_all = kv_all[:, :kv_width]
    value_all = kv_all[:, kv_width:]
    gain_all = packed_all[:, kv_rows]
    gains = []
    offset = 0
    for size in gain_sizes:
        gains.append(gain_all[:, offset : offset + size].reshape(-1))
        offset += size
    gain_attn, gain_query, gain_key, gain_ffn = gains
    gain_attn = gain_attn.astype(jnp.float32)
    gain_query = gain_query.astype(jnp.float32)
    gain_key = gain_key.astype(jnp.float32)
    gain_ffn = gain_ffn.astype(jnp.float32)
    query_w, out_w, gate_w, up_w, down_w = (
        lax.all_gather(query_proj, "fsdp", axis=0, tiled=True),
        lax.all_gather(output_proj, "fsdp", axis=1, tiled=True),
        lax.all_gather(expert_gate, "fsdp", axis=0, tiled=True),
        lax.all_gather(expert_up, "fsdp", axis=0, tiled=True),
        lax.all_gather(expert_down, "fsdp", axis=0, tiled=True),
    )
    per_dev = query_w.shape[1] // HD
    kv_head = lax.axis_index("tp") * per_dev // (HQ // HK)
    key_w = lax.dynamic_slice_in_dim(key_all, kv_head * HD, HD, 1)
    value_w = lax.dynamic_slice_in_dim(value_all, kv_head * HD, HD, 1)
    tokens_f = layer_in.astype(jnp.float32)
    attn_in = rms_norm(tokens_f, gain_attn).astype(jnp.bfloat16)
    attn_rows = lax.all_gather(attn_in, "tp", axis=0, tiled=True)
    query_raw = jnp.dot(attn_rows, query_w, preferred_element_type=jnp.float32)
    key_raw = jnp.dot(attn_rows, key_w, preferred_element_type=jnp.float32)
    value_rows = jnp.dot(attn_rows, value_w, preferred_element_type=jnp.float32).astype(
        jnp.bfloat16
    )
    cosine, sine = rotary_tables((lax.iota(jnp.int32, group_rows) % SEQ).astype(jnp.float32), HD)

    def prepare(query_in, key_in, weight_query, weight_key):
        query_heads = rms_norm(query_in.reshape(group_rows, per_dev, HD), weight_query)
        return (
            rotate(query_heads, cosine[:, None, :], sine[:, None, :]),
            rotate(rms_norm(key_in, weight_key), cosine, sine),
        )

    (query_norm, key_norm), prepare_back = jax.vjp(
        prepare, query_raw, key_raw, gain_query, gain_key
    )
    query_seq = query_norm.astype(jnp.bfloat16).reshape(seq_count, SEQ, per_dev, HD)
    key_seq = key_norm.astype(jnp.bfloat16).reshape(seq_count, SEQ, HD)
    value_seq = value_rows.reshape(seq_count, SEQ, HD)

    def attend(operands):
        queries, keys_b, values_b, prefix_end = operands
        scores = masked_scores(queries, keys_b, prefix_end, factor)
        highest = jnp.max(scores, axis=-1, keepdims=True)
        expo = jnp.exp(scores - highest)
        denom = jnp.sum(expo, axis=-1, keepdims=True)
        attn_probs = (expo / denom).astype(jnp.bfloat16)
        context = jnp.einsum(
            "hqk,kd->qhd", attn_probs, values_b, preferred_element_type=jnp.float32
        )
        return (context, (highest + jnp.log(denom))[..., 0])

    context_all, log_sums = lax.map(attend, (query_seq, key_seq, value_seq, prefix_len))
    context_b = context_all.reshape(group_rows, per_dev * HD).astype(jnp.bfloat16)
    attn_out = lax.psum_scatter(
        jnp.dot(context_b, out_w, preferred_element_type=jnp.float32).astype(jnp.bfloat16),
        "tp",
        scatter_dimension=0,
        tiled=True,
    ).astype(jnp.float32)
    residual = tokens_f + attn_out
    ffn_in = rms_norm(residual, gain_ffn).astype(jnp.bfloat16)
    ffn_rows = lax.all_gather(ffn_in, "tp", axis=0, tiled=True)
    expert_count = gate_w.shape[0]
    chosen = routes[:, :, None] == lax.iota(jnp.int32, expert_count)[None, None, :]
    share = jnp.sum(jnp.where(chosen, route_weights[:, :, None], 0.0), axis=1)
    gate_val = jnp.einsum("td,edf->tef", ffn_rows, gate_w, preferred_element_type=jnp.float32)
    up_val = jnp.einsum("td,edf->tef", ffn_rows, up_w, preferred_element_type=jnp.float32)
    sigma = jax.nn.sigmoid(gate_val)
    active = gate_val * sigma
    hidden = (active * up_val).astype(jnp.bfloat16)
    hidden_share = (hidden.astype(jnp.float32) * share[:, :, None]).astype(jnp.bfloat16)
    mixture = jnp.einsum(
        "tef,efd->td", hidden_share, down_w, preferred_element_type=jnp.float32
    )
    mixture_own = lax.psum_scatter(
        mixture.astype(jnp.bfloat16), "tp", scatter_dimension=0, tiled=True
    ).astype(jnp.float32)
    layer_out = (residual + mixture_own).astype(jnp.bfloat16)
    grad_out = out_grad.astype(jnp.float32)
    grad_rows = lax.all_gather(out_grad, "tp", axis=0, tiled=True)
    hidden_grad = (
        jnp.einsum("td,efd->tef", grad_rows, down_w, preferred_element_type=jnp.float32)
        * share[:, :, None]
    )
    gate_back = (hidden_grad * up_val * sigma * (1.0 + gate_val * (1.0 - sigma))).astype(
        jnp.bfloat16
    )
    up_back = (hidden_grad * active).astype(jnp.bfloat16)
    ffn_in_grad = jnp.einsum(
        "tef,edf->td", gate_back, gate_w, preferred_element_type=jnp.float32
    ) + jnp.einsum("tef,edf->td", up_back, up_w, preferred_element_type=jnp.float32)
    gate_part = jnp.einsum("td,tef->edf", ffn_rows, gate_back, preferred_element_type=jnp.float32)
    up_part = jnp.einsum("td,tef->edf", ffn_rows, up_back, preferred_element_type=jnp.float32)
    down_part = jnp.einsum(
        "tef,td->efd", hidden_share, grad_rows, preferred_element_type=jnp.float32
    )
    gate_grad, up_grad, down_grad = (
        lax.psum_scatter(
            part.astype(jnp.bfloat16), "fsdp", scatter_dimension=0, tiled=True
        ).astype(jnp.float32)
        for part in (gate_part, up_part, down_part)
    )
    ffn_in_own = lax.psum_scatter(
        ffn_in_grad.astype(jnp.bfloat16), "tp", scatter_dimension=0, tiled=True
    ).astype(jnp.float32)
    _, second_back = jax.vjp(rms_norm, residual, gain_ffn)
    residual_norm_grad, ffn_gain_part = second_back(ffn_in_own)
    residual_grad = grad_out + residual_norm_grad
    attn_out_grad = lax.all_gather(residual_grad.astype(jnp.bfloat16), "tp", axis=0, tiled=True)
    output_part = jnp.einsum(
        "gq,gd->qd", context_b, attn_out_grad, preferred_element_type=jnp.float32
    )
    context_grad = (
        jnp.einsum("gd,qd->gq", attn_out_grad, out_w, preferred_element_type=jnp.float32)
        .astype(jnp.bfloat16)
        .reshape(seq_count, SEQ, per_dev, HD)
    )

    def attend_back(operands):
        queries, keys_b, values_b, prefix_end, log_sum, ctx_grad = operands
        scores = masked_scores(queries, keys_b, prefix_end, factor)
        attn_probs = jnp.exp(scores - log_sum[..., None])
        value_grad = jnp.einsum(
            "hqk,qhd->kd",
            attn_probs.astype(jnp.bfloat16),
            ctx_grad,
            preferred_element_type=jnp.float32,
        )
        probs_grad = jnp.einsum(
            "qhd,kd->hqk", ctx_grad, values_b, preferred_element_type=jnp.float32
        )
        scores_grad = (
            attn_probs * (probs_grad - jnp.sum(attn_probs * probs_grad, axis=-1, keepdims=True))
        ).astype(jnp.bfloat16)
        query_grad = (
            jnp.einsum("hqk,kd->qhd", scores_grad, keys_b, preferred_element_type=jnp.float32)
            * factor
        )
        key_grad = (
            jnp.einsum("hqk,qhd->kd", scores_grad, queries, preferred_element_type=jnp.float32)
            * factor
        )
        return (query_grad, key_grad, value_grad)

    query_norm_grad, key_norm_grad, value_grad = lax.map(
        attend_back, (query_seq, key_seq, value_seq, prefix_len, log_sums, context_grad)
    )
    query_raw_grad, key_raw_grad, query_gain_part, key_gain_part = prepare_back(
        (query_norm_grad.reshape(group_rows, per_dev, HD), key_norm_grad.reshape(group_rows, HD))
    )
    query_back = query_raw_grad.astype(jnp.bfloat16)
    key_back = key_raw_grad.astype(jnp.bfloat16)
    value_back = value_grad.reshape(group_rows, HD).astype(jnp.bfloat16)
    result = jnp.einsum("gq,dq->gd", query_back, query_w, preferred_element_type=jnp.float32)
    result = result + jnp.einsum("gk,dk->gd", key_back, key_w, preferred_element_type=jnp.float32)
    attn_in_grad = lax.psum_scatter(
        (
            result
            + jnp.einsum("gk,dk->gd", value_back, value_w, preferred_element_type=jnp.float32)
        ).astype(jnp.bfloat16),
        "tp",
        scatter_dimension=0,
        tiled=True,
    ).astype(jnp.float32)
    query_part = jnp.einsum("gd,gq->dq", attn_rows, query_back, preferred_element_type=jnp.float32)
    key_head_part = jnp.einsum("gd,gk->dk", attn_rows, key_back, preferred_element_type=jnp.float32)
    value_head_part = jnp.einsum(
        "gd,gk->dk", attn_rows, value_back, preferred_element_type=jnp.float32
    )
    kv_part = lax.psum_scatter(
        jnp.concatenate([key_head_part, value_head_part], axis=1),
        "fsdp",
        scatter_dimension=0,
        tiled=True,
    )
    tp_size = lax.axis_size("tp")
    kv_got = lax.all_to_all(
        kv_part.reshape(tp_size, kv_part.shape[0] // tp_size, 2 * HD),
        "tp",
        split_axis=0,
        concat_axis=0,
        tiled=True,
    )
    sub_rows = kv_part.shape[0] // tp_size
    kv_got = jnp.sum(kv_got.reshape(HK, tp_size // HK, sub_rows, 2 * HD), axis=1)
    key_proj_grad = kv_got[:, :, :HD].transpose(1, 0, 2).reshape(sub_rows, HK * HD)
    value_proj_grad = kv_got[:, :, HD:].transpose(1, 0, 2).reshape(sub_rows, HK * HD)
    _, first_back = jax.vjp(rms_norm, tokens_f, gain_attn)
    input_norm_grad, attn_gain_part = first_back(attn_in_grad)
    in_grad = residual_grad + input_norm_grad
    query_proj_grad, output_proj_grad = (
        lax.psum_scatter(
            query_part.astype(jnp.bfloat16), "fsdp", scatter_dimension=0, tiled=True
        ).astype(jnp.float32),
        lax.psum_scatter(
            output_part.astype(jnp.bfloat16), "fsdp", scatter_dimension=1, tiled=True
        ).astype(jnp.float32),
    )
    attn_gain_grad, query_gain_grad, key_gain_grad, ffn_gain_grad = (
        lax.psum_scatter(attn_gain_part, ("fsdp", "tp"), scatter_dimension=0, tiled=True),
        lax.psum_scatter(query_gain_part, ("fsdp", "tp"), scatter_dimension=0, tiled=True),
        lax.psum_scatter(key_gain_part, ("fsdp", "tp"), scatter_dimension=0, tiled=True),
        lax.psum_scatter(ffn_gain_part, ("fsdp", "tp"), scatter_dimension=0, tiled=True),
    )
    return (
        layer_out,
        in_grad,
        query_proj_grad,
        key_proj_grad,
        value_proj_grad,
        output_proj_grad,
        attn_gain_grad,
        query_gain_grad,
        key_gain_grad,
        ffn_gain_grad,
        gate_grad,
        up_grad,
        down_grad,
    )


def solution(mesh):
    in_specs = (
        P(("fsdp", "tp"), None),
        P("fsdp", "tp"),
        P(("fsdp", "tp"), None),
        P(("fsdp", "tp"), None),
        P("tp", "fsdp"),
        P(("fsdp", "tp")),
        P(("fsdp", "tp")),
        P(("fsdp", "tp")),
        P(("fsdp", "tp")),
        P("fsdp", None, "tp"),
        P("fsdp", None, "tp"),
        P("fsdp", "tp", None),
        P("fsdp", None),
        P("fsdp", None),
        P("fsdp"),
        P(("fsdp", "tp"), None),
    )
    out_specs = (
        P(("fsdp", "tp"), None),
        P(("fsdp", "tp"), None),
        P("fsdp", "tp"),
        P(("fsdp", "tp"), None),
        P(("fsdp", "tp"), None),
        P("tp", "fsdp"),
        P(("fsdp", "tp")),
        P(("fsdp", "tp")),
        P(("fsdp", "tp")),
        P(("fsdp", "tp")),
        P("fsdp", None, "tp"),
        P("fsdp", None, "tp"),
        P("fsdp", "tp", None),
    )
    return jax.shard_map(body, mesh=mesh, in_specs=in_specs, out_specs=out_specs, check_vma=False)
```

```python
import math

import jax
import jax.numpy as jnp
from jax import lax
from jax.sharding import PartitionSpec as P

HQ = 32
HK = 4
HD = 128
TOP = 8
SEQ = 1024


EPSILON = 1e-06


def rms_norm(values, weight):
    return values * lax.rsqrt(jnp.mean(values * values, axis=-1, keepdims=True) + EPSILON) * weight


def rotate(values, cosine, sine):
    half_width = values.shape[-1] // 2
    first_half = values[..., :half_width]
    second_half = values[..., half_width:]
    return jnp.concatenate(
        [first_half * cosine - second_half * sine, second_half * cosine + first_half * sine],
        axis=-1,
    )


def rotary_tables(positions, width):
    half_width = width // 2
    inverse = jnp.exp(
        -math.log(1000000.0) * 2.0 * jnp.arange(half_width, dtype=jnp.float32) / width
    )
    angles = positions[:, None] * inverse[None, :]
    return (jnp.cos(angles), jnp.sin(angles))


def masked_scores(queries, keys_b, prefix_end, factor):
    scores = jnp.einsum("qhd,kd->hqk", queries, keys_b, preferred_element_type=jnp.float32) * factor
    position = lax.iota(jnp.int32, queries.shape[0])
    allowed = (position[None, :] <= position[:, None]) | (position[None, :] < prefix_end)
    return jnp.where(allowed[None], scores, -1e30)


def tp_gather(block, count):
    place = lax.axis_index("tp")
    from_left = []
    from_right = []
    going_right = block
    going_left = block
    for step in range(1, count):
        going_right = lax.ppermute(
            going_right, "tp", [(i, i + 1) for i in range(step - 1, count - 1)]
        )
        going_left = lax.ppermute(going_left, "tp", [(i + 1, i) for i in range(0, count - step)])
        from_left.append(going_right)
        from_right.append(going_left)
    stacked = jnp.stack(from_left[::-1] + [block] + from_right, axis=0)
    picked = lax.dynamic_slice_in_dim(stacked, count - 1 - place, count, 0)
    return picked.reshape((count * block.shape[0],) + block.shape[1:])


def tp_scatter_sum(partial, count, send_type):
    place = lax.axis_index("tp")
    rows = partial.shape[0] // count
    pieces = partial.reshape((count, rows) + partial.shape[1:])

    def piece(target):
        return lax.dynamic_index_in_dim(pieces, jnp.clip(target, 0, count - 1), 0, keepdims=False)

    left_sum = None
    right_sum = None
    for step in range(1, count):
        outgoing = piece(place + count - step)
        if left_sum is not None:
            outgoing = outgoing + left_sum.astype(outgoing.dtype)
        left_sum = lax.ppermute(
            outgoing.astype(send_type), "tp", [(i, i + 1) for i in range(step)]
        )
        outgoing = piece(place - count + step)
        if right_sum is not None:
            outgoing = outgoing + right_sum.astype(outgoing.dtype)
        right_sum = lax.ppermute(
            outgoing.astype(send_type), "tp", [(i, i - 1) for i in range(count - step, count)]
        )
    own = piece(place)
    if left_sum is not None:
        own = own + left_sum.astype(own.dtype) + right_sum.astype(own.dtype)
    return own


def body(
    layer_in,
    query_proj,
    key_proj,
    value_proj,
    output_proj,
    attn_gain,
    query_gain,
    key_gain,
    ffn_gain,
    expert_gate,
    expert_up,
    expert_down,
    routes,
    route_weights,
    prefix_len,
    out_grad,
):
    tok_rows = layer_in.shape[0]
    width = layer_in.shape[1]
    group_rows = tok_rows * lax.axis_size("tp")
    seq_count = group_rows // SEQ
    factor = 1.0 / math.sqrt(HD)
    gain_sizes = (attn_gain.shape[0], query_gain.shape[0], key_gain.shape[0], ffn_gain.shape[0])
    kv_rows, kv_width = key_proj.shape
    gain_row = jnp.concatenate([attn_gain, query_gain, key_gain, ffn_gain])
    gain_block = jnp.zeros((8, 2 * kv_width), jnp.bfloat16).at[0, : gain_row.shape[0]].set(gain_row)
    packed = jnp.concatenate(
        [jnp.concatenate([key_proj, value_proj], axis=1), gain_block], axis=0
    )
    packed_all = lax.all_gather(packed, ("fsdp", "tp"), axis=0, tiled=False)
    kv_all = packed_all[:, :kv_rows].reshape(-1, 2 * kv_width)
    key_all = kv_all[:, :kv_width]
    value_all = kv_all[:, kv_width:]
    gain_all = packed_all[:, kv_rows]
    gains = []
    offset = 0
    for size in gain_sizes:
        gains.append(gain_all[:, offset : offset + size].reshape(-1))
        offset += size
    gain_attn, gain_query, gain_key, gain_ffn = gains
    gain_attn = gain_attn.astype(jnp.float32)
    gain_query = gain_query.astype(jnp.float32)
    gain_key = gain_key.astype(jnp.float32)
    gain_ffn = gain_ffn.astype(jnp.float32)
    query_w, out_w, gate_w, up_w, down_w = (
        lax.all_gather(query_proj, "fsdp", axis=0, tiled=True),
        lax.all_gather(output_proj, "fsdp", axis=1, tiled=True),
        lax.all_gather(expert_gate, "fsdp", axis=0, tiled=True),
        lax.all_gather(expert_up, "fsdp", axis=0, tiled=True),
        lax.all_gather(expert_down, "fsdp", axis=0, tiled=True),
    )
    per_dev = query_w.shape[1] // HD
    kv_head = lax.axis_index("tp") * per_dev // (HQ // HK)
    key_w = lax.dynamic_slice_in_dim(key_all, kv_head * HD, HD, 1)
    value_w = lax.dynamic_slice_in_dim(value_all, kv_head * HD, HD, 1)
    tokens_f = layer_in.astype(jnp.float32)
    tp_size = lax.axis_size("tp")
    layer_rows = tp_gather(layer_in, tp_size)
    attn_rows = rms_norm(layer_rows.astype(jnp.float32), gain_attn).astype(jnp.bfloat16)
    query_raw = jnp.dot(attn_rows, query_w, preferred_element_type=jnp.float32)
    key_raw = jnp.dot(attn_rows, key_w, preferred_element_type=jnp.float32)
    value_rows = jnp.dot(attn_rows, value_w, preferred_element_type=jnp.float32).astype(
        jnp.bfloat16
    )
    cosine, sine = rotary_tables((lax.iota(jnp.int32, group_rows) % SEQ).astype(jnp.float32), HD)

    def prepare(query_in, key_in, weight_query, weight_key):
        query_heads = rms_norm(query_in.reshape(group_rows, per_dev, HD), weight_query)
        return (
            rotate(query_heads, cosine[:, None, :], sine[:, None, :]),
            rotate(rms_norm(key_in, weight_key), cosine, sine),
        )

    (query_norm, key_norm), prepare_back = jax.vjp(
        prepare, query_raw, key_raw, gain_query, gain_key
    )
    query_seq = query_norm.astype(jnp.bfloat16).reshape(seq_count, SEQ, per_dev, HD)
    key_seq = key_norm.astype(jnp.bfloat16).reshape(seq_count, SEQ, HD)
    value_seq = value_rows.reshape(seq_count, SEQ, HD)

    def attend(operands):
        queries, keys_b, values_b, prefix_end = operands
        scores = masked_scores(queries, keys_b, prefix_end, factor)
        highest = jnp.max(scores, axis=-1, keepdims=True)
        expo = jnp.exp(scores - highest)
        denom = jnp.sum(expo, axis=-1, keepdims=True)
        attn_probs = (expo / denom).astype(jnp.bfloat16)
        context = jnp.einsum(
            "hqk,kd->qhd", attn_probs, values_b, preferred_element_type=jnp.float32
        )
        return (context, (highest + jnp.log(denom))[..., 0])

    context_all, log_sums = lax.map(attend, (query_seq, key_seq, value_seq, prefix_len))
    context_b = context_all.reshape(group_rows, per_dev * HD).astype(jnp.bfloat16)
    attn_out = tp_scatter_sum(
        jnp.dot(context_b, out_w, preferred_element_type=jnp.float32), tp_size, jnp.bfloat16
    )
    residual = tokens_f + attn_out
    ffn_in = rms_norm(residual, gain_ffn).astype(jnp.bfloat16)
    ffn_rows = tp_gather(ffn_in, tp_size)
    expert_count = gate_w.shape[0]
    chosen = routes[:, :, None] == lax.iota(jnp.int32, expert_count)[None, None, :]
    share = jnp.sum(jnp.where(chosen, route_weights[:, :, None], 0.0), axis=1)
    gate_val = jnp.einsum("td,edf->tef", ffn_rows, gate_w, preferred_element_type=jnp.float32)
    up_val = jnp.einsum("td,edf->tef", ffn_rows, up_w, preferred_element_type=jnp.float32)
    sigma = jax.nn.sigmoid(gate_val)
    active = gate_val * sigma
    hidden = (active * up_val).astype(jnp.bfloat16)
    hidden_share = (hidden.astype(jnp.float32) * share[:, :, None]).astype(jnp.bfloat16)
    mixture = jnp.einsum(
        "tef,efd->td", hidden_share, down_w, preferred_element_type=jnp.float32
    )
    mixture_own = tp_scatter_sum(mixture, tp_size, jnp.bfloat16)
    layer_out = (residual + mixture_own).astype(jnp.bfloat16)
    grad_out = out_grad.astype(jnp.float32)
    grad_rows = tp_gather(out_grad, tp_size)
    hidden_grad = (
        jnp.einsum("td,efd->tef", grad_rows, down_w, preferred_element_type=jnp.float32)
        * share[:, :, None]
    )
    gate_back = (hidden_grad * up_val * sigma * (1.0 + gate_val * (1.0 - sigma))).astype(
        jnp.bfloat16
    )
    up_back = (hidden_grad * active).astype(jnp.bfloat16)
    ffn_in_grad = jnp.einsum(
        "tef,edf->td", gate_back, gate_w, preferred_element_type=jnp.float32
    ) + jnp.einsum("tef,edf->td", up_back, up_w, preferred_element_type=jnp.float32)
    gate_part = jnp.einsum("td,tef->edf", ffn_rows, gate_back, preferred_element_type=jnp.float32)
    up_part = jnp.einsum("td,tef->edf", ffn_rows, up_back, preferred_element_type=jnp.float32)
    down_part = jnp.einsum(
        "tef,td->efd", hidden_share, grad_rows, preferred_element_type=jnp.float32
    )
    gate_grad, up_grad, down_grad = (
        lax.psum_scatter(
            part.astype(jnp.bfloat16), "fsdp", scatter_dimension=0, tiled=True
        ).astype(jnp.float32)
        for part in (gate_part, up_part, down_part)
    )
    ffn_in_own = tp_scatter_sum(ffn_in_grad, tp_size, jnp.bfloat16)
    _, second_back = jax.vjp(rms_norm, residual, gain_ffn)
    residual_norm_grad, ffn_gain_part = second_back(ffn_in_own)
    residual_grad = grad_out + residual_norm_grad
    attn_out_grad = tp_gather(residual_grad.astype(jnp.bfloat16), tp_size)
    output_part = jnp.einsum(
        "gq,gd->qd", context_b, attn_out_grad, preferred_element_type=jnp.float32
    )
    context_grad = (
        jnp.einsum("gd,qd->gq", attn_out_grad, out_w, preferred_element_type=jnp.float32)
        .astype(jnp.bfloat16)
        .reshape(seq_count, SEQ, per_dev, HD)
    )

    def attend_back(operands):
        queries, keys_b, values_b, prefix_end, log_sum, ctx_grad = operands
        scores = masked_scores(queries, keys_b, prefix_end, factor)
        attn_probs = jnp.exp(scores - log_sum[..., None])
        value_grad = jnp.einsum(
            "hqk,qhd->kd",
            attn_probs.astype(jnp.bfloat16),
            ctx_grad,
            preferred_element_type=jnp.float32,
        )
        probs_grad = jnp.einsum(
            "qhd,kd->hqk", ctx_grad, values_b, preferred_element_type=jnp.float32
        )
        scores_grad = (
            attn_probs * (probs_grad - jnp.sum(attn_probs * probs_grad, axis=-1, keepdims=True))
        ).astype(jnp.bfloat16)
        query_grad = (
            jnp.einsum("hqk,kd->qhd", scores_grad, keys_b, preferred_element_type=jnp.float32)
            * factor
        )
        key_grad = (
            jnp.einsum("hqk,qhd->kd", scores_grad, queries, preferred_element_type=jnp.float32)
            * factor
        )
        return (query_grad, key_grad, value_grad)

    query_norm_grad, key_norm_grad, value_grad = lax.map(
        attend_back, (query_seq, key_seq, value_seq, prefix_len, log_sums, context_grad)
    )
    query_raw_grad, key_raw_grad, query_gain_part, key_gain_part = prepare_back(
        (query_norm_grad.reshape(group_rows, per_dev, HD), key_norm_grad.reshape(group_rows, HD))
    )
    query_back = query_raw_grad.astype(jnp.bfloat16)
    key_back = key_raw_grad.astype(jnp.bfloat16)
    value_back = value_grad.reshape(group_rows, HD).astype(jnp.bfloat16)
    result = jnp.einsum("gq,dq->gd", query_back, query_w, preferred_element_type=jnp.float32)
    result = result + jnp.einsum("gk,dk->gd", key_back, key_w, preferred_element_type=jnp.float32)
    attn_in_part = result + jnp.einsum(
        "gk,dk->gd", value_back, value_w, preferred_element_type=jnp.float32
    )
    attn_in_grad = tp_scatter_sum(attn_in_part, tp_size, jnp.bfloat16)
    query_part = jnp.einsum("gd,gq->dq", attn_rows, query_back, preferred_element_type=jnp.float32)
    key_head_part = jnp.einsum("gd,gk->dk", attn_rows, key_back, preferred_element_type=jnp.float32)
    value_head_part = jnp.einsum(
        "gd,gk->dk", attn_rows, value_back, preferred_element_type=jnp.float32
    )
    kv_part = lax.psum_scatter(
        jnp.concatenate([key_head_part, value_head_part], axis=1),
        "fsdp",
        scatter_dimension=0,
        tiled=True,
    )
    kv_got = lax.all_to_all(
        kv_part.reshape(tp_size, kv_part.shape[0] // tp_size, 2 * HD),
        "tp",
        split_axis=0,
        concat_axis=0,
        tiled=True,
    )
    sub_rows = kv_part.shape[0] // tp_size
    kv_got = jnp.sum(kv_got.reshape(HK, tp_size // HK, sub_rows, 2 * HD), axis=1)
    key_proj_grad = kv_got[:, :, :HD].transpose(1, 0, 2).reshape(sub_rows, HK * HD)
    value_proj_grad = kv_got[:, :, HD:].transpose(1, 0, 2).reshape(sub_rows, HK * HD)
    _, first_back = jax.vjp(rms_norm, tokens_f, gain_attn)
    input_norm_grad, _ = first_back(attn_in_grad)
    _, rows_back = jax.vjp(
        lambda weight: rms_norm(layer_rows.astype(jnp.float32), weight), gain_attn
    )
    (attn_gain_part,) = rows_back(attn_in_part)
    in_grad = residual_grad + input_norm_grad
    query_proj_grad, output_proj_grad = (
        lax.psum_scatter(
            query_part.astype(jnp.bfloat16), "fsdp", scatter_dimension=0, tiled=True
        ).astype(jnp.float32),
        lax.psum_scatter(
            output_part.astype(jnp.bfloat16), "fsdp", scatter_dimension=1, tiled=True
        ).astype(jnp.float32),
    )
    attn_gain_grad, query_gain_grad, key_gain_grad, ffn_gain_grad = (
        lax.psum_scatter(attn_gain_part, ("fsdp", "tp"), scatter_dimension=0, tiled=True),
        lax.psum_scatter(query_gain_part, ("fsdp", "tp"), scatter_dimension=0, tiled=True),
        lax.psum_scatter(key_gain_part, ("fsdp", "tp"), scatter_dimension=0, tiled=True),
        lax.psum_scatter(ffn_gain_part, ("fsdp", "tp"), scatter_dimension=0, tiled=True),
    )
    return (
        layer_out,
        in_grad,
        query_proj_grad,
        key_proj_grad,
        value_proj_grad,
        output_proj_grad,
        attn_gain_grad,
        query_gain_grad,
        key_gain_grad,
        ffn_gain_grad,
        gate_grad,
        up_grad,
        down_grad,
    )


def solution(mesh):
    in_specs = (
        P(("fsdp", "tp"), None),
        P("fsdp", "tp"),
        P(("fsdp", "tp"), None),
        P(("fsdp", "tp"), None),
        P("tp", "fsdp"),
        P(("fsdp", "tp")),
        P(("fsdp", "tp")),
        P(("fsdp", "tp")),
        P(("fsdp", "tp")),
        P("fsdp", None, "tp"),
        P("fsdp", None, "tp"),
        P("fsdp", "tp", None),
        P("fsdp", None),
        P("fsdp", None),
        P("fsdp"),
        P(("fsdp", "tp"), None),
    )
    out_specs = (
        P(("fsdp", "tp"), None),
        P(("fsdp", "tp"), None),
        P("fsdp", "tp"),
        P(("fsdp", "tp"), None),
        P(("fsdp", "tp"), None),
        P("tp", "fsdp"),
        P(("fsdp", "tp")),
        P(("fsdp", "tp")),
        P(("fsdp", "tp")),
        P(("fsdp", "tp")),
        P("fsdp", None, "tp"),
        P("fsdp", None, "tp"),
        P("fsdp", "tp", None),
    )
    return jax.shard_map(body, mesh=mesh, in_specs=in_specs, out_specs=out_specs, check_vma=False)
```

```python
import math

import jax
import jax.numpy as jnp
from jax import lax
from jax.sharding import PartitionSpec as P

HQ = 32
HK = 4
HD = 128
TOP = 8
SEQ = 1024


EPSILON = 1e-06


def rms_norm(values, weight):
    return values * lax.rsqrt(jnp.mean(values * values, axis=-1, keepdims=True) + EPSILON) * weight


def rotate(values, cosine, sine):
    half_width = values.shape[-1] // 2
    first_half = values[..., :half_width]
    second_half = values[..., half_width:]
    return jnp.concatenate(
        [first_half * cosine - second_half * sine, second_half * cosine + first_half * sine],
        axis=-1,
    )


def rotary_tables(positions, width):
    half_width = width // 2
    inverse = jnp.exp(
        -math.log(1000000.0) * 2.0 * jnp.arange(half_width, dtype=jnp.float32) / width
    )
    angles = positions[:, None] * inverse[None, :]
    return (jnp.cos(angles), jnp.sin(angles))


def masked_scores(queries, keys_b, prefix_end, factor):
    scores = jnp.einsum("qhd,kd->hqk", queries, keys_b, preferred_element_type=jnp.float32) * factor
    position = lax.iota(jnp.int32, queries.shape[0])
    allowed = (position[None, :] <= position[:, None]) | (position[None, :] < prefix_end)
    return jnp.where(allowed[None], scores, -1e30)


def tp_gather(block, count):
    place = lax.axis_index("tp")
    from_left = []
    from_right = []
    going_right = block
    going_left = block
    for step in range(1, count):
        going_right = lax.ppermute(
            going_right, "tp", [(i, i + 1) for i in range(step - 1, count - 1)]
        )
        going_left = lax.ppermute(going_left, "tp", [(i + 1, i) for i in range(0, count - step)])
        from_left.append(going_right)
        from_right.append(going_left)
    stacked = jnp.stack(from_left[::-1] + [block] + from_right, axis=0)
    picked = lax.dynamic_slice_in_dim(stacked, count - 1 - place, count, 0)
    return picked.reshape((count * block.shape[0],) + block.shape[1:])


def tp_scatter_sum(partial, count, send_type):
    place = lax.axis_index("tp")
    rows = partial.shape[0] // count
    pieces = partial.reshape((count, rows) + partial.shape[1:])

    def piece(target):
        return lax.dynamic_index_in_dim(pieces, jnp.clip(target, 0, count - 1), 0, keepdims=False)

    left_sum = None
    right_sum = None
    for step in range(1, count):
        outgoing = piece(place + count - step)
        if left_sum is not None:
            outgoing = outgoing + left_sum.astype(outgoing.dtype)
        left_sum = lax.ppermute(
            outgoing.astype(send_type), "tp", [(i, i + 1) for i in range(step)]
        )
        outgoing = piece(place - count + step)
        if right_sum is not None:
            outgoing = outgoing + right_sum.astype(outgoing.dtype)
        right_sum = lax.ppermute(
            outgoing.astype(send_type), "tp", [(i, i - 1) for i in range(count - step, count)]
        )
    own = piece(place)
    if left_sum is not None:
        own = own + left_sum.astype(own.dtype) + right_sum.astype(own.dtype)
    return own


def body(
    layer_in,
    query_proj,
    key_proj,
    value_proj,
    output_proj,
    attn_gain,
    query_gain,
    key_gain,
    ffn_gain,
    expert_gate,
    expert_up,
    expert_down,
    routes,
    route_weights,
    prefix_len,
    out_grad,
):
    tok_rows = layer_in.shape[0]
    width = layer_in.shape[1]
    group_rows = tok_rows * lax.axis_size("tp")
    seq_count = group_rows // SEQ
    factor = 1.0 / math.sqrt(HD)
    gain_sizes = (attn_gain.shape[0], query_gain.shape[0], key_gain.shape[0], ffn_gain.shape[0])
    kv_rows, kv_width = key_proj.shape
    gain_row = jnp.concatenate([attn_gain, query_gain, key_gain, ffn_gain])
    gain_block = jnp.zeros((8, 2 * kv_width), jnp.bfloat16).at[0, : gain_row.shape[0]].set(gain_row)
    packed = jnp.concatenate(
        [jnp.concatenate([key_proj, value_proj], axis=1), gain_block], axis=0
    )
    packed_all = lax.all_gather(packed, ("fsdp", "tp"), axis=0, tiled=False)
    kv_all = packed_all[:, :kv_rows].reshape(-1, 2 * kv_width)
    key_all = kv_all[:, :kv_width]
    value_all = kv_all[:, kv_width:]
    gain_all = packed_all[:, kv_rows]
    gains = []
    offset = 0
    for size in gain_sizes:
        gains.append(gain_all[:, offset : offset + size].reshape(-1))
        offset += size
    gain_attn, gain_query, gain_key, gain_ffn = gains
    gain_attn = gain_attn.astype(jnp.float32)
    gain_query = gain_query.astype(jnp.float32)
    gain_key = gain_key.astype(jnp.float32)
    gain_ffn = gain_ffn.astype(jnp.float32)
    packed_all, query_proj = lax.optimization_barrier((packed_all, query_proj))
    query_w, out_w, gate_w, up_w, down_w = (
        lax.all_gather(query_proj, "fsdp", axis=0, tiled=True),
        lax.all_gather(output_proj, "fsdp", axis=1, tiled=True),
        lax.all_gather(expert_gate, "fsdp", axis=0, tiled=True),
        lax.all_gather(expert_up, "fsdp", axis=0, tiled=True),
        lax.all_gather(expert_down, "fsdp", axis=0, tiled=True),
    )
    per_dev = query_w.shape[1] // HD
    kv_head = lax.axis_index("tp") * per_dev // (HQ // HK)
    key_w = lax.dynamic_slice_in_dim(key_all, kv_head * HD, HD, 1)
    value_w = lax.dynamic_slice_in_dim(value_all, kv_head * HD, HD, 1)
    tokens_f = layer_in.astype(jnp.float32)
    tp_size = lax.axis_size("tp")
    layer_rows = tp_gather(layer_in, tp_size)
    attn_rows = rms_norm(layer_rows.astype(jnp.float32), gain_attn).astype(jnp.bfloat16)
    out_grad, attn_rows = lax.optimization_barrier((out_grad, attn_rows))
    grad_rows = tp_gather(out_grad, tp_size)
    query_raw = jnp.dot(attn_rows, query_w, preferred_element_type=jnp.float32)
    key_raw = jnp.dot(attn_rows, key_w, preferred_element_type=jnp.float32)
    value_rows = jnp.dot(attn_rows, value_w, preferred_element_type=jnp.float32).astype(
        jnp.bfloat16
    )
    cosine, sine = rotary_tables((lax.iota(jnp.int32, group_rows) % SEQ).astype(jnp.float32), HD)

    def prepare(query_in, key_in, weight_query, weight_key):
        query_heads = rms_norm(query_in.reshape(group_rows, per_dev, HD), weight_query)
        return (
            rotate(query_heads, cosine[:, None, :], sine[:, None, :]),
            rotate(rms_norm(key_in, weight_key), cosine, sine),
        )

    (query_norm, key_norm), prepare_back = jax.vjp(
        prepare, query_raw, key_raw, gain_query, gain_key
    )
    query_seq = query_norm.astype(jnp.bfloat16).reshape(seq_count, SEQ, per_dev, HD)
    key_seq = key_norm.astype(jnp.bfloat16).reshape(seq_count, SEQ, HD)
    value_seq = value_rows.reshape(seq_count, SEQ, HD)

    def attend(operands):
        queries, keys_b, values_b, prefix_end = operands
        scores = masked_scores(queries, keys_b, prefix_end, factor)
        highest = jnp.max(scores, axis=-1, keepdims=True)
        expo = jnp.exp(scores - highest)
        denom = jnp.sum(expo, axis=-1, keepdims=True)
        attn_probs = (expo / denom).astype(jnp.bfloat16)
        context = jnp.einsum(
            "hqk,kd->qhd", attn_probs, values_b, preferred_element_type=jnp.float32
        )
        return (context, (highest + jnp.log(denom))[..., 0])

    context_all, log_sums = lax.map(attend, (query_seq, key_seq, value_seq, prefix_len))
    context_b = context_all.reshape(group_rows, per_dev * HD).astype(jnp.bfloat16)
    context_b, grad_rows = lax.optimization_barrier((context_b, grad_rows))
    attn_out = tp_scatter_sum(
        jnp.dot(context_b, out_w, preferred_element_type=jnp.float32), tp_size, jnp.bfloat16
    )
    residual = tokens_f + attn_out
    ffn_in = rms_norm(residual, gain_ffn).astype(jnp.bfloat16)
    ffn_rows = tp_gather(ffn_in, tp_size)
    expert_count = gate_w.shape[0]
    chosen = routes[:, :, None] == lax.iota(jnp.int32, expert_count)[None, None, :]
    share = jnp.sum(jnp.where(chosen, route_weights[:, :, None], 0.0), axis=1)
    gate_val = jnp.einsum("td,edf->tef", ffn_rows, gate_w, preferred_element_type=jnp.float32)
    up_val = jnp.einsum("td,edf->tef", ffn_rows, up_w, preferred_element_type=jnp.float32)
    sigma = jax.nn.sigmoid(gate_val)
    active = gate_val * sigma
    hidden = (active * up_val).astype(jnp.bfloat16)
    hidden_share = (hidden.astype(jnp.float32) * share[:, :, None]).astype(jnp.bfloat16)
    mixture = jnp.einsum(
        "tef,efd->td", hidden_share, down_w, preferred_element_type=jnp.float32
    )
    mixture_own = tp_scatter_sum(mixture, tp_size, jnp.bfloat16)
    grad_out = out_grad.astype(jnp.float32)
    hidden_grad = (
        jnp.einsum("td,efd->tef", grad_rows, down_w, preferred_element_type=jnp.float32)
        * share[:, :, None]
    )
    gate_back = (hidden_grad * up_val * sigma * (1.0 + gate_val * (1.0 - sigma))).astype(
        jnp.bfloat16
    )
    up_back = (hidden_grad * active).astype(jnp.bfloat16)
    ffn_in_grad = jnp.einsum(
        "tef,edf->td", gate_back, gate_w, preferred_element_type=jnp.float32
    ) + jnp.einsum("tef,edf->td", up_back, up_w, preferred_element_type=jnp.float32)
    gate_part = jnp.einsum("td,tef->edf", ffn_rows, gate_back, preferred_element_type=jnp.float32)
    up_part = jnp.einsum("td,tef->edf", ffn_rows, up_back, preferred_element_type=jnp.float32)
    down_part = jnp.einsum(
        "tef,td->efd", hidden_share, grad_rows, preferred_element_type=jnp.float32
    )
    ffn_in_own = tp_scatter_sum(ffn_in_grad, tp_size, jnp.bfloat16)
    _, second_back = jax.vjp(rms_norm, residual, gain_ffn)
    residual_norm_grad, ffn_gain_part = second_back(ffn_in_own)
    residual_grad = grad_out + residual_norm_grad
    residual_grad, mixture_own, gate_part, up_part, down_part = lax.optimization_barrier(
        (residual_grad, mixture_own, gate_part, up_part, down_part)
    )
    gate_grad, up_grad, down_grad = (
        lax.psum_scatter(
            part.astype(jnp.bfloat16), "fsdp", scatter_dimension=0, tiled=True
        ).astype(jnp.float32)
        for part in (gate_part, up_part, down_part)
    )
    layer_out = (residual + mixture_own).astype(jnp.bfloat16)
    attn_out_grad = tp_gather(residual_grad.astype(jnp.bfloat16), tp_size)
    output_part = jnp.einsum(
        "gq,gd->qd", context_b, attn_out_grad, preferred_element_type=jnp.float32
    )
    context_grad = (
        jnp.einsum("gd,qd->gq", attn_out_grad, out_w, preferred_element_type=jnp.float32)
        .astype(jnp.bfloat16)
        .reshape(seq_count, SEQ, per_dev, HD)
    )

    def attend_back(operands):
        queries, keys_b, values_b, prefix_end, log_sum, ctx_grad = operands
        scores = masked_scores(queries, keys_b, prefix_end, factor)
        attn_probs = jnp.exp(scores - log_sum[..., None])
        value_grad = jnp.einsum(
            "hqk,qhd->kd",
            attn_probs.astype(jnp.bfloat16),
            ctx_grad,
            preferred_element_type=jnp.float32,
        )
        probs_grad = jnp.einsum(
            "qhd,kd->hqk", ctx_grad, values_b, preferred_element_type=jnp.float32
        )
        scores_grad = (
            attn_probs * (probs_grad - jnp.sum(attn_probs * probs_grad, axis=-1, keepdims=True))
        ).astype(jnp.bfloat16)
        query_grad = (
            jnp.einsum("hqk,kd->qhd", scores_grad, keys_b, preferred_element_type=jnp.float32)
            * factor
        )
        key_grad = (
            jnp.einsum("hqk,qhd->kd", scores_grad, queries, preferred_element_type=jnp.float32)
            * factor
        )
        return (query_grad, key_grad, value_grad)

    query_norm_grad, key_norm_grad, value_grad = lax.map(
        attend_back, (query_seq, key_seq, value_seq, prefix_len, log_sums, context_grad)
    )
    query_raw_grad, key_raw_grad, query_gain_part, key_gain_part = prepare_back(
        (query_norm_grad.reshape(group_rows, per_dev, HD), key_norm_grad.reshape(group_rows, HD))
    )
    query_back = query_raw_grad.astype(jnp.bfloat16)
    key_back = key_raw_grad.astype(jnp.bfloat16)
    value_back = value_grad.reshape(group_rows, HD).astype(jnp.bfloat16)
    result = jnp.einsum("gq,dq->gd", query_back, query_w, preferred_element_type=jnp.float32)
    result = result + jnp.einsum("gk,dk->gd", key_back, key_w, preferred_element_type=jnp.float32)
    attn_in_part = result + jnp.einsum(
        "gk,dk->gd", value_back, value_w, preferred_element_type=jnp.float32
    )
    attn_in_grad = tp_scatter_sum(attn_in_part, tp_size, jnp.bfloat16)
    query_part = jnp.einsum("gd,gq->dq", attn_rows, query_back, preferred_element_type=jnp.float32)
    key_head_part = jnp.einsum("gd,gk->dk", attn_rows, key_back, preferred_element_type=jnp.float32)
    value_head_part = jnp.einsum(
        "gd,gk->dk", attn_rows, value_back, preferred_element_type=jnp.float32
    )
    _, first_back = jax.vjp(rms_norm, tokens_f, gain_attn)
    input_norm_grad, _ = first_back(attn_in_grad)
    _, rows_back = jax.vjp(
        lambda weight: rms_norm(layer_rows.astype(jnp.float32), weight), gain_attn
    )
    (attn_gain_part,) = rows_back(attn_in_part)
    in_grad = residual_grad + input_norm_grad
    query_proj_grad, output_proj_grad = (
        lax.psum_scatter(
            query_part.astype(jnp.bfloat16), "fsdp", scatter_dimension=0, tiled=True
        ).astype(jnp.float32),
        lax.psum_scatter(
            output_part.astype(jnp.bfloat16), "fsdp", scatter_dimension=1, tiled=True
        ).astype(jnp.float32),
    )
    fsdp_size = lax.axis_size("fsdp")
    device_count = fsdp_size * tp_size
    gain_parts = (attn_gain_part, query_gain_part, key_gain_part, ffn_gain_part)
    gain_table = jnp.concatenate(
        [part.reshape(device_count, -1) for part in gain_parts], axis=1
    )
    gain_width = gain_table.shape[1]
    kv_full = jnp.concatenate([key_head_part, value_head_part], axis=1)
    block_rows = kv_full.shape[0] // fsdp_size
    sub_rows = block_rows // tp_size
    gain_rows = -(-(tp_size * gain_width) // (8 * 2 * HD)) * 8
    gain_block = jnp.pad(
        gain_table.reshape(fsdp_size, tp_size * gain_width),
        ((0, 0), (0, gain_rows * 2 * HD - tp_size * gain_width)),
    ).reshape(fsdp_size, gain_rows, 2 * HD)
    combined = jnp.concatenate(
        [kv_full.reshape(fsdp_size, block_rows, 2 * HD), gain_block], axis=1
    ).reshape(fsdp_size * (block_rows + gain_rows), 2 * HD)
    summed = lax.psum_scatter(combined, "fsdp", scatter_dimension=0, tiled=True)
    summed = jnp.concatenate(
        [
            summed[:block_rows].reshape(-1),
            summed[block_rows:].reshape(-1)[: tp_size * gain_width],
        ]
    )
    kv_local = summed[: block_rows * 2 * HD].reshape(tp_size, sub_rows * 2 * HD)
    gain_local = summed[block_rows * 2 * HD :].reshape(tp_size, gain_width)
    got = lax.all_to_all(
        jnp.concatenate([kv_local, gain_local], axis=1),
        "tp",
        split_axis=0,
        concat_axis=0,
        tiled=True,
    )
    kv_got = got[:, : sub_rows * 2 * HD].reshape(tp_size, sub_rows, 2 * HD)
    kv_got = jnp.sum(kv_got.reshape(HK, tp_size // HK, sub_rows, 2 * HD), axis=1)
    key_proj_grad = kv_got[:, :, :HD].transpose(1, 0, 2).reshape(sub_rows, HK * HD)
    value_proj_grad = kv_got[:, :, HD:].transpose(1, 0, 2).reshape(sub_rows, HK * HD)
    gain_sum = jnp.sum(got[:, sub_rows * 2 * HD :], axis=0)
    gain_grads = []
    offset = 0
    for part in gain_parts:
        size = part.shape[0] // device_count
        gain_grads.append(gain_sum[offset : offset + size])
        offset += size
    attn_gain_grad, query_gain_grad, key_gain_grad, ffn_gain_grad = gain_grads
    return (
        layer_out,
        in_grad,
        query_proj_grad,
        key_proj_grad,
        value_proj_grad,
        output_proj_grad,
        attn_gain_grad,
        query_gain_grad,
        key_gain_grad,
        ffn_gain_grad,
        gate_grad,
        up_grad,
        down_grad,
    )


def solution(mesh):
    in_specs = (
        P(("fsdp", "tp"), None),
        P("fsdp", "tp"),
        P(("fsdp", "tp"), None),
        P(("fsdp", "tp"), None),
        P("tp", "fsdp"),
        P(("fsdp", "tp")),
        P(("fsdp", "tp")),
        P(("fsdp", "tp")),
        P(("fsdp", "tp")),
        P("fsdp", None, "tp"),
        P("fsdp", None, "tp"),
        P("fsdp", "tp", None),
        P("fsdp", None),
        P("fsdp", None),
        P("fsdp"),
        P(("fsdp", "tp"), None),
    )
    out_specs = (
        P(("fsdp", "tp"), None),
        P(("fsdp", "tp"), None),
        P("fsdp", "tp"),
        P(("fsdp", "tp"), None),
        P(("fsdp", "tp"), None),
        P("tp", "fsdp"),
        P(("fsdp", "tp")),
        P(("fsdp", "tp")),
        P(("fsdp", "tp")),
        P(("fsdp", "tp")),
        P("fsdp", None, "tp"),
        P("fsdp", None, "tp"),
        P("fsdp", "tp", None),
    )
    return jax.shard_map(body, mesh=mesh, in_specs=in_specs, out_specs=out_specs, check_vma=False)
```

```python
import math

import jax
import jax.numpy as jnp
from jax import lax
from jax.sharding import PartitionSpec as P

HQ = 32
HK = 4
HD = 128
TOP = 8
SEQ = 1024


EPSILON = 1e-06


def rms_norm(values, weight):
    return values * lax.rsqrt(jnp.mean(values * values, axis=-1, keepdims=True) + EPSILON) * weight


def rotate(values, cosine, sine):
    half_width = values.shape[-1] // 2
    first_half = values[..., :half_width]
    second_half = values[..., half_width:]
    return jnp.concatenate(
        [first_half * cosine - second_half * sine, second_half * cosine + first_half * sine],
        axis=-1,
    )


def rotary_tables(positions, width):
    half_width = width // 2
    inverse = jnp.exp(
        -math.log(1000000.0) * 2.0 * jnp.arange(half_width, dtype=jnp.float32) / width
    )
    angles = positions[:, None] * inverse[None, :]
    return (jnp.cos(angles), jnp.sin(angles))


def masked_scores(queries, keys_b, prefix_end, factor):
    scores = jnp.einsum("qhd,kd->hqk", queries, keys_b, preferred_element_type=jnp.float32) * factor
    position = lax.iota(jnp.int32, queries.shape[0])
    allowed = (position[None, :] <= position[:, None]) | (position[None, :] < prefix_end)
    return jnp.where(allowed[None], scores, -1e30)


def tp_gather(block, count):
    place = lax.axis_index("tp")
    from_left = []
    from_right = []
    going_right = block
    going_left = block
    for step in range(1, count):
        going_right = lax.ppermute(
            going_right, "tp", [(i, i + 1) for i in range(step - 1, count - 1)]
        )
        going_left = lax.ppermute(going_left, "tp", [(i + 1, i) for i in range(0, count - step)])
        from_left.append(going_right)
        from_right.append(going_left)
    stacked = jnp.stack(from_left[::-1] + [block] + from_right, axis=0)
    picked = lax.dynamic_slice_in_dim(stacked, count - 1 - place, count, 0)
    return picked.reshape((count * block.shape[0],) + block.shape[1:])


def tp_scatter_sum(partial, count, send_type):
    place = lax.axis_index("tp")
    rows = partial.shape[0] // count
    pieces = partial.reshape((count, rows) + partial.shape[1:])

    def piece(target):
        return lax.dynamic_index_in_dim(pieces, jnp.clip(target, 0, count - 1), 0, keepdims=False)

    left_sum = None
    right_sum = None
    for step in range(1, count):
        outgoing = piece(place + count - step)
        if left_sum is not None:
            outgoing = outgoing + left_sum.astype(outgoing.dtype)
        left_sum = lax.ppermute(
            outgoing.astype(send_type), "tp", [(i, i + 1) for i in range(step)]
        )
        outgoing = piece(place - count + step)
        if right_sum is not None:
            outgoing = outgoing + right_sum.astype(outgoing.dtype)
        right_sum = lax.ppermute(
            outgoing.astype(send_type), "tp", [(i, i - 1) for i in range(count - step, count)]
        )
    own = piece(place)
    if left_sum is not None:
        own = own + left_sum.astype(own.dtype) + right_sum.astype(own.dtype)
    return own


def body(
    layer_in,
    query_proj,
    key_proj,
    value_proj,
    output_proj,
    attn_gain,
    query_gain,
    key_gain,
    ffn_gain,
    expert_gate,
    expert_up,
    expert_down,
    routes,
    route_weights,
    prefix_len,
    out_grad,
):
    tok_rows = layer_in.shape[0]
    width = layer_in.shape[1]
    group_rows = tok_rows * lax.axis_size("tp")
    seq_count = group_rows // SEQ
    factor = 1.0 / math.sqrt(HD)
    gain_sizes = (attn_gain.shape[0], query_gain.shape[0], key_gain.shape[0], ffn_gain.shape[0])
    kv_rows, kv_width = key_proj.shape
    gain_row = jnp.concatenate([attn_gain, query_gain, key_gain, ffn_gain])
    gain_block = jnp.zeros((8, 2 * kv_width), jnp.bfloat16).at[0, : gain_row.shape[0]].set(gain_row)
    packed = jnp.concatenate(
        [jnp.concatenate([key_proj, value_proj], axis=1), gain_block], axis=0
    )
    packed_all = lax.all_gather(packed, ("fsdp", "tp"), axis=0, tiled=False)
    kv_all = packed_all[:, :kv_rows].reshape(-1, 2 * kv_width)
    key_all = kv_all[:, :kv_width]
    value_all = kv_all[:, kv_width:]
    gain_all = packed_all[:, kv_rows]
    gains = []
    offset = 0
    for size in gain_sizes:
        gains.append(gain_all[:, offset : offset + size].reshape(-1))
        offset += size
    gain_attn, gain_query, gain_key, gain_ffn = gains
    gain_attn = gain_attn.astype(jnp.float32)
    gain_query = gain_query.astype(jnp.float32)
    gain_key = gain_key.astype(jnp.float32)
    gain_ffn = gain_ffn.astype(jnp.float32)
    query_w, out_w, gate_w, up_w, down_w = (
        lax.all_gather(query_proj, "fsdp", axis=0, tiled=True),
        lax.all_gather(output_proj, "fsdp", axis=1, tiled=True),
        lax.all_gather(expert_gate, "fsdp", axis=0, tiled=True),
        lax.all_gather(expert_up, "fsdp", axis=0, tiled=True),
        lax.all_gather(expert_down, "fsdp", axis=0, tiled=True),
    )
    per_dev = query_w.shape[1] // HD
    kv_head = lax.axis_index("tp") * per_dev // (HQ // HK)
    key_w = lax.dynamic_slice_in_dim(key_all, kv_head * HD, HD, 1)
    value_w = lax.dynamic_slice_in_dim(value_all, kv_head * HD, HD, 1)
    tokens_f = layer_in.astype(jnp.float32)
    tp_size = lax.axis_size("tp")
    layer_rows = tp_gather(layer_in, tp_size)
    attn_rows = rms_norm(layer_rows.astype(jnp.float32), gain_attn).astype(jnp.bfloat16)
    grad_rows = tp_gather(out_grad, tp_size)
    query_raw = jnp.dot(attn_rows, query_w, preferred_element_type=jnp.float32)
    key_raw = jnp.dot(attn_rows, key_w, preferred_element_type=jnp.float32)
    value_rows = jnp.dot(attn_rows, value_w, preferred_element_type=jnp.float32).astype(
        jnp.bfloat16
    )
    cosine, sine = rotary_tables((lax.iota(jnp.int32, group_rows) % SEQ).astype(jnp.float32), HD)

    def prepare(query_in, key_in, weight_query, weight_key):
        query_heads = rms_norm(query_in.reshape(group_rows, per_dev, HD), weight_query)
        return (
            rotate(query_heads, cosine[:, None, :], sine[:, None, :]),
            rotate(rms_norm(key_in, weight_key), cosine, sine),
        )

    (query_norm, key_norm), prepare_back = jax.vjp(
        prepare, query_raw, key_raw, gain_query, gain_key
    )
    query_seq = query_norm.astype(jnp.bfloat16).reshape(seq_count, SEQ, per_dev, HD)
    key_seq = key_norm.astype(jnp.bfloat16).reshape(seq_count, SEQ, HD)
    value_seq = value_rows.reshape(seq_count, SEQ, HD)

    def attend(operands):
        queries, keys_b, values_b, prefix_end = operands
        scores = masked_scores(queries, keys_b, prefix_end, factor)
        highest = jnp.max(scores, axis=-1, keepdims=True)
        expo = jnp.exp(scores - highest)
        denom = jnp.sum(expo, axis=-1, keepdims=True)
        attn_probs = (expo / denom).astype(jnp.bfloat16)
        context = jnp.einsum(
            "hqk,kd->qhd", attn_probs, values_b, preferred_element_type=jnp.float32
        )
        return (context, (highest + jnp.log(denom))[..., 0])

    context_all, log_sums = lax.map(attend, (query_seq, key_seq, value_seq, prefix_len))
    context_b = context_all.reshape(group_rows, per_dev * HD).astype(jnp.bfloat16)
    attn_out = tp_scatter_sum(
        jnp.dot(context_b, out_w, preferred_element_type=jnp.float32), tp_size, jnp.bfloat16
    )
    residual = tokens_f + attn_out
    ffn_in = rms_norm(residual, gain_ffn).astype(jnp.bfloat16)
    ffn_rows = tp_gather(ffn_in, tp_size)
    expert_count = gate_w.shape[0]
    chosen = routes[:, :, None] == lax.iota(jnp.int32, expert_count)[None, None, :]
    share = jnp.sum(jnp.where(chosen, route_weights[:, :, None], 0.0), axis=1)
    gate_val = jnp.einsum("td,edf->tef", ffn_rows, gate_w, preferred_element_type=jnp.float32)
    up_val = jnp.einsum("td,edf->tef", ffn_rows, up_w, preferred_element_type=jnp.float32)
    sigma = jax.nn.sigmoid(gate_val)
    active = gate_val * sigma
    hidden = (active * up_val).astype(jnp.bfloat16)
    hidden_share = (hidden.astype(jnp.float32) * share[:, :, None]).astype(jnp.bfloat16)
    mixture = jnp.einsum(
        "tef,efd->td", hidden_share, down_w, preferred_element_type=jnp.float32
    )
    mixture_own = tp_scatter_sum(mixture, tp_size, jnp.bfloat16)
    grad_out = out_grad.astype(jnp.float32)
    hidden_grad = (
        jnp.einsum("td,efd->tef", grad_rows, down_w, preferred_element_type=jnp.float32)
        * share[:, :, None]
    )
    gate_back = (hidden_grad * up_val * sigma * (1.0 + gate_val * (1.0 - sigma))).astype(
        jnp.bfloat16
    )
    up_back = (hidden_grad * active).astype(jnp.bfloat16)
    ffn_in_grad = jnp.einsum(
        "tef,edf->td", gate_back, gate_w, preferred_element_type=jnp.float32
    ) + jnp.einsum("tef,edf->td", up_back, up_w, preferred_element_type=jnp.float32)
    gate_part = jnp.einsum("td,tef->edf", ffn_rows, gate_back, preferred_element_type=jnp.float32)
    up_part = jnp.einsum("td,tef->edf", ffn_rows, up_back, preferred_element_type=jnp.float32)
    down_part = jnp.einsum(
        "tef,td->efd", hidden_share, grad_rows, preferred_element_type=jnp.float32
    )
    ffn_in_own = tp_scatter_sum(ffn_in_grad, tp_size, jnp.bfloat16)
    _, second_back = jax.vjp(rms_norm, residual, gain_ffn)
    residual_norm_grad, ffn_gain_part = second_back(ffn_in_own)
    residual_grad = grad_out + residual_norm_grad
    residual_grad, mixture_own, gate_part, up_part, down_part = lax.optimization_barrier(
        (residual_grad, mixture_own, gate_part, up_part, down_part)
    )
    gate_grad, up_grad, down_grad = (
        lax.psum_scatter(
            part.astype(jnp.bfloat16), "fsdp", scatter_dimension=0, tiled=True
        ).astype(jnp.float32)
        for part in (gate_part, up_part, down_part)
    )
    layer_out = (residual + mixture_own).astype(jnp.bfloat16)
    attn_out_grad = tp_gather(residual_grad.astype(jnp.bfloat16), tp_size)
    output_part = jnp.einsum(
        "gq,gd->qd", context_b, attn_out_grad, preferred_element_type=jnp.float32
    )
    context_grad = (
        jnp.einsum("gd,qd->gq", attn_out_grad, out_w, preferred_element_type=jnp.float32)
        .astype(jnp.bfloat16)
        .reshape(seq_count, SEQ, per_dev, HD)
    )

    def attend_back(operands):
        queries, keys_b, values_b, prefix_end, log_sum, ctx_grad = operands
        scores = masked_scores(queries, keys_b, prefix_end, factor)
        attn_probs = jnp.exp(scores - log_sum[..., None])
        value_grad = jnp.einsum(
            "hqk,qhd->kd",
            attn_probs.astype(jnp.bfloat16),
            ctx_grad,
            preferred_element_type=jnp.float32,
        )
        probs_grad = jnp.einsum(
            "qhd,kd->hqk", ctx_grad, values_b, preferred_element_type=jnp.float32
        )
        scores_grad = (
            attn_probs * (probs_grad - jnp.sum(attn_probs * probs_grad, axis=-1, keepdims=True))
        ).astype(jnp.bfloat16)
        query_grad = (
            jnp.einsum("hqk,kd->qhd", scores_grad, keys_b, preferred_element_type=jnp.float32)
            * factor
        )
        key_grad = (
            jnp.einsum("hqk,qhd->kd", scores_grad, queries, preferred_element_type=jnp.float32)
            * factor
        )
        return (query_grad, key_grad, value_grad)

    query_norm_grad, key_norm_grad, value_grad = lax.map(
        attend_back, (query_seq, key_seq, value_seq, prefix_len, log_sums, context_grad)
    )
    query_raw_grad, key_raw_grad, query_gain_part, key_gain_part = prepare_back(
        (query_norm_grad.reshape(group_rows, per_dev, HD), key_norm_grad.reshape(group_rows, HD))
    )
    query_back = query_raw_grad.astype(jnp.bfloat16)
    key_back = key_raw_grad.astype(jnp.bfloat16)
    value_back = value_grad.reshape(group_rows, HD).astype(jnp.bfloat16)
    result = jnp.einsum("gq,dq->gd", query_back, query_w, preferred_element_type=jnp.float32)
    result = result + jnp.einsum("gk,dk->gd", key_back, key_w, preferred_element_type=jnp.float32)
    attn_in_part = result + jnp.einsum(
        "gk,dk->gd", value_back, value_w, preferred_element_type=jnp.float32
    )
    attn_in_part, down_grad, gate_grad, up_grad = lax.optimization_barrier(
        (attn_in_part, down_grad, gate_grad, up_grad)
    )
    attn_in_grad = tp_scatter_sum(attn_in_part, tp_size, jnp.bfloat16)
    query_part = jnp.einsum("gd,gq->dq", attn_rows, query_back, preferred_element_type=jnp.float32)
    key_head_part = jnp.einsum("gd,gk->dk", attn_rows, key_back, preferred_element_type=jnp.float32)
    value_head_part = jnp.einsum(
        "gd,gk->dk", attn_rows, value_back, preferred_element_type=jnp.float32
    )
    _, first_back = jax.vjp(rms_norm, tokens_f, gain_attn)
    input_norm_grad, _ = first_back(attn_in_grad)
    _, rows_back = jax.vjp(
        lambda weight: rms_norm(layer_rows.astype(jnp.float32), weight), gain_attn
    )
    (attn_gain_part,) = rows_back(attn_in_part)
    in_grad = residual_grad + input_norm_grad
    fsdp_size = lax.axis_size("fsdp")
    query_proj_grad = jnp.sum(
        lax.all_to_all(
            query_part.astype(jnp.bfloat16).reshape(fsdp_size, -1, query_part.shape[1]),
            "fsdp",
            split_axis=0,
            concat_axis=0,
            tiled=True,
        ).astype(jnp.float32),
        axis=0,
    )
    output_proj_grad = jnp.sum(
        lax.all_to_all(
            output_part.astype(jnp.bfloat16)
            .reshape(output_part.shape[0], fsdp_size, -1)
            .transpose(1, 0, 2),
            "fsdp",
            split_axis=0,
            concat_axis=0,
            tiled=True,
        ).astype(jnp.float32),
        axis=0,
    )
    device_count = fsdp_size * tp_size
    gain_parts = (attn_gain_part, query_gain_part, key_gain_part, ffn_gain_part)
    gain_table = jnp.concatenate(
        [part.reshape(device_count, -1) for part in gain_parts], axis=1
    )
    gain_width = gain_table.shape[1]
    kv_full = jnp.concatenate([key_head_part, value_head_part], axis=1)
    block_rows = kv_full.shape[0] // fsdp_size
    sub_rows = block_rows // tp_size
    gain_rows = -(-(tp_size * gain_width) // (8 * 2 * HD)) * 8
    gain_block = jnp.pad(
        gain_table.reshape(fsdp_size, tp_size * gain_width),
        ((0, 0), (0, gain_rows * 2 * HD - tp_size * gain_width)),
    ).reshape(fsdp_size, gain_rows, 2 * HD)
    combined = jnp.concatenate(
        [kv_full.reshape(fsdp_size, block_rows, 2 * HD), gain_block], axis=1
    ).reshape(fsdp_size * (block_rows + gain_rows), 2 * HD)
    summed = lax.psum_scatter(combined, "fsdp", scatter_dimension=0, tiled=True)
    summed = jnp.concatenate(
        [
            summed[:block_rows].reshape(-1),
            summed[block_rows:].reshape(-1)[: tp_size * gain_width],
        ]
    )
    kv_local = summed[: block_rows * 2 * HD].reshape(tp_size, sub_rows * 2 * HD)
    gain_local = summed[block_rows * 2 * HD :].reshape(tp_size, gain_width)
    got = lax.all_to_all(
        jnp.concatenate([kv_local, gain_local], axis=1),
        "tp",
        split_axis=0,
        concat_axis=0,
        tiled=True,
    )
    kv_got = got[:, : sub_rows * 2 * HD].reshape(tp_size, sub_rows, 2 * HD)
    kv_got = jnp.sum(kv_got.reshape(HK, tp_size // HK, sub_rows, 2 * HD), axis=1)
    key_proj_grad = kv_got[:, :, :HD].transpose(1, 0, 2).reshape(sub_rows, HK * HD)
    value_proj_grad = kv_got[:, :, HD:].transpose(1, 0, 2).reshape(sub_rows, HK * HD)
    gain_sum = jnp.sum(got[:, sub_rows * 2 * HD :], axis=0)
    gain_grads = []
    offset = 0
    for part in gain_parts:
        size = part.shape[0] // device_count
        gain_grads.append(gain_sum[offset : offset + size])
        offset += size
    attn_gain_grad, query_gain_grad, key_gain_grad, ffn_gain_grad = gain_grads
    return (
        layer_out,
        in_grad,
        query_proj_grad,
        key_proj_grad,
        value_proj_grad,
        output_proj_grad,
        attn_gain_grad,
        query_gain_grad,
        key_gain_grad,
        ffn_gain_grad,
        gate_grad,
        up_grad,
        down_grad,
    )


def solution(mesh):
    in_specs = (
        P(("fsdp", "tp"), None),
        P("fsdp", "tp"),
        P(("fsdp", "tp"), None),
        P(("fsdp", "tp"), None),
        P("tp", "fsdp"),
        P(("fsdp", "tp")),
        P(("fsdp", "tp")),
        P(("fsdp", "tp")),
        P(("fsdp", "tp")),
        P("fsdp", None, "tp"),
        P("fsdp", None, "tp"),
        P("fsdp", "tp", None),
        P("fsdp", None),
        P("fsdp", None),
        P("fsdp"),
        P(("fsdp", "tp"), None),
    )
    out_specs = (
        P(("fsdp", "tp"), None),
        P(("fsdp", "tp"), None),
        P("fsdp", "tp"),
        P(("fsdp", "tp"), None),
        P(("fsdp", "tp"), None),
        P("tp", "fsdp"),
        P(("fsdp", "tp")),
        P(("fsdp", "tp")),
        P(("fsdp", "tp")),
        P(("fsdp", "tp")),
        P("fsdp", None, "tp"),
        P("fsdp", None, "tp"),
        P("fsdp", "tp", None),
    )
    return jax.shard_map(body, mesh=mesh, in_specs=in_specs, out_specs=out_specs, check_vma=False)
```

```python
import math

import jax
import jax.numpy as jnp
from jax import lax
from jax.sharding import PartitionSpec as P

HQ = 32
HK = 4
HD = 128
TOP = 8
SEQ = 1024


EPSILON = 1e-06


def rms_norm(values, weight):
    return values * lax.rsqrt(jnp.mean(values * values, axis=-1, keepdims=True) + EPSILON) * weight


def rotate(values, cosine, sine):
    half_width = values.shape[-1] // 2
    first_half = values[..., :half_width]
    second_half = values[..., half_width:]
    return jnp.concatenate(
        [first_half * cosine - second_half * sine, second_half * cosine + first_half * sine],
        axis=-1,
    )


def rotary_tables(positions, width):
    half_width = width // 2
    inverse = jnp.exp(
        -math.log(1000000.0) * 2.0 * jnp.arange(half_width, dtype=jnp.float32) / width
    )
    angles = positions[:, None] * inverse[None, :]
    return (jnp.cos(angles), jnp.sin(angles))


def masked_scores(queries, keys_b, prefix_end, factor):
    scores = jnp.einsum("qhd,kd->hqk", queries, keys_b, preferred_element_type=jnp.float32) * factor
    position = lax.iota(jnp.int32, queries.shape[0])
    allowed = (position[None, :] <= position[:, None]) | (position[None, :] < prefix_end)
    return jnp.where(allowed[None], scores, -1e30)


def tp_gather(block, count):
    place = lax.axis_index("tp")
    from_left = []
    from_right = []
    going_right = block
    going_left = block
    for step in range(1, count):
        going_right = lax.ppermute(
            going_right, "tp", [(i, i + 1) for i in range(step - 1, count - 1)]
        )
        going_left = lax.ppermute(going_left, "tp", [(i + 1, i) for i in range(0, count - step)])
        from_left.append(going_right)
        from_right.append(going_left)
    stacked = jnp.stack(from_left[::-1] + [block] + from_right, axis=0)
    picked = lax.dynamic_slice_in_dim(stacked, count - 1 - place, count, 0)
    return picked.reshape((count * block.shape[0],) + block.shape[1:])


def tp_scatter_sum(partial, count, send_type):
    place = lax.axis_index("tp")
    rows = partial.shape[0] // count
    pieces = partial.reshape((count, rows) + partial.shape[1:])

    def piece(target):
        return lax.dynamic_index_in_dim(pieces, jnp.clip(target, 0, count - 1), 0, keepdims=False)

    left_sum = None
    right_sum = None
    for step in range(1, count):
        outgoing = piece(place + count - step)
        if left_sum is not None:
            outgoing = outgoing + left_sum.astype(outgoing.dtype)
        left_sum = lax.ppermute(
            outgoing.astype(send_type), "tp", [(i, i + 1) for i in range(step)]
        )
        outgoing = piece(place - count + step)
        if right_sum is not None:
            outgoing = outgoing + right_sum.astype(outgoing.dtype)
        right_sum = lax.ppermute(
            outgoing.astype(send_type), "tp", [(i, i - 1) for i in range(count - step, count)]
        )
    own = piece(place)
    if left_sum is not None:
        own = own + left_sum.astype(own.dtype) + right_sum.astype(own.dtype)
    return own


def body(
    layer_in,
    query_proj,
    key_proj,
    value_proj,
    output_proj,
    attn_gain,
    query_gain,
    key_gain,
    ffn_gain,
    expert_gate,
    expert_up,
    expert_down,
    routes,
    route_weights,
    prefix_len,
    out_grad,
):
    tok_rows = layer_in.shape[0]
    width = layer_in.shape[1]
    group_rows = tok_rows * lax.axis_size("tp")
    seq_count = group_rows // SEQ
    factor = 1.0 / math.sqrt(HD)
    gain_sizes = (attn_gain.shape[0], query_gain.shape[0], key_gain.shape[0], ffn_gain.shape[0])
    kv_rows, kv_width = key_proj.shape
    gain_row = jnp.concatenate([attn_gain, query_gain, key_gain, ffn_gain])
    gain_block = jnp.zeros((8, 2 * kv_width), jnp.bfloat16).at[0, : gain_row.shape[0]].set(gain_row)
    packed = jnp.concatenate(
        [jnp.concatenate([key_proj, value_proj], axis=1), gain_block], axis=0
    )
    packed_all = lax.all_gather(packed, ("fsdp", "tp"), axis=0, tiled=False)
    kv_all = packed_all[:, :kv_rows].reshape(-1, 2 * kv_width)
    key_all = kv_all[:, :kv_width]
    value_all = kv_all[:, kv_width:]
    gain_all = packed_all[:, kv_rows]
    gains = []
    offset = 0
    for size in gain_sizes:
        gains.append(gain_all[:, offset : offset + size].reshape(-1))
        offset += size
    gain_attn, gain_query, gain_key, gain_ffn = gains
    gain_attn = gain_attn.astype(jnp.float32)
    gain_query = gain_query.astype(jnp.float32)
    gain_key = gain_key.astype(jnp.float32)
    gain_ffn = gain_ffn.astype(jnp.float32)
    query_w, out_w, gate_w, up_w, down_w = (
        lax.all_gather(query_proj, "fsdp", axis=0, tiled=True),
        lax.all_gather(output_proj, "fsdp", axis=1, tiled=True),
        lax.all_gather(expert_gate, "fsdp", axis=0, tiled=True),
        lax.all_gather(expert_up, "fsdp", axis=0, tiled=True),
        lax.all_gather(expert_down, "fsdp", axis=0, tiled=True),
    )
    per_dev = query_w.shape[1] // HD
    kv_head = lax.axis_index("tp") * per_dev // (HQ // HK)
    key_w = lax.dynamic_slice_in_dim(key_all, kv_head * HD, HD, 1)
    value_w = lax.dynamic_slice_in_dim(value_all, kv_head * HD, HD, 1)
    tokens_f = layer_in.astype(jnp.float32)
    tp_size = lax.axis_size("tp")
    layer_rows = tp_gather(layer_in, tp_size)
    attn_rows = rms_norm(layer_rows.astype(jnp.float32), gain_attn).astype(jnp.bfloat16)
    out_grad, attn_rows = lax.optimization_barrier((out_grad, attn_rows))
    grad_rows = tp_gather(out_grad, tp_size)
    query_raw = jnp.dot(attn_rows, query_w, preferred_element_type=jnp.float32)
    key_raw = jnp.dot(attn_rows, key_w, preferred_element_type=jnp.float32)
    value_rows = jnp.dot(attn_rows, value_w, preferred_element_type=jnp.float32).astype(
        jnp.bfloat16
    )
    cosine, sine = rotary_tables((lax.iota(jnp.int32, group_rows) % SEQ).astype(jnp.float32), HD)

    def prepare(query_in, key_in, weight_query, weight_key):
        query_heads = rms_norm(query_in.reshape(group_rows, per_dev, HD), weight_query)
        return (
            rotate(query_heads, cosine[:, None, :], sine[:, None, :]),
            rotate(rms_norm(key_in, weight_key), cosine, sine),
        )

    (query_norm, key_norm), prepare_back = jax.vjp(
        prepare, query_raw, key_raw, gain_query, gain_key
    )
    query_seq = query_norm.astype(jnp.bfloat16).reshape(seq_count, SEQ, per_dev, HD)
    key_seq = key_norm.astype(jnp.bfloat16).reshape(seq_count, SEQ, HD)
    value_seq = value_rows.reshape(seq_count, SEQ, HD)

    def attend(operands):
        queries, keys_b, values_b, prefix_end = operands
        scores = masked_scores(queries, keys_b, prefix_end, factor)
        highest = jnp.max(scores, axis=-1, keepdims=True)
        expo = jnp.exp(scores - highest)
        denom = jnp.sum(expo, axis=-1, keepdims=True)
        attn_probs = (expo / denom).astype(jnp.bfloat16)
        context = jnp.einsum(
            "hqk,kd->qhd", attn_probs, values_b, preferred_element_type=jnp.float32
        )
        return (context, (highest + jnp.log(denom))[..., 0])

    context_all, log_sums = lax.map(attend, (query_seq, key_seq, value_seq, prefix_len))
    context_b = context_all.reshape(group_rows, per_dev * HD).astype(jnp.bfloat16)
    context_b, grad_rows = lax.optimization_barrier((context_b, grad_rows))
    attn_out = tp_scatter_sum(
        jnp.dot(context_b, out_w, preferred_element_type=jnp.float32), tp_size, jnp.bfloat16
    )
    residual = tokens_f + attn_out
    ffn_in = rms_norm(residual, gain_ffn).astype(jnp.bfloat16)
    ffn_rows = tp_gather(ffn_in, tp_size)
    expert_count = gate_w.shape[0]
    chosen = routes[:, :, None] == lax.iota(jnp.int32, expert_count)[None, None, :]
    share = jnp.sum(jnp.where(chosen, route_weights[:, :, None], 0.0), axis=1)
    gate_val = jnp.einsum("td,edf->tef", ffn_rows, gate_w, preferred_element_type=jnp.float32)
    up_val = jnp.einsum("td,edf->tef", ffn_rows, up_w, preferred_element_type=jnp.float32)
    sigma = jax.nn.sigmoid(gate_val)
    active = gate_val * sigma
    hidden = (active * up_val).astype(jnp.bfloat16)
    hidden_share = (hidden.astype(jnp.float32) * share[:, :, None]).astype(jnp.bfloat16)
    mixture = jnp.einsum(
        "tef,efd->td", hidden_share, down_w, preferred_element_type=jnp.float32
    )
    mixture_own = tp_scatter_sum(mixture, tp_size, jnp.bfloat16)
    grad_out = out_grad.astype(jnp.float32)
    hidden_grad = (
        jnp.einsum("td,efd->tef", grad_rows, down_w, preferred_element_type=jnp.float32)
        * share[:, :, None]
    )
    gate_back = (hidden_grad * up_val * sigma * (1.0 + gate_val * (1.0 - sigma))).astype(
        jnp.bfloat16
    )
    up_back = (hidden_grad * active).astype(jnp.bfloat16)
    ffn_in_grad = jnp.einsum(
        "tef,edf->td", gate_back, gate_w, preferred_element_type=jnp.float32
    ) + jnp.einsum("tef,edf->td", up_back, up_w, preferred_element_type=jnp.float32)
    gate_part = jnp.einsum("td,tef->edf", ffn_rows, gate_back, preferred_element_type=jnp.float32)
    up_part = jnp.einsum("td,tef->edf", ffn_rows, up_back, preferred_element_type=jnp.float32)
    down_part = jnp.einsum(
        "tef,td->efd", hidden_share, grad_rows, preferred_element_type=jnp.float32
    )
    ffn_in_own = tp_scatter_sum(ffn_in_grad, tp_size, jnp.bfloat16)
    _, second_back = jax.vjp(rms_norm, residual, gain_ffn)
    residual_norm_grad, ffn_gain_part = second_back(ffn_in_own)
    residual_grad = grad_out + residual_norm_grad
    residual_grad, mixture_own = lax.optimization_barrier((residual_grad, mixture_own))
    gate_grad, up_grad, down_grad = (
        lax.psum_scatter(
            part.astype(jnp.bfloat16), "fsdp", scatter_dimension=0, tiled=True
        ).astype(jnp.float32)
        for part in (gate_part, up_part, down_part)
    )
    layer_out = (residual + mixture_own).astype(jnp.bfloat16)
    attn_out_grad = tp_gather(residual_grad.astype(jnp.bfloat16), tp_size)
    output_part = jnp.einsum(
        "gq,gd->qd", context_b, attn_out_grad, preferred_element_type=jnp.float32
    )
    context_grad = (
        jnp.einsum("gd,qd->gq", attn_out_grad, out_w, preferred_element_type=jnp.float32)
        .astype(jnp.bfloat16)
        .reshape(seq_count, SEQ, per_dev, HD)
    )

    def attend_back(operands):
        queries, keys_b, values_b, prefix_end, log_sum, ctx_grad = operands
        scores = masked_scores(queries, keys_b, prefix_end, factor)
        attn_probs = jnp.exp(scores - log_sum[..., None])
        value_grad = jnp.einsum(
            "hqk,qhd->kd",
            attn_probs.astype(jnp.bfloat16),
            ctx_grad,
            preferred_element_type=jnp.float32,
        )
        probs_grad = jnp.einsum(
            "qhd,kd->hqk", ctx_grad, values_b, preferred_element_type=jnp.float32
        )
        scores_grad = (
            attn_probs * (probs_grad - jnp.sum(attn_probs * probs_grad, axis=-1, keepdims=True))
        ).astype(jnp.bfloat16)
        query_grad = (
            jnp.einsum("hqk,kd->qhd", scores_grad, keys_b, preferred_element_type=jnp.float32)
            * factor
        )
        key_grad = (
            jnp.einsum("hqk,qhd->kd", scores_grad, queries, preferred_element_type=jnp.float32)
            * factor
        )
        return (query_grad, key_grad, value_grad)

    query_norm_grad, key_norm_grad, value_grad = lax.map(
        attend_back, (query_seq, key_seq, value_seq, prefix_len, log_sums, context_grad)
    )
    query_raw_grad, key_raw_grad, query_gain_part, key_gain_part = prepare_back(
        (query_norm_grad.reshape(group_rows, per_dev, HD), key_norm_grad.reshape(group_rows, HD))
    )
    query_back = query_raw_grad.astype(jnp.bfloat16)
    key_back = key_raw_grad.astype(jnp.bfloat16)
    value_back = value_grad.reshape(group_rows, HD).astype(jnp.bfloat16)
    result = jnp.einsum("gq,dq->gd", query_back, query_w, preferred_element_type=jnp.float32)
    result = result + jnp.einsum("gk,dk->gd", key_back, key_w, preferred_element_type=jnp.float32)
    attn_in_part = result + jnp.einsum(
        "gk,dk->gd", value_back, value_w, preferred_element_type=jnp.float32
    )
    attn_in_part, down_grad, gate_grad, up_grad = lax.optimization_barrier(
        (attn_in_part, down_grad, gate_grad, up_grad)
    )
    attn_in_grad = tp_scatter_sum(attn_in_part, tp_size, jnp.bfloat16)
    query_part = jnp.einsum("gd,gq->dq", attn_rows, query_back, preferred_element_type=jnp.float32)
    key_head_part = jnp.einsum("gd,gk->dk", attn_rows, key_back, preferred_element_type=jnp.float32)
    value_head_part = jnp.einsum(
        "gd,gk->dk", attn_rows, value_back, preferred_element_type=jnp.float32
    )
    _, first_back = jax.vjp(rms_norm, tokens_f, gain_attn)
    input_norm_grad, _ = first_back(attn_in_grad)
    _, rows_back = jax.vjp(
        lambda weight: rms_norm(layer_rows.astype(jnp.float32), weight), gain_attn
    )
    (attn_gain_part,) = rows_back(attn_in_part)
    in_grad = residual_grad + input_norm_grad
    fsdp_size = lax.axis_size("fsdp")
    query_proj_grad = jnp.sum(
        lax.all_to_all(
            query_part.astype(jnp.bfloat16).reshape(fsdp_size, -1, query_part.shape[1]),
            "fsdp",
            split_axis=0,
            concat_axis=0,
            tiled=True,
        ).astype(jnp.float32),
        axis=0,
    )
    output_proj_grad = jnp.sum(
        lax.all_to_all(
            output_part.astype(jnp.bfloat16)
            .reshape(output_part.shape[0], fsdp_size, -1)
            .transpose(1, 0, 2),
            "fsdp",
            split_axis=0,
            concat_axis=0,
            tiled=True,
        ).astype(jnp.float32),
        axis=0,
    )
    device_count = fsdp_size * tp_size
    gain_parts = (attn_gain_part, query_gain_part, key_gain_part, ffn_gain_part)
    gain_table = jnp.concatenate(
        [part.reshape(device_count, -1) for part in gain_parts], axis=1
    )
    gain_width = gain_table.shape[1]
    kv_full = jnp.concatenate([key_head_part, value_head_part], axis=1)
    block_rows = kv_full.shape[0] // fsdp_size
    sub_rows = block_rows // tp_size
    gain_rows = -(-(tp_size * gain_width) // (8 * 2 * HD)) * 8
    gain_block = jnp.pad(
        gain_table.reshape(fsdp_size, tp_size * gain_width),
        ((0, 0), (0, gain_rows * 2 * HD - tp_size * gain_width)),
    ).reshape(fsdp_size, gain_rows, 2 * HD)
    combined = jnp.concatenate(
        [kv_full.reshape(fsdp_size, block_rows, 2 * HD), gain_block], axis=1
    ).reshape(fsdp_size * (block_rows + gain_rows), 2 * HD)
    summed = lax.psum_scatter(combined, "fsdp", scatter_dimension=0, tiled=True)
    summed = jnp.concatenate(
        [
            summed[:block_rows].reshape(-1),
            summed[block_rows:].reshape(-1)[: tp_size * gain_width],
        ]
    )
    kv_local = summed[: block_rows * 2 * HD].reshape(tp_size, sub_rows * 2 * HD)
    gain_local = summed[block_rows * 2 * HD :].reshape(tp_size, gain_width)
    got = lax.all_to_all(
        jnp.concatenate([kv_local, gain_local], axis=1),
        "tp",
        split_axis=0,
        concat_axis=0,
        tiled=True,
    )
    kv_got = got[:, : sub_rows * 2 * HD].reshape(tp_size, sub_rows, 2 * HD)
    kv_got = jnp.sum(kv_got.reshape(HK, tp_size // HK, sub_rows, 2 * HD), axis=1)
    key_proj_grad = kv_got[:, :, :HD].transpose(1, 0, 2).reshape(sub_rows, HK * HD)
    value_proj_grad = kv_got[:, :, HD:].transpose(1, 0, 2).reshape(sub_rows, HK * HD)
    gain_sum = jnp.sum(got[:, sub_rows * 2 * HD :], axis=0)
    gain_grads = []
    offset = 0
    for part in gain_parts:
        size = part.shape[0] // device_count
        gain_grads.append(gain_sum[offset : offset + size])
        offset += size
    attn_gain_grad, query_gain_grad, key_gain_grad, ffn_gain_grad = gain_grads
    return (
        layer_out,
        in_grad,
        query_proj_grad,
        key_proj_grad,
        value_proj_grad,
        output_proj_grad,
        attn_gain_grad,
        query_gain_grad,
        key_gain_grad,
        ffn_gain_grad,
        gate_grad,
        up_grad,
        down_grad,
    )


def solution(mesh):
    in_specs = (
        P(("fsdp", "tp"), None),
        P("fsdp", "tp"),
        P(("fsdp", "tp"), None),
        P(("fsdp", "tp"), None),
        P("tp", "fsdp"),
        P(("fsdp", "tp")),
        P(("fsdp", "tp")),
        P(("fsdp", "tp")),
        P(("fsdp", "tp")),
        P("fsdp", None, "tp"),
        P("fsdp", None, "tp"),
        P("fsdp", "tp", None),
        P("fsdp", None),
        P("fsdp", None),
        P("fsdp"),
        P(("fsdp", "tp"), None),
    )
    out_specs = (
        P(("fsdp", "tp"), None),
        P(("fsdp", "tp"), None),
        P("fsdp", "tp"),
        P(("fsdp", "tp"), None),
        P(("fsdp", "tp"), None),
        P("tp", "fsdp"),
        P(("fsdp", "tp")),
        P(("fsdp", "tp")),
        P(("fsdp", "tp")),
        P(("fsdp", "tp")),
        P("fsdp", None, "tp"),
        P("fsdp", None, "tp"),
        P("fsdp", "tp", None),
    )
    return jax.shard_map(body, mesh=mesh, in_specs=in_specs, out_specs=out_specs, check_vma=False)
```

```python
import math

import jax
import jax.numpy as jnp
from jax import lax
from jax.sharding import PartitionSpec as P

HQ = 32
HK = 4
HD = 128
TOP = 8
SEQ = 1024


EPSILON = 1e-06


def rms_norm(values, weight):
    return values * lax.rsqrt(jnp.mean(values * values, axis=-1, keepdims=True) + EPSILON) * weight


def rotate(values, cosine, sine):
    half_width = values.shape[-1] // 2
    first_half = values[..., :half_width]
    second_half = values[..., half_width:]
    return jnp.concatenate(
        [first_half * cosine - second_half * sine, second_half * cosine + first_half * sine],
        axis=-1,
    )


def rotary_tables(positions, width):
    half_width = width // 2
    inverse = jnp.exp(
        -math.log(1000000.0) * 2.0 * jnp.arange(half_width, dtype=jnp.float32) / width
    )
    angles = positions[:, None] * inverse[None, :]
    return (jnp.cos(angles), jnp.sin(angles))


def masked_scores(queries, keys_b, prefix_end, factor):
    scores = jnp.einsum("qhd,kd->hqk", queries, keys_b, preferred_element_type=jnp.float32) * factor
    position = lax.iota(jnp.int32, queries.shape[0])
    allowed = (position[None, :] <= position[:, None]) | (position[None, :] < prefix_end)
    return jnp.where(allowed[None], scores, -1e30)


def tp_gather(block, count):
    place = lax.axis_index("tp")
    from_left = []
    from_right = []
    going_right = block
    going_left = block
    for step in range(1, count):
        going_right = lax.ppermute(
            going_right, "tp", [(i, i + 1) for i in range(step - 1, count - 1)]
        )
        going_left = lax.ppermute(going_left, "tp", [(i + 1, i) for i in range(0, count - step)])
        from_left.append(going_right)
        from_right.append(going_left)
    stacked = jnp.stack(from_left[::-1] + [block] + from_right, axis=0)
    picked = lax.dynamic_slice_in_dim(stacked, count - 1 - place, count, 0)
    return picked.reshape((count * block.shape[0],) + block.shape[1:])


def tp_scatter_sum(partial, count, send_type):
    place = lax.axis_index("tp")
    rows = partial.shape[0] // count
    pieces = partial.reshape((count, rows) + partial.shape[1:])

    def piece(target):
        return lax.dynamic_index_in_dim(pieces, jnp.clip(target, 0, count - 1), 0, keepdims=False)

    left_sum = None
    right_sum = None
    for step in range(1, count):
        outgoing = piece(place + count - step)
        if left_sum is not None:
            outgoing = outgoing + left_sum.astype(outgoing.dtype)
        left_sum = lax.ppermute(
            outgoing.astype(send_type), "tp", [(i, i + 1) for i in range(step)]
        )
        outgoing = piece(place - count + step)
        if right_sum is not None:
            outgoing = outgoing + right_sum.astype(outgoing.dtype)
        right_sum = lax.ppermute(
            outgoing.astype(send_type), "tp", [(i, i - 1) for i in range(count - step, count)]
        )
    own = piece(place)
    if left_sum is not None:
        own = own + left_sum.astype(own.dtype) + right_sum.astype(own.dtype)
    return own


def body(
    layer_in,
    query_proj,
    key_proj,
    value_proj,
    output_proj,
    attn_gain,
    query_gain,
    key_gain,
    ffn_gain,
    expert_gate,
    expert_up,
    expert_down,
    routes,
    route_weights,
    prefix_len,
    out_grad,
):
    tok_rows = layer_in.shape[0]
    width = layer_in.shape[1]
    group_rows = tok_rows * lax.axis_size("tp")
    seq_count = group_rows // SEQ
    factor = 1.0 / math.sqrt(HD)
    gain_sizes = (attn_gain.shape[0], query_gain.shape[0], key_gain.shape[0], ffn_gain.shape[0])
    kv_rows, kv_width = key_proj.shape
    gain_row = jnp.concatenate([attn_gain, query_gain, key_gain, ffn_gain])
    gain_block = jnp.zeros((8, 2 * kv_width), jnp.bfloat16).at[0, : gain_row.shape[0]].set(gain_row)
    packed = jnp.concatenate(
        [jnp.concatenate([key_proj, value_proj], axis=1), gain_block], axis=0
    )
    packed_all = lax.all_gather(packed, ("fsdp", "tp"), axis=0, tiled=False)
    kv_all = packed_all[:, :kv_rows].reshape(-1, 2 * kv_width)
    key_all = kv_all[:, :kv_width]
    value_all = kv_all[:, kv_width:]
    gain_all = packed_all[:, kv_rows]
    gains = []
    offset = 0
    for size in gain_sizes:
        gains.append(gain_all[:, offset : offset + size].reshape(-1))
        offset += size
    gain_attn, gain_query, gain_key, gain_ffn = gains
    gain_attn = gain_attn.astype(jnp.float32)
    gain_query = gain_query.astype(jnp.float32)
    gain_key = gain_key.astype(jnp.float32)
    gain_ffn = gain_ffn.astype(jnp.float32)
    query_w, out_w, gate_w, up_w, down_w = (
        lax.all_gather(query_proj, "fsdp", axis=0, tiled=True),
        lax.all_gather(output_proj, "fsdp", axis=1, tiled=True),
        lax.all_gather(expert_gate, "fsdp", axis=0, tiled=True),
        lax.all_gather(expert_up, "fsdp", axis=0, tiled=True),
        lax.all_gather(expert_down, "fsdp", axis=0, tiled=True),
    )
    per_dev = query_w.shape[1] // HD
    kv_head = lax.axis_index("tp") * per_dev // (HQ // HK)
    key_w = lax.dynamic_slice_in_dim(key_all, kv_head * HD, HD, 1)
    value_w = lax.dynamic_slice_in_dim(value_all, kv_head * HD, HD, 1)
    tokens_f = layer_in.astype(jnp.float32)
    tp_size = lax.axis_size("tp")
    layer_rows = tp_gather(layer_in, tp_size)
    attn_rows = rms_norm(layer_rows.astype(jnp.float32), gain_attn).astype(jnp.bfloat16)
    out_grad, attn_rows = lax.optimization_barrier((out_grad, attn_rows))
    grad_rows = tp_gather(out_grad, tp_size)
    query_raw = jnp.dot(attn_rows, query_w, preferred_element_type=jnp.float32)
    key_raw = jnp.dot(attn_rows, key_w, preferred_element_type=jnp.float32)
    value_rows = jnp.dot(attn_rows, value_w, preferred_element_type=jnp.float32).astype(
        jnp.bfloat16
    )
    cosine, sine = rotary_tables((lax.iota(jnp.int32, group_rows) % SEQ).astype(jnp.float32), HD)

    def prepare(query_in, key_in, weight_query, weight_key):
        query_heads = rms_norm(query_in.reshape(group_rows, per_dev, HD), weight_query)
        return (
            rotate(query_heads, cosine[:, None, :], sine[:, None, :]),
            rotate(rms_norm(key_in, weight_key), cosine, sine),
        )

    (query_norm, key_norm), prepare_back = jax.vjp(
        prepare, query_raw, key_raw, gain_query, gain_key
    )
    query_seq = query_norm.astype(jnp.bfloat16).reshape(seq_count, SEQ, per_dev, HD)
    key_seq = key_norm.astype(jnp.bfloat16).reshape(seq_count, SEQ, HD)
    value_seq = value_rows.reshape(seq_count, SEQ, HD)

    def attend(operands):
        queries, keys_b, values_b, prefix_end = operands
        scores = masked_scores(queries, keys_b, prefix_end, factor)
        highest = jnp.max(scores, axis=-1, keepdims=True)
        expo = jnp.exp(scores - highest)
        denom = jnp.sum(expo, axis=-1, keepdims=True)
        attn_probs = (expo / denom).astype(jnp.bfloat16)
        context = jnp.einsum(
            "hqk,kd->qhd", attn_probs, values_b, preferred_element_type=jnp.float32
        )
        return (context, (highest + jnp.log(denom))[..., 0])

    context_all, log_sums = lax.map(attend, (query_seq, key_seq, value_seq, prefix_len))
    context_b = context_all.reshape(group_rows, per_dev * HD).astype(jnp.bfloat16)
    context_b, grad_rows = lax.optimization_barrier((context_b, grad_rows))
    attn_out = tp_scatter_sum(
        jnp.dot(context_b, out_w, preferred_element_type=jnp.float32), tp_size, jnp.bfloat16
    )
    residual = tokens_f + attn_out
    ffn_in = rms_norm(residual, gain_ffn).astype(jnp.bfloat16)
    ffn_rows = tp_gather(ffn_in, tp_size)
    expert_count = gate_w.shape[0]
    chosen = routes[:, :, None] == lax.iota(jnp.int32, expert_count)[None, None, :]
    share = jnp.sum(jnp.where(chosen, route_weights[:, :, None], 0.0), axis=1)
    gate_val = jnp.einsum("td,edf->tef", ffn_rows, gate_w, preferred_element_type=jnp.float32)
    up_val = jnp.einsum("td,edf->tef", ffn_rows, up_w, preferred_element_type=jnp.float32)
    sigma = jax.nn.sigmoid(gate_val)
    active = gate_val * sigma
    hidden = (active * up_val).astype(jnp.bfloat16)
    hidden_share = (hidden.astype(jnp.float32) * share[:, :, None]).astype(jnp.bfloat16)
    mixture = jnp.einsum(
        "tef,efd->td", hidden_share, down_w, preferred_element_type=jnp.float32
    )
    grad_out = out_grad.astype(jnp.float32)
    hidden_grad = (
        jnp.einsum("td,efd->tef", grad_rows, down_w, preferred_element_type=jnp.float32)
        * share[:, :, None]
    )
    gate_back = (hidden_grad * up_val * sigma * (1.0 + gate_val * (1.0 - sigma))).astype(
        jnp.bfloat16
    )
    up_back = (hidden_grad * active).astype(jnp.bfloat16)
    ffn_in_grad = jnp.einsum(
        "tef,edf->td", gate_back, gate_w, preferred_element_type=jnp.float32
    ) + jnp.einsum("tef,edf->td", up_back, up_w, preferred_element_type=jnp.float32)
    gate_part = jnp.einsum("td,tef->edf", ffn_rows, gate_back, preferred_element_type=jnp.float32)
    up_part = jnp.einsum("td,tef->edf", ffn_rows, up_back, preferred_element_type=jnp.float32)
    down_part = jnp.einsum(
        "tef,td->efd", hidden_share, grad_rows, preferred_element_type=jnp.float32
    )
    ffn_in_own = tp_scatter_sum(ffn_in_grad, tp_size, jnp.bfloat16)
    _, second_back = jax.vjp(rms_norm, residual, gain_ffn)
    residual_norm_grad, ffn_gain_part = second_back(ffn_in_own)
    residual_grad = grad_out + residual_norm_grad
    gate_grad, up_grad, down_grad = (
        lax.psum_scatter(
            part.astype(jnp.bfloat16), "fsdp", scatter_dimension=0, tiled=True
        ).astype(jnp.float32)
        for part in (gate_part, up_part, down_part)
    )
    attn_out_grad = tp_gather(residual_grad.astype(jnp.bfloat16), tp_size)
    attn_out_grad, mixture = lax.optimization_barrier((attn_out_grad, mixture))
    mixture_own = tp_scatter_sum(mixture, tp_size, jnp.bfloat16)
    output_part = jnp.einsum(
        "gq,gd->qd", context_b, attn_out_grad, preferred_element_type=jnp.float32
    )
    context_grad = (
        jnp.einsum("gd,qd->gq", attn_out_grad, out_w, preferred_element_type=jnp.float32)
        .astype(jnp.bfloat16)
        .reshape(seq_count, SEQ, per_dev, HD)
    )

    def attend_back(operands):
        queries, keys_b, values_b, prefix_end, log_sum, ctx_grad = operands
        scores = masked_scores(queries, keys_b, prefix_end, factor)
        attn_probs = jnp.exp(scores - log_sum[..., None])
        value_grad = jnp.einsum(
            "hqk,qhd->kd",
            attn_probs.astype(jnp.bfloat16),
            ctx_grad,
            preferred_element_type=jnp.float32,
        )
        probs_grad = jnp.einsum(
            "qhd,kd->hqk", ctx_grad, values_b, preferred_element_type=jnp.float32
        )
        scores_grad = (
            attn_probs * (probs_grad - jnp.sum(attn_probs * probs_grad, axis=-1, keepdims=True))
        ).astype(jnp.bfloat16)
        query_grad = (
            jnp.einsum("hqk,kd->qhd", scores_grad, keys_b, preferred_element_type=jnp.float32)
            * factor
        )
        key_grad = (
            jnp.einsum("hqk,qhd->kd", scores_grad, queries, preferred_element_type=jnp.float32)
            * factor
        )
        return (query_grad, key_grad, value_grad)

    query_norm_grad, key_norm_grad, value_grad = lax.map(
        attend_back, (query_seq, key_seq, value_seq, prefix_len, log_sums, context_grad)
    )
    query_raw_grad, key_raw_grad, query_gain_part, key_gain_part = prepare_back(
        (query_norm_grad.reshape(group_rows, per_dev, HD), key_norm_grad.reshape(group_rows, HD))
    )
    query_back = query_raw_grad.astype(jnp.bfloat16)
    key_back = key_raw_grad.astype(jnp.bfloat16)
    value_back = value_grad.reshape(group_rows, HD).astype(jnp.bfloat16)
    result = jnp.einsum("gq,dq->gd", query_back, query_w, preferred_element_type=jnp.float32)
    result = result + jnp.einsum("gk,dk->gd", key_back, key_w, preferred_element_type=jnp.float32)
    attn_in_part = result + jnp.einsum(
        "gk,dk->gd", value_back, value_w, preferred_element_type=jnp.float32
    )
    attn_in_part, down_grad, gate_grad, up_grad, mixture_own = lax.optimization_barrier(
        (attn_in_part, down_grad, gate_grad, up_grad, mixture_own)
    )
    layer_out = (residual + mixture_own).astype(jnp.bfloat16)
    attn_in_grad = tp_scatter_sum(attn_in_part, tp_size, jnp.bfloat16)
    query_part = jnp.einsum("gd,gq->dq", attn_rows, query_back, preferred_element_type=jnp.float32)
    key_head_part = jnp.einsum("gd,gk->dk", attn_rows, key_back, preferred_element_type=jnp.float32)
    value_head_part = jnp.einsum(
        "gd,gk->dk", attn_rows, value_back, preferred_element_type=jnp.float32
    )
    _, first_back = jax.vjp(rms_norm, tokens_f, gain_attn)
    input_norm_grad, _ = first_back(attn_in_grad)
    _, rows_back = jax.vjp(
        lambda weight: rms_norm(layer_rows.astype(jnp.float32), weight), gain_attn
    )
    (attn_gain_part,) = rows_back(attn_in_part)
    in_grad = residual_grad + input_norm_grad
    fsdp_size = lax.axis_size("fsdp")
    query_proj_grad = jnp.sum(
        lax.all_to_all(
            query_part.astype(jnp.bfloat16).reshape(fsdp_size, -1, query_part.shape[1]),
            "fsdp",
            split_axis=0,
            concat_axis=0,
            tiled=True,
        ).astype(jnp.float32),
        axis=0,
    )
    output_proj_grad = jnp.sum(
        lax.all_to_all(
            output_part.astype(jnp.bfloat16)
            .reshape(output_part.shape[0], fsdp_size, -1)
            .transpose(1, 0, 2),
            "fsdp",
            split_axis=0,
            concat_axis=0,
            tiled=True,
        ).astype(jnp.float32),
        axis=0,
    )
    device_count = fsdp_size * tp_size
    gain_parts = (attn_gain_part, query_gain_part, key_gain_part, ffn_gain_part)
    gain_table = jnp.concatenate(
        [part.reshape(device_count, -1) for part in gain_parts], axis=1
    )
    gain_width = gain_table.shape[1]
    kv_full = jnp.concatenate([key_head_part, value_head_part], axis=1)
    block_rows = kv_full.shape[0] // fsdp_size
    sub_rows = block_rows // tp_size
    gain_rows = -(-(tp_size * gain_width) // (8 * 2 * HD)) * 8
    gain_block = jnp.pad(
        gain_table.reshape(fsdp_size, tp_size * gain_width),
        ((0, 0), (0, gain_rows * 2 * HD - tp_size * gain_width)),
    ).reshape(fsdp_size, gain_rows, 2 * HD)
    combined = jnp.concatenate(
        [kv_full.reshape(fsdp_size, block_rows, 2 * HD), gain_block], axis=1
    ).reshape(fsdp_size * (block_rows + gain_rows), 2 * HD)
    summed = lax.psum_scatter(combined, "fsdp", scatter_dimension=0, tiled=True)
    summed = jnp.concatenate(
        [
            summed[:block_rows].reshape(-1),
            summed[block_rows:].reshape(-1)[: tp_size * gain_width],
        ]
    )
    kv_local = summed[: block_rows * 2 * HD].reshape(tp_size, sub_rows * 2 * HD)
    gain_local = summed[block_rows * 2 * HD :].reshape(tp_size, gain_width)
    got = lax.all_to_all(
        jnp.concatenate([kv_local, gain_local], axis=1),
        "tp",
        split_axis=0,
        concat_axis=0,
        tiled=True,
    )
    kv_got = got[:, : sub_rows * 2 * HD].reshape(tp_size, sub_rows, 2 * HD)
    kv_got = jnp.sum(kv_got.reshape(HK, tp_size // HK, sub_rows, 2 * HD), axis=1)
    key_proj_grad = kv_got[:, :, :HD].transpose(1, 0, 2).reshape(sub_rows, HK * HD)
    value_proj_grad = kv_got[:, :, HD:].transpose(1, 0, 2).reshape(sub_rows, HK * HD)
    gain_sum = jnp.sum(got[:, sub_rows * 2 * HD :], axis=0)
    gain_grads = []
    offset = 0
    for part in gain_parts:
        size = part.shape[0] // device_count
        gain_grads.append(gain_sum[offset : offset + size])
        offset += size
    attn_gain_grad, query_gain_grad, key_gain_grad, ffn_gain_grad = gain_grads
    return (
        layer_out,
        in_grad,
        query_proj_grad,
        key_proj_grad,
        value_proj_grad,
        output_proj_grad,
        attn_gain_grad,
        query_gain_grad,
        key_gain_grad,
        ffn_gain_grad,
        gate_grad,
        up_grad,
        down_grad,
    )


def solution(mesh):
    in_specs = (
        P(("fsdp", "tp"), None),
        P("fsdp", "tp"),
        P(("fsdp", "tp"), None),
        P(("fsdp", "tp"), None),
        P("tp", "fsdp"),
        P(("fsdp", "tp")),
        P(("fsdp", "tp")),
        P(("fsdp", "tp")),
        P(("fsdp", "tp")),
        P("fsdp", None, "tp"),
        P("fsdp", None, "tp"),
        P("fsdp", "tp", None),
        P("fsdp", None),
        P("fsdp", None),
        P("fsdp"),
        P(("fsdp", "tp"), None),
    )
    out_specs = (
        P(("fsdp", "tp"), None),
        P(("fsdp", "tp"), None),
        P("fsdp", "tp"),
        P(("fsdp", "tp"), None),
        P(("fsdp", "tp"), None),
        P("tp", "fsdp"),
        P(("fsdp", "tp")),
        P(("fsdp", "tp")),
        P(("fsdp", "tp")),
        P(("fsdp", "tp")),
        P("fsdp", None, "tp"),
        P("fsdp", None, "tp"),
        P("fsdp", "tp", None),
    )
    return jax.shard_map(body, mesh=mesh, in_specs=in_specs, out_specs=out_specs, check_vma=False)
```

```python
import math

import jax
import jax.numpy as jnp
from jax import lax
from jax.sharding import PartitionSpec as P

HQ = 32
HK = 4
HD = 128
TOP = 8
SEQ = 1024


EPSILON = 1e-06


def rms_norm(values, weight):
    return values * lax.rsqrt(jnp.mean(values * values, axis=-1, keepdims=True) + EPSILON) * weight


def rotate(values, cosine, sine):
    half_width = values.shape[-1] // 2
    first_half = values[..., :half_width]
    second_half = values[..., half_width:]
    return jnp.concatenate(
        [first_half * cosine - second_half * sine, second_half * cosine + first_half * sine],
        axis=-1,
    )


def rotary_tables(positions, width):
    half_width = width // 2
    inverse = jnp.exp(
        -math.log(1000000.0) * 2.0 * jnp.arange(half_width, dtype=jnp.float32) / width
    )
    angles = positions[:, None] * inverse[None, :]
    return (jnp.cos(angles), jnp.sin(angles))


def masked_scores(queries, keys_b, prefix_end, factor):
    scores = jnp.einsum("qhd,kd->hqk", queries, keys_b, preferred_element_type=jnp.float32) * factor
    position = lax.iota(jnp.int32, queries.shape[0])
    allowed = (position[None, :] <= position[:, None]) | (position[None, :] < prefix_end)
    return jnp.where(allowed[None], scores, -1e30)


def tp_gather(block, count):
    place = lax.axis_index("tp")
    from_left = []
    from_right = []
    going_right = block
    going_left = block
    for step in range(1, count):
        going_right = lax.ppermute(
            going_right, "tp", [(i, i + 1) for i in range(step - 1, count - 1)]
        )
        going_left = lax.ppermute(going_left, "tp", [(i + 1, i) for i in range(0, count - step)])
        from_left.append(going_right)
        from_right.append(going_left)
    stacked = jnp.stack(from_left[::-1] + [block] + from_right, axis=0)
    picked = lax.dynamic_slice_in_dim(stacked, count - 1 - place, count, 0)
    return picked.reshape((count * block.shape[0],) + block.shape[1:])


def tp_scatter_sum(partial, count, send_type):
    place = lax.axis_index("tp")
    rows = partial.shape[0] // count
    pieces = partial.reshape((count, rows) + partial.shape[1:])

    def piece(target):
        return lax.dynamic_index_in_dim(pieces, jnp.clip(target, 0, count - 1), 0, keepdims=False)

    left_sum = None
    right_sum = None
    for step in range(1, count):
        outgoing = piece(place + count - step)
        if left_sum is not None:
            outgoing = outgoing + left_sum.astype(outgoing.dtype)
        left_sum = lax.ppermute(
            outgoing.astype(send_type), "tp", [(i, i + 1) for i in range(step)]
        )
        outgoing = piece(place - count + step)
        if right_sum is not None:
            outgoing = outgoing + right_sum.astype(outgoing.dtype)
        right_sum = lax.ppermute(
            outgoing.astype(send_type), "tp", [(i, i - 1) for i in range(count - step, count)]
        )
    own = piece(place)
    if left_sum is not None:
        own = own + left_sum.astype(own.dtype) + right_sum.astype(own.dtype)
    return own


def body(
    layer_in,
    query_proj,
    key_proj,
    value_proj,
    output_proj,
    attn_gain,
    query_gain,
    key_gain,
    ffn_gain,
    expert_gate,
    expert_up,
    expert_down,
    routes,
    route_weights,
    prefix_len,
    out_grad,
):
    tok_rows = layer_in.shape[0]
    width = layer_in.shape[1]
    group_rows = tok_rows * lax.axis_size("tp")
    seq_count = group_rows // SEQ
    factor = 1.0 / math.sqrt(HD)
    gain_sizes = (attn_gain.shape[0], query_gain.shape[0], key_gain.shape[0], ffn_gain.shape[0])
    kv_rows, kv_width = key_proj.shape
    gain_row = jnp.concatenate([attn_gain, query_gain, key_gain, ffn_gain])
    gain_block = jnp.zeros((8, 2 * kv_width), jnp.bfloat16).at[0, : gain_row.shape[0]].set(gain_row)
    packed = jnp.concatenate(
        [jnp.concatenate([key_proj, value_proj], axis=1), gain_block], axis=0
    )
    packed_all = lax.all_gather(packed, ("fsdp", "tp"), axis=0, tiled=False)
    kv_all = packed_all[:, :kv_rows].reshape(-1, 2 * kv_width)
    key_all = kv_all[:, :kv_width]
    value_all = kv_all[:, kv_width:]
    gain_all = packed_all[:, kv_rows]
    gains = []
    offset = 0
    for size in gain_sizes:
        gains.append(gain_all[:, offset : offset + size].reshape(-1))
        offset += size
    gain_attn, gain_query, gain_key, gain_ffn = gains
    gain_attn = gain_attn.astype(jnp.float32)
    gain_query = gain_query.astype(jnp.float32)
    gain_key = gain_key.astype(jnp.float32)
    gain_ffn = gain_ffn.astype(jnp.float32)
    query_w, out_w, gate_w, up_w, down_w = (
        lax.all_gather(query_proj, "fsdp", axis=0, tiled=True),
        lax.all_gather(output_proj, "fsdp", axis=1, tiled=True),
        lax.all_gather(expert_gate, "fsdp", axis=0, tiled=True),
        lax.all_gather(expert_up, "fsdp", axis=0, tiled=True),
        lax.all_gather(expert_down, "fsdp", axis=0, tiled=True),
    )
    per_dev = query_w.shape[1] // HD
    kv_head = lax.axis_index("tp") * per_dev // (HQ // HK)
    key_w = lax.dynamic_slice_in_dim(key_all, kv_head * HD, HD, 1)
    value_w = lax.dynamic_slice_in_dim(value_all, kv_head * HD, HD, 1)
    tokens_f = layer_in.astype(jnp.float32)
    tp_size = lax.axis_size("tp")
    layer_rows = tp_gather(layer_in, tp_size)
    attn_rows = rms_norm(layer_rows.astype(jnp.float32), gain_attn).astype(jnp.bfloat16)
    out_grad, attn_rows = lax.optimization_barrier((out_grad, attn_rows))
    grad_rows = tp_gather(out_grad, tp_size)
    query_raw = jnp.dot(attn_rows, query_w, preferred_element_type=jnp.float32)
    key_raw = jnp.dot(attn_rows, key_w, preferred_element_type=jnp.float32)
    value_rows = jnp.dot(attn_rows, value_w, preferred_element_type=jnp.float32).astype(
        jnp.bfloat16
    )
    cosine, sine = rotary_tables((lax.iota(jnp.int32, group_rows) % SEQ).astype(jnp.float32), HD)

    def prepare(query_in, key_in, weight_query, weight_key):
        query_heads = rms_norm(query_in.reshape(group_rows, per_dev, HD), weight_query)
        return (
            rotate(query_heads, cosine[:, None, :], sine[:, None, :]),
            rotate(rms_norm(key_in, weight_key), cosine, sine),
        )

    (query_norm, key_norm), prepare_back = jax.vjp(
        prepare, query_raw, key_raw, gain_query, gain_key
    )
    query_seq = query_norm.astype(jnp.bfloat16).reshape(seq_count, SEQ, per_dev, HD)
    key_seq = key_norm.astype(jnp.bfloat16).reshape(seq_count, SEQ, HD)
    value_seq = value_rows.reshape(seq_count, SEQ, HD)

    def attend(operands):
        queries, keys_b, values_b, prefix_end = operands
        scores = masked_scores(queries, keys_b, prefix_end, factor)
        highest = jnp.max(scores, axis=-1, keepdims=True)
        expo = jnp.exp(scores - highest)
        denom = jnp.sum(expo, axis=-1, keepdims=True)
        attn_probs = (expo / denom).astype(jnp.bfloat16)
        context = jnp.einsum(
            "hqk,kd->qhd", attn_probs, values_b, preferred_element_type=jnp.float32
        )
        return (context, (highest + jnp.log(denom))[..., 0])

    context_all, log_sums = lax.map(attend, (query_seq, key_seq, value_seq, prefix_len))
    context_b = context_all.reshape(group_rows, per_dev * HD).astype(jnp.bfloat16)
    context_b, grad_rows = lax.optimization_barrier((context_b, grad_rows))
    attn_out = tp_scatter_sum(
        jnp.dot(context_b, out_w, preferred_element_type=jnp.float32), tp_size, jnp.bfloat16
    )
    residual = tokens_f + attn_out
    ffn_in = rms_norm(residual, gain_ffn).astype(jnp.bfloat16)
    expert_count = gate_w.shape[0]
    chosen = routes[:, :, None] == lax.iota(jnp.int32, expert_count)[None, None, :]
    share_all = jnp.sum(jnp.where(chosen, route_weights[:, :, None], 0.0), axis=1)
    grad_out = out_grad.astype(jnp.float32)
    chunks = 2
    chunk_rows = tok_rows // chunks

    def chunk_of(rows_all, index):
        split = rows_all.reshape((tp_size, chunks, chunk_rows) + rows_all.shape[1:])
        return split[:, index].reshape((tp_size * chunk_rows,) + rows_all.shape[1:])

    rows_list = []
    share_list = []
    grad_list = []
    hidden_list = []
    gate_list = []
    up_list = []
    mixture_list = []
    in_grad_list = []
    previous_rows = None
    previous_grad = None
    for index in range(chunks):
        ffn_piece = ffn_in[index * chunk_rows : (index + 1) * chunk_rows]
        if previous_rows is not None:
            ffn_piece, previous_rows = lax.optimization_barrier((ffn_piece, previous_rows))
            rows_list[-1] = previous_rows
        ffn_rows = tp_gather(ffn_piece, tp_size)
        if previous_grad is not None:
            ffn_rows, previous_grad = lax.optimization_barrier((ffn_rows, previous_grad))
            in_grad_list[-1] = tp_scatter_sum(previous_grad, tp_size, jnp.bfloat16)
        share = chunk_of(share_all, index)
        grad_part = chunk_of(grad_rows, index)
        gate_val = jnp.einsum(
            "td,edf->tef", ffn_rows, gate_w, preferred_element_type=jnp.float32
        )
        up_val = jnp.einsum("td,edf->tef", ffn_rows, up_w, preferred_element_type=jnp.float32)
        sigma = jax.nn.sigmoid(gate_val)
        active = gate_val * sigma
        hidden = (active * up_val).astype(jnp.bfloat16)
        hidden_share = (hidden.astype(jnp.float32) * share[:, :, None]).astype(jnp.bfloat16)
        mixture = jnp.einsum(
            "tef,efd->td", hidden_share, down_w, preferred_element_type=jnp.float32
        )
        hidden_grad = (
            jnp.einsum("td,efd->tef", grad_part, down_w, preferred_element_type=jnp.float32)
            * share[:, :, None]
        )
        gate_back = (hidden_grad * up_val * sigma * (1.0 + gate_val * (1.0 - sigma))).astype(
            jnp.bfloat16
        )
        up_back = (hidden_grad * active).astype(jnp.bfloat16)
        ffn_in_grad = jnp.einsum(
            "tef,edf->td", gate_back, gate_w, preferred_element_type=jnp.float32
        ) + jnp.einsum("tef,edf->td", up_back, up_w, preferred_element_type=jnp.float32)
        in_grad_list.append(None)
        previous_grad = ffn_in_grad
        mixture_list.append(mixture)
        rows_list.append(ffn_rows)
        previous_rows = ffn_rows
        grad_list.append(grad_part)
        hidden_list.append(hidden_share)
        gate_list.append(gate_back)
        up_list.append(up_back)
    in_grad_list[-1] = tp_scatter_sum(previous_grad, tp_size, jnp.bfloat16)
    ffn_rows = jnp.concatenate(rows_list, axis=0)
    gate_back = jnp.concatenate(gate_list, axis=0)
    up_back = jnp.concatenate(up_list, axis=0)
    hidden_share = jnp.concatenate(hidden_list, axis=0)
    grad_part = jnp.concatenate(grad_list, axis=0)
    gate_part = jnp.einsum("td,tef->edf", ffn_rows, gate_back, preferred_element_type=jnp.float32)
    up_part = jnp.einsum("td,tef->edf", ffn_rows, up_back, preferred_element_type=jnp.float32)
    down_part = jnp.einsum(
        "tef,td->efd", hidden_share, grad_part, preferred_element_type=jnp.float32
    )
    mixture_own = jnp.concatenate(
        [tp_scatter_sum(part, tp_size, jnp.bfloat16) for part in mixture_list], axis=0
    )
    ffn_in_own = jnp.concatenate(in_grad_list, axis=0)
    _, second_back = jax.vjp(rms_norm, residual, gain_ffn)
    residual_norm_grad, ffn_gain_part = second_back(ffn_in_own)
    residual_grad = grad_out + residual_norm_grad
    residual_grad, mixture_own = lax.optimization_barrier((residual_grad, mixture_own))
    gate_grad, up_grad, down_grad = (
        lax.psum_scatter(
            part.astype(jnp.bfloat16), "fsdp", scatter_dimension=0, tiled=True
        ).astype(jnp.float32)
        for part in (gate_part, up_part, down_part)
    )
    layer_out = (residual + mixture_own).astype(jnp.bfloat16)
    attn_out_grad = tp_gather(residual_grad.astype(jnp.bfloat16), tp_size)
    output_part = jnp.einsum(
        "gq,gd->qd", context_b, attn_out_grad, preferred_element_type=jnp.float32
    )
    context_grad = (
        jnp.einsum("gd,qd->gq", attn_out_grad, out_w, preferred_element_type=jnp.float32)
        .astype(jnp.bfloat16)
        .reshape(seq_count, SEQ, per_dev, HD)
    )

    def attend_back(operands):
        queries, keys_b, values_b, prefix_end, log_sum, ctx_grad = operands
        scores = masked_scores(queries, keys_b, prefix_end, factor)
        attn_probs = jnp.exp(scores - log_sum[..., None])
        value_grad = jnp.einsum(
            "hqk,qhd->kd",
            attn_probs.astype(jnp.bfloat16),
            ctx_grad,
            preferred_element_type=jnp.float32,
        )
        probs_grad = jnp.einsum(
            "qhd,kd->hqk", ctx_grad, values_b, preferred_element_type=jnp.float32
        )
        scores_grad = (
            attn_probs * (probs_grad - jnp.sum(attn_probs * probs_grad, axis=-1, keepdims=True))
        ).astype(jnp.bfloat16)
        query_grad = (
            jnp.einsum("hqk,kd->qhd", scores_grad, keys_b, preferred_element_type=jnp.float32)
            * factor
        )
        key_grad = (
            jnp.einsum("hqk,qhd->kd", scores_grad, queries, preferred_element_type=jnp.float32)
            * factor
        )
        return (query_grad, key_grad, value_grad)

    query_norm_grad, key_norm_grad, value_grad = lax.map(
        attend_back, (query_seq, key_seq, value_seq, prefix_len, log_sums, context_grad)
    )
    query_raw_grad, key_raw_grad, query_gain_part, key_gain_part = prepare_back(
        (query_norm_grad.reshape(group_rows, per_dev, HD), key_norm_grad.reshape(group_rows, HD))
    )
    query_back = query_raw_grad.astype(jnp.bfloat16)
    key_back = key_raw_grad.astype(jnp.bfloat16)
    value_back = value_grad.reshape(group_rows, HD).astype(jnp.bfloat16)
    result = jnp.einsum("gq,dq->gd", query_back, query_w, preferred_element_type=jnp.float32)
    result = result + jnp.einsum("gk,dk->gd", key_back, key_w, preferred_element_type=jnp.float32)
    attn_in_part = result + jnp.einsum(
        "gk,dk->gd", value_back, value_w, preferred_element_type=jnp.float32
    )
    attn_in_part, down_grad, gate_grad, up_grad = lax.optimization_barrier(
        (attn_in_part, down_grad, gate_grad, up_grad)
    )
    attn_in_grad = tp_scatter_sum(attn_in_part, tp_size, jnp.bfloat16)
    query_part = jnp.einsum("gd,gq->dq", attn_rows, query_back, preferred_element_type=jnp.float32)
    key_head_part = jnp.einsum("gd,gk->dk", attn_rows, key_back, preferred_element_type=jnp.float32)
    value_head_part = jnp.einsum(
        "gd,gk->dk", attn_rows, value_back, preferred_element_type=jnp.float32
    )
    _, first_back = jax.vjp(rms_norm, tokens_f, gain_attn)
    input_norm_grad, _ = first_back(attn_in_grad)
    _, rows_back = jax.vjp(
        lambda weight: rms_norm(layer_rows.astype(jnp.float32), weight), gain_attn
    )
    (attn_gain_part,) = rows_back(attn_in_part)
    in_grad = residual_grad + input_norm_grad
    fsdp_size = lax.axis_size("fsdp")
    query_proj_grad = jnp.sum(
        lax.all_to_all(
            query_part.astype(jnp.bfloat16).reshape(fsdp_size, -1, query_part.shape[1]),
            "fsdp",
            split_axis=0,
            concat_axis=0,
            tiled=True,
        ).astype(jnp.float32),
        axis=0,
    )
    output_proj_grad = jnp.sum(
        lax.all_to_all(
            output_part.astype(jnp.bfloat16)
            .reshape(output_part.shape[0], fsdp_size, -1)
            .transpose(1, 0, 2),
            "fsdp",
            split_axis=0,
            concat_axis=0,
            tiled=True,
        ).astype(jnp.float32),
        axis=0,
    )
    device_count = fsdp_size * tp_size
    gain_parts = (attn_gain_part, query_gain_part, key_gain_part, ffn_gain_part)
    gain_table = jnp.concatenate(
        [part.reshape(device_count, -1) for part in gain_parts], axis=1
    )
    gain_width = gain_table.shape[1]
    kv_full = jnp.concatenate([key_head_part, value_head_part], axis=1)
    block_rows = kv_full.shape[0] // fsdp_size
    sub_rows = block_rows // tp_size
    gain_rows = -(-(tp_size * gain_width) // (8 * 2 * HD)) * 8
    gain_block = jnp.pad(
        gain_table.reshape(fsdp_size, tp_size * gain_width),
        ((0, 0), (0, gain_rows * 2 * HD - tp_size * gain_width)),
    ).reshape(fsdp_size, gain_rows, 2 * HD)
    combined = jnp.concatenate(
        [kv_full.reshape(fsdp_size, block_rows, 2 * HD), gain_block], axis=1
    ).reshape(fsdp_size * (block_rows + gain_rows), 2 * HD)
    summed = lax.psum_scatter(combined, "fsdp", scatter_dimension=0, tiled=True)
    summed = jnp.concatenate(
        [
            summed[:block_rows].reshape(-1),
            summed[block_rows:].reshape(-1)[: tp_size * gain_width],
        ]
    )
    kv_local = summed[: block_rows * 2 * HD].reshape(tp_size, sub_rows * 2 * HD)
    gain_local = summed[block_rows * 2 * HD :].reshape(tp_size, gain_width)
    got = lax.all_to_all(
        jnp.concatenate([kv_local, gain_local], axis=1),
        "tp",
        split_axis=0,
        concat_axis=0,
        tiled=True,
    )
    kv_got = got[:, : sub_rows * 2 * HD].reshape(tp_size, sub_rows, 2 * HD)
    kv_got = jnp.sum(kv_got.reshape(HK, tp_size // HK, sub_rows, 2 * HD), axis=1)
    key_proj_grad = kv_got[:, :, :HD].transpose(1, 0, 2).reshape(sub_rows, HK * HD)
    value_proj_grad = kv_got[:, :, HD:].transpose(1, 0, 2).reshape(sub_rows, HK * HD)
    gain_sum = jnp.sum(got[:, sub_rows * 2 * HD :], axis=0)
    gain_grads = []
    offset = 0
    for part in gain_parts:
        size = part.shape[0] // device_count
        gain_grads.append(gain_sum[offset : offset + size])
        offset += size
    attn_gain_grad, query_gain_grad, key_gain_grad, ffn_gain_grad = gain_grads
    return (
        layer_out,
        in_grad,
        query_proj_grad,
        key_proj_grad,
        value_proj_grad,
        output_proj_grad,
        attn_gain_grad,
        query_gain_grad,
        key_gain_grad,
        ffn_gain_grad,
        gate_grad,
        up_grad,
        down_grad,
    )


def solution(mesh):
    in_specs = (
        P(("fsdp", "tp"), None),
        P("fsdp", "tp"),
        P(("fsdp", "tp"), None),
        P(("fsdp", "tp"), None),
        P("tp", "fsdp"),
        P(("fsdp", "tp")),
        P(("fsdp", "tp")),
        P(("fsdp", "tp")),
        P(("fsdp", "tp")),
        P("fsdp", None, "tp"),
        P("fsdp", None, "tp"),
        P("fsdp", "tp", None),
        P("fsdp", None),
        P("fsdp", None),
        P("fsdp"),
        P(("fsdp", "tp"), None),
    )
    out_specs = (
        P(("fsdp", "tp"), None),
        P(("fsdp", "tp"), None),
        P("fsdp", "tp"),
        P(("fsdp", "tp"), None),
        P(("fsdp", "tp"), None),
        P("tp", "fsdp"),
        P(("fsdp", "tp")),
        P(("fsdp", "tp")),
        P(("fsdp", "tp")),
        P(("fsdp", "tp")),
        P("fsdp", None, "tp"),
        P("fsdp", None, "tp"),
        P("fsdp", "tp", None),
    )
    return jax.shard_map(body, mesh=mesh, in_specs=in_specs, out_specs=out_specs, check_vma=False)
```

```python
import math

import jax
import jax.numpy as jnp
from jax import lax
from jax.sharding import PartitionSpec as P

HQ = 32
HK = 4
HD = 128
TOP = 8
SEQ = 1024


EPSILON = 1e-06


def rms_norm(values, weight):
    return values * lax.rsqrt(jnp.mean(values * values, axis=-1, keepdims=True) + EPSILON) * weight


def rotate(values, cosine, sine):
    half_width = values.shape[-1] // 2
    first_half = values[..., :half_width]
    second_half = values[..., half_width:]
    return jnp.concatenate(
        [first_half * cosine - second_half * sine, second_half * cosine + first_half * sine],
        axis=-1,
    )


def rotary_tables(positions, width):
    half_width = width // 2
    inverse = jnp.exp(
        -math.log(1000000.0) * 2.0 * jnp.arange(half_width, dtype=jnp.float32) / width
    )
    angles = positions[:, None] * inverse[None, :]
    return (jnp.cos(angles), jnp.sin(angles))


def masked_scores(queries, keys_b, prefix_end, factor):
    scores = jnp.einsum("qhd,kd->hqk", queries, keys_b, preferred_element_type=jnp.float32) * factor
    position = lax.iota(jnp.int32, queries.shape[0])
    allowed = (position[None, :] <= position[:, None]) | (position[None, :] < prefix_end)
    return jnp.where(allowed[None], scores, -1e30)


def tp_gather(block, count):
    place = lax.axis_index("tp")
    from_left = []
    from_right = []
    going_right = block
    going_left = block
    for step in range(1, count):
        going_right = lax.ppermute(
            going_right, "tp", [(i, i + 1) for i in range(step - 1, count - 1)]
        )
        going_left = lax.ppermute(going_left, "tp", [(i + 1, i) for i in range(0, count - step)])
        from_left.append(going_right)
        from_right.append(going_left)
    stacked = jnp.stack(from_left[::-1] + [block] + from_right, axis=0)
    picked = lax.dynamic_slice_in_dim(stacked, count - 1 - place, count, 0)
    return picked.reshape((count * block.shape[0],) + block.shape[1:])


def tp_scatter_sum(partial, count, send_type):
    place = lax.axis_index("tp")
    rows = partial.shape[0] // count
    pieces = partial.reshape((count, rows) + partial.shape[1:])

    def piece(target):
        return lax.dynamic_index_in_dim(pieces, jnp.clip(target, 0, count - 1), 0, keepdims=False)

    left_sum = None
    right_sum = None
    for step in range(1, count):
        outgoing = piece(place + count - step)
        if left_sum is not None:
            outgoing = outgoing + left_sum.astype(outgoing.dtype)
        left_sum = lax.ppermute(
            outgoing.astype(send_type), "tp", [(i, i + 1) for i in range(step)]
        )
        outgoing = piece(place - count + step)
        if right_sum is not None:
            outgoing = outgoing + right_sum.astype(outgoing.dtype)
        right_sum = lax.ppermute(
            outgoing.astype(send_type), "tp", [(i, i - 1) for i in range(count - step, count)]
        )
    own = piece(place)
    if left_sum is not None:
        own = own + left_sum.astype(own.dtype) + right_sum.astype(own.dtype)
    return own


def body(
    layer_in,
    query_proj,
    key_proj,
    value_proj,
    output_proj,
    attn_gain,
    query_gain,
    key_gain,
    ffn_gain,
    expert_gate,
    expert_up,
    expert_down,
    routes,
    route_weights,
    prefix_len,
    out_grad,
):
    tok_rows = layer_in.shape[0]
    width = layer_in.shape[1]
    group_rows = tok_rows * lax.axis_size("tp")
    seq_count = group_rows // SEQ
    factor = 1.0 / math.sqrt(HD)
    gain_sizes = (attn_gain.shape[0], query_gain.shape[0], key_gain.shape[0], ffn_gain.shape[0])
    kv_rows, kv_width = key_proj.shape
    gain_row = jnp.concatenate([attn_gain, query_gain, key_gain, ffn_gain])
    gain_block = jnp.zeros((8, 2 * kv_width), jnp.bfloat16).at[0, : gain_row.shape[0]].set(gain_row)
    packed = jnp.concatenate(
        [jnp.concatenate([key_proj, value_proj], axis=1), gain_block], axis=0
    )
    packed_all = lax.all_gather(packed, ("fsdp", "tp"), axis=0, tiled=False)
    kv_all = packed_all[:, :kv_rows].reshape(-1, 2 * kv_width)
    key_all = kv_all[:, :kv_width]
    value_all = kv_all[:, kv_width:]
    gain_all = packed_all[:, kv_rows]
    gains = []
    offset = 0
    for size in gain_sizes:
        gains.append(gain_all[:, offset : offset + size].reshape(-1))
        offset += size
    gain_attn, gain_query, gain_key, gain_ffn = gains
    gain_attn = gain_attn.astype(jnp.float32)
    gain_query = gain_query.astype(jnp.float32)
    gain_key = gain_key.astype(jnp.float32)
    gain_ffn = gain_ffn.astype(jnp.float32)
    query_w, out_w, gate_w, up_w, down_w = (
        lax.all_gather(query_proj, "fsdp", axis=0, tiled=True),
        lax.all_gather(output_proj, "fsdp", axis=1, tiled=True),
        lax.all_gather(expert_gate, "fsdp", axis=0, tiled=True),
        lax.all_gather(expert_up, "fsdp", axis=0, tiled=True),
        lax.all_gather(expert_down, "fsdp", axis=0, tiled=True),
    )
    per_dev = query_w.shape[1] // HD
    kv_head = lax.axis_index("tp") * per_dev // (HQ // HK)
    key_w = lax.dynamic_slice_in_dim(key_all, kv_head * HD, HD, 1)
    value_w = lax.dynamic_slice_in_dim(value_all, kv_head * HD, HD, 1)
    tokens_f = layer_in.astype(jnp.float32)
    tp_size = lax.axis_size("tp")
    layer_rows = tp_gather(layer_in, tp_size)
    attn_rows = rms_norm(layer_rows.astype(jnp.float32), gain_attn).astype(jnp.bfloat16)
    out_grad, attn_rows = lax.optimization_barrier((out_grad, attn_rows))
    grad_rows = tp_gather(out_grad, tp_size)
    query_raw = jnp.dot(attn_rows, query_w, preferred_element_type=jnp.float32)
    key_raw = jnp.dot(attn_rows, key_w, preferred_element_type=jnp.float32)
    value_rows = jnp.dot(attn_rows, value_w, preferred_element_type=jnp.float32).astype(
        jnp.bfloat16
    )
    cosine, sine = rotary_tables((lax.iota(jnp.int32, group_rows) % SEQ).astype(jnp.float32), HD)

    def prepare(query_in, key_in, weight_query, weight_key):
        query_heads = rms_norm(query_in.reshape(group_rows, per_dev, HD), weight_query)
        return (
            rotate(query_heads, cosine[:, None, :], sine[:, None, :]),
            rotate(rms_norm(key_in, weight_key), cosine, sine),
        )

    (query_norm, key_norm), prepare_back = jax.vjp(
        prepare, query_raw, key_raw, gain_query, gain_key
    )
    query_seq = query_norm.astype(jnp.bfloat16).reshape(seq_count, SEQ, per_dev, HD)
    key_seq = key_norm.astype(jnp.bfloat16).reshape(seq_count, SEQ, HD)
    value_seq = value_rows.reshape(seq_count, SEQ, HD)

    def attend(operands):
        queries, keys_b, values_b, prefix_end = operands
        scores = masked_scores(queries, keys_b, prefix_end, factor)
        highest = jnp.max(scores, axis=-1, keepdims=True)
        expo = jnp.exp(scores - highest)
        denom = jnp.sum(expo, axis=-1, keepdims=True)
        attn_probs = (expo / denom).astype(jnp.bfloat16)
        context = jnp.einsum(
            "hqk,kd->qhd", attn_probs, values_b, preferred_element_type=jnp.float32
        )
        return (context, (highest + jnp.log(denom))[..., 0])

    context_all, log_sums = lax.map(attend, (query_seq, key_seq, value_seq, prefix_len))
    context_b = context_all.reshape(group_rows, per_dev * HD).astype(jnp.bfloat16)
    context_b, grad_rows = lax.optimization_barrier((context_b, grad_rows))
    attn_out = tp_scatter_sum(
        jnp.dot(context_b, out_w, preferred_element_type=jnp.float32), tp_size, jnp.bfloat16
    )
    residual = tokens_f + attn_out
    ffn_in = rms_norm(residual, gain_ffn).astype(jnp.bfloat16)
    ffn_rows = tp_gather(ffn_in, tp_size)
    expert_count = gate_w.shape[0]
    chosen = routes[:, :, None] == lax.iota(jnp.int32, expert_count)[None, None, :]
    share = jnp.sum(jnp.where(chosen, route_weights[:, :, None], 0.0), axis=1)
    gate_val = jnp.einsum("td,edf->tef", ffn_rows, gate_w, preferred_element_type=jnp.float32)
    up_val = jnp.einsum("td,edf->tef", ffn_rows, up_w, preferred_element_type=jnp.float32)
    sigma = jax.nn.sigmoid(gate_val)
    active = gate_val * sigma
    hidden = (active * up_val).astype(jnp.bfloat16)
    hidden_share = (hidden.astype(jnp.float32) * share[:, :, None]).astype(jnp.bfloat16)
    mixture = jnp.einsum(
        "tef,efd->td", hidden_share, down_w, preferred_element_type=jnp.float32
    )
    mixture_own = tp_scatter_sum(mixture, tp_size, jnp.bfloat16)
    grad_out = out_grad.astype(jnp.float32)
    hidden_grad = (
        jnp.einsum("td,efd->tef", grad_rows, down_w, preferred_element_type=jnp.float32)
        * share[:, :, None]
    )
    gate_back = (hidden_grad * up_val * sigma * (1.0 + gate_val * (1.0 - sigma))).astype(
        jnp.bfloat16
    )
    up_back = (hidden_grad * active).astype(jnp.bfloat16)
    gate_tied, up_tied, mixture_own = lax.optimization_barrier((gate_back, up_back, mixture_own))
    ffn_in_grad = jnp.einsum(
        "tef,edf->td", gate_tied, gate_w, preferred_element_type=jnp.float32
    ) + jnp.einsum("tef,edf->td", up_tied, up_w, preferred_element_type=jnp.float32)
    gate_part = jnp.einsum("td,tef->edf", ffn_rows, gate_back, preferred_element_type=jnp.float32)
    up_part = jnp.einsum("td,tef->edf", ffn_rows, up_back, preferred_element_type=jnp.float32)
    down_part = jnp.einsum(
        "tef,td->efd", hidden_share, grad_rows, preferred_element_type=jnp.float32
    )
    ffn_in_own = tp_scatter_sum(ffn_in_grad, tp_size, jnp.bfloat16)
    _, second_back = jax.vjp(rms_norm, residual, gain_ffn)
    residual_norm_grad, ffn_gain_part = second_back(ffn_in_own)
    residual_grad = grad_out + residual_norm_grad
    residual_grad, mixture_own = lax.optimization_barrier((residual_grad, mixture_own))
    gate_grad, up_grad, down_grad = (
        lax.psum_scatter(
            part.astype(jnp.bfloat16), "fsdp", scatter_dimension=0, tiled=True
        ).astype(jnp.float32)
        for part in (gate_part, up_part, down_part)
    )
    layer_out = (residual + mixture_own).astype(jnp.bfloat16)
    attn_out_grad = tp_gather(residual_grad.astype(jnp.bfloat16), tp_size)
    output_part = jnp.einsum(
        "gq,gd->qd", context_b, attn_out_grad, preferred_element_type=jnp.float32
    )
    context_grad = (
        jnp.einsum("gd,qd->gq", attn_out_grad, out_w, preferred_element_type=jnp.float32)
        .astype(jnp.bfloat16)
        .reshape(seq_count, SEQ, per_dev, HD)
    )

    def attend_back(operands):
        queries, keys_b, values_b, prefix_end, log_sum, ctx_grad = operands
        scores = masked_scores(queries, keys_b, prefix_end, factor)
        attn_probs = jnp.exp(scores - log_sum[..., None])
        value_grad = jnp.einsum(
            "hqk,qhd->kd",
            attn_probs.astype(jnp.bfloat16),
            ctx_grad,
            preferred_element_type=jnp.float32,
        )
        probs_grad = jnp.einsum(
            "qhd,kd->hqk", ctx_grad, values_b, preferred_element_type=jnp.float32
        )
        scores_grad = (
            attn_probs * (probs_grad - jnp.sum(attn_probs * probs_grad, axis=-1, keepdims=True))
        ).astype(jnp.bfloat16)
        query_grad = (
            jnp.einsum("hqk,kd->qhd", scores_grad, keys_b, preferred_element_type=jnp.float32)
            * factor
        )
        key_grad = (
            jnp.einsum("hqk,qhd->kd", scores_grad, queries, preferred_element_type=jnp.float32)
            * factor
        )
        return (query_grad, key_grad, value_grad)

    query_norm_grad, key_norm_grad, value_grad = lax.map(
        attend_back, (query_seq, key_seq, value_seq, prefix_len, log_sums, context_grad)
    )
    query_raw_grad, key_raw_grad, query_gain_part, key_gain_part = prepare_back(
        (query_norm_grad.reshape(group_rows, per_dev, HD), key_norm_grad.reshape(group_rows, HD))
    )
    query_back = query_raw_grad.astype(jnp.bfloat16)
    key_back = key_raw_grad.astype(jnp.bfloat16)
    value_back = value_grad.reshape(group_rows, HD).astype(jnp.bfloat16)
    result = jnp.einsum("gq,dq->gd", query_back, query_w, preferred_element_type=jnp.float32)
    result = result + jnp.einsum("gk,dk->gd", key_back, key_w, preferred_element_type=jnp.float32)
    attn_in_part = result + jnp.einsum(
        "gk,dk->gd", value_back, value_w, preferred_element_type=jnp.float32
    )
    attn_in_part, down_grad, gate_grad, up_grad = lax.optimization_barrier(
        (attn_in_part, down_grad, gate_grad, up_grad)
    )
    attn_in_grad = tp_scatter_sum(attn_in_part, tp_size, jnp.bfloat16)
    query_part = jnp.einsum("gd,gq->dq", attn_rows, query_back, preferred_element_type=jnp.float32)
    key_head_part = jnp.einsum("gd,gk->dk", attn_rows, key_back, preferred_element_type=jnp.float32)
    value_head_part = jnp.einsum(
        "gd,gk->dk", attn_rows, value_back, preferred_element_type=jnp.float32
    )
    _, first_back = jax.vjp(rms_norm, tokens_f, gain_attn)
    input_norm_grad, _ = first_back(attn_in_grad)
    _, rows_back = jax.vjp(
        lambda weight: rms_norm(layer_rows.astype(jnp.float32), weight), gain_attn
    )
    (attn_gain_part,) = rows_back(attn_in_part)
    in_grad = residual_grad + input_norm_grad
    fsdp_size = lax.axis_size("fsdp")
    query_proj_grad = jnp.sum(
        lax.all_to_all(
            query_part.astype(jnp.bfloat16).reshape(fsdp_size, -1, query_part.shape[1]),
            "fsdp",
            split_axis=0,
            concat_axis=0,
            tiled=True,
        ).astype(jnp.float32),
        axis=0,
    )
    output_proj_grad = jnp.sum(
        lax.all_to_all(
            output_part.astype(jnp.bfloat16)
            .reshape(output_part.shape[0], fsdp_size, -1)
            .transpose(1, 0, 2),
            "fsdp",
            split_axis=0,
            concat_axis=0,
            tiled=True,
        ).astype(jnp.float32),
        axis=0,
    )
    device_count = fsdp_size * tp_size
    gain_parts = (attn_gain_part, query_gain_part, key_gain_part, ffn_gain_part)
    gain_table = jnp.concatenate(
        [part.reshape(device_count, -1) for part in gain_parts], axis=1
    )
    gain_width = gain_table.shape[1]
    kv_full = jnp.concatenate([key_head_part, value_head_part], axis=1)
    block_rows = kv_full.shape[0] // fsdp_size
    sub_rows = block_rows // tp_size
    gain_rows = -(-(tp_size * gain_width) // (8 * 2 * HD)) * 8
    gain_block = jnp.pad(
        gain_table.reshape(fsdp_size, tp_size * gain_width),
        ((0, 0), (0, gain_rows * 2 * HD - tp_size * gain_width)),
    ).reshape(fsdp_size, gain_rows, 2 * HD)
    combined = jnp.concatenate(
        [kv_full.reshape(fsdp_size, block_rows, 2 * HD), gain_block], axis=1
    ).reshape(fsdp_size * (block_rows + gain_rows), 2 * HD)
    summed = lax.psum_scatter(combined, "fsdp", scatter_dimension=0, tiled=True)
    summed = jnp.concatenate(
        [
            summed[:block_rows].reshape(-1),
            summed[block_rows:].reshape(-1)[: tp_size * gain_width],
        ]
    )
    kv_local = summed[: block_rows * 2 * HD].reshape(tp_size, sub_rows * 2 * HD)
    gain_local = summed[block_rows * 2 * HD :].reshape(tp_size, gain_width)
    got = lax.all_to_all(
        jnp.concatenate([kv_local, gain_local], axis=1),
        "tp",
        split_axis=0,
        concat_axis=0,
        tiled=True,
    )
    kv_got = got[:, : sub_rows * 2 * HD].reshape(tp_size, sub_rows, 2 * HD)
    kv_got = jnp.sum(kv_got.reshape(HK, tp_size // HK, sub_rows, 2 * HD), axis=1)
    key_proj_grad = kv_got[:, :, :HD].transpose(1, 0, 2).reshape(sub_rows, HK * HD)
    value_proj_grad = kv_got[:, :, HD:].transpose(1, 0, 2).reshape(sub_rows, HK * HD)
    gain_sum = jnp.sum(got[:, sub_rows * 2 * HD :], axis=0)
    gain_grads = []
    offset = 0
    for part in gain_parts:
        size = part.shape[0] // device_count
        gain_grads.append(gain_sum[offset : offset + size])
        offset += size
    attn_gain_grad, query_gain_grad, key_gain_grad, ffn_gain_grad = gain_grads
    return (
        layer_out,
        in_grad,
        query_proj_grad,
        key_proj_grad,
        value_proj_grad,
        output_proj_grad,
        attn_gain_grad,
        query_gain_grad,
        key_gain_grad,
        ffn_gain_grad,
        gate_grad,
        up_grad,
        down_grad,
    )


def solution(mesh):
    in_specs = (
        P(("fsdp", "tp"), None),
        P("fsdp", "tp"),
        P(("fsdp", "tp"), None),
        P(("fsdp", "tp"), None),
        P("tp", "fsdp"),
        P(("fsdp", "tp")),
        P(("fsdp", "tp")),
        P(("fsdp", "tp")),
        P(("fsdp", "tp")),
        P("fsdp", None, "tp"),
        P("fsdp", None, "tp"),
        P("fsdp", "tp", None),
        P("fsdp", None),
        P("fsdp", None),
        P("fsdp"),
        P(("fsdp", "tp"), None),
    )
    out_specs = (
        P(("fsdp", "tp"), None),
        P(("fsdp", "tp"), None),
        P("fsdp", "tp"),
        P(("fsdp", "tp"), None),
        P(("fsdp", "tp"), None),
        P("tp", "fsdp"),
        P(("fsdp", "tp")),
        P(("fsdp", "tp")),
        P(("fsdp", "tp")),
        P(("fsdp", "tp")),
        P("fsdp", None, "tp"),
        P("fsdp", None, "tp"),
        P("fsdp", "tp", None),
    )
    return jax.shard_map(body, mesh=mesh, in_specs=in_specs, out_specs=out_specs, check_vma=False)
```

```python
import math

import jax
import jax.numpy as jnp
from jax import lax
from jax.sharding import PartitionSpec as P

HQ = 32
HK = 4
HD = 128
TOP = 8
SEQ = 1024


EPSILON = 1e-06


def rms_norm(values, weight):
    return values * lax.rsqrt(jnp.mean(values * values, axis=-1, keepdims=True) + EPSILON) * weight


def rotate(values, cosine, sine):
    half_width = values.shape[-1] // 2
    first_half = values[..., :half_width]
    second_half = values[..., half_width:]
    return jnp.concatenate(
        [first_half * cosine - second_half * sine, second_half * cosine + first_half * sine],
        axis=-1,
    )


def rotary_tables(positions, width):
    half_width = width // 2
    inverse = jnp.exp(
        -math.log(1000000.0) * 2.0 * jnp.arange(half_width, dtype=jnp.float32) / width
    )
    angles = positions[:, None] * inverse[None, :]
    return (jnp.cos(angles), jnp.sin(angles))


def masked_scores(queries, keys_b, prefix_end, factor):
    scores = jnp.einsum("qhd,kd->hqk", queries, keys_b, preferred_element_type=jnp.float32) * factor
    position = lax.iota(jnp.int32, queries.shape[0])
    allowed = (position[None, :] <= position[:, None]) | (position[None, :] < prefix_end)
    return jnp.where(allowed[None], scores, -1e30)


def tp_gather(block, count):
    place = lax.axis_index("tp")
    from_left = []
    from_right = []
    going_right = block
    going_left = block
    for step in range(1, count):
        going_right = lax.ppermute(
            going_right, "tp", [(i, i + 1) for i in range(step - 1, count - 1)]
        )
        going_left = lax.ppermute(going_left, "tp", [(i + 1, i) for i in range(0, count - step)])
        from_left.append(going_right)
        from_right.append(going_left)
    stacked = jnp.stack(from_left[::-1] + [block] + from_right, axis=0)
    picked = lax.dynamic_slice_in_dim(stacked, count - 1 - place, count, 0)
    return picked.reshape((count * block.shape[0],) + block.shape[1:])


def tp_scatter_sum(partial, count, send_type):
    place = lax.axis_index("tp")
    rows = partial.shape[0] // count
    pieces = partial.reshape((count, rows) + partial.shape[1:])

    def piece(target):
        return lax.dynamic_index_in_dim(pieces, jnp.clip(target, 0, count - 1), 0, keepdims=False)

    left_sum = None
    right_sum = None
    for step in range(1, count):
        outgoing = piece(place + count - step)
        if left_sum is not None:
            outgoing = outgoing + left_sum.astype(outgoing.dtype)
        left_sum = lax.ppermute(
            outgoing.astype(send_type), "tp", [(i, i + 1) for i in range(step)]
        )
        outgoing = piece(place - count + step)
        if right_sum is not None:
            outgoing = outgoing + right_sum.astype(outgoing.dtype)
        right_sum = lax.ppermute(
            outgoing.astype(send_type), "tp", [(i, i - 1) for i in range(count - step, count)]
        )
    own = piece(place)
    if left_sum is not None:
        own = own + left_sum.astype(own.dtype) + right_sum.astype(own.dtype)
    return own


def body(
    layer_in,
    query_proj,
    key_proj,
    value_proj,
    output_proj,
    attn_gain,
    query_gain,
    key_gain,
    ffn_gain,
    expert_gate,
    expert_up,
    expert_down,
    routes,
    route_weights,
    prefix_len,
    out_grad,
):
    tok_rows = layer_in.shape[0]
    width = layer_in.shape[1]
    group_rows = tok_rows * lax.axis_size("tp")
    seq_count = group_rows // SEQ
    factor = 1.0 / math.sqrt(HD)
    gain_sizes = (attn_gain.shape[0], query_gain.shape[0], key_gain.shape[0], ffn_gain.shape[0])
    kv_rows, kv_width = key_proj.shape
    gain_row = jnp.concatenate([attn_gain, query_gain, key_gain, ffn_gain])
    gain_block = jnp.zeros((8, 2 * kv_width), jnp.bfloat16).at[0, : gain_row.shape[0]].set(gain_row)
    packed = jnp.concatenate(
        [jnp.concatenate([key_proj, value_proj], axis=1), gain_block], axis=0
    )
    packed_all = lax.all_gather(packed, ("fsdp", "tp"), axis=0, tiled=False)
    kv_all = packed_all[:, :kv_rows].reshape(-1, 2 * kv_width)
    key_all = kv_all[:, :kv_width]
    value_all = kv_all[:, kv_width:]
    gain_all = packed_all[:, kv_rows]
    gains = []
    offset = 0
    for size in gain_sizes:
        gains.append(gain_all[:, offset : offset + size].reshape(-1))
        offset += size
    gain_attn, gain_query, gain_key, gain_ffn = gains
    gain_attn = gain_attn.astype(jnp.float32)
    gain_query = gain_query.astype(jnp.float32)
    gain_key = gain_key.astype(jnp.float32)
    gain_ffn = gain_ffn.astype(jnp.float32)
    query_w, out_w, gate_w, up_w, down_w = (
        lax.all_gather(query_proj, "fsdp", axis=0, tiled=True),
        lax.all_gather(output_proj, "fsdp", axis=1, tiled=True),
        lax.all_gather(expert_gate, "fsdp", axis=0, tiled=True),
        lax.all_gather(expert_up, "fsdp", axis=0, tiled=True),
        lax.all_gather(expert_down, "fsdp", axis=0, tiled=True),
    )
    per_dev = query_w.shape[1] // HD
    kv_head = lax.axis_index("tp") * per_dev // (HQ // HK)
    key_w = lax.dynamic_slice_in_dim(key_all, kv_head * HD, HD, 1)
    value_w = lax.dynamic_slice_in_dim(value_all, kv_head * HD, HD, 1)
    tokens_f = layer_in.astype(jnp.float32)
    tp_size = lax.axis_size("tp")
    layer_rows = tp_gather(layer_in, tp_size)
    attn_rows = rms_norm(layer_rows.astype(jnp.float32), gain_attn).astype(jnp.bfloat16)
    out_grad, attn_rows = lax.optimization_barrier((out_grad, attn_rows))
    grad_rows = tp_gather(out_grad, tp_size)
    query_raw = jnp.dot(attn_rows, query_w, preferred_element_type=jnp.float32)
    key_raw = jnp.dot(attn_rows, key_w, preferred_element_type=jnp.float32)
    value_rows = jnp.dot(attn_rows, value_w, preferred_element_type=jnp.float32).astype(
        jnp.bfloat16
    )
    cosine, sine = rotary_tables((lax.iota(jnp.int32, group_rows) % SEQ).astype(jnp.float32), HD)

    def prepare(query_in, key_in, weight_query, weight_key):
        query_heads = rms_norm(query_in.reshape(group_rows, per_dev, HD), weight_query)
        return (
            rotate(query_heads, cosine[:, None, :], sine[:, None, :]),
            rotate(rms_norm(key_in, weight_key), cosine, sine),
        )

    (query_norm, key_norm), prepare_back = jax.vjp(
        prepare, query_raw, key_raw, gain_query, gain_key
    )
    query_seq = query_norm.astype(jnp.bfloat16).reshape(seq_count, SEQ, per_dev, HD)
    key_seq = key_norm.astype(jnp.bfloat16).reshape(seq_count, SEQ, HD)
    value_seq = value_rows.reshape(seq_count, SEQ, HD)

    def attend(operands):
        queries, keys_b, values_b, prefix_end = operands
        scores = masked_scores(queries, keys_b, prefix_end, factor)
        highest = jnp.max(scores, axis=-1, keepdims=True)
        expo = jnp.exp(scores - highest)
        denom = jnp.sum(expo, axis=-1, keepdims=True)
        probs_full = expo / denom
        context = jnp.einsum(
            "hqk,kd->qhd",
            probs_full.astype(jnp.bfloat16),
            values_b,
            preferred_element_type=jnp.float32,
        )
        return (context, probs_full)

    context_all, probs_all = lax.map(attend, (query_seq, key_seq, value_seq, prefix_len))
    context_b = context_all.reshape(group_rows, per_dev * HD).astype(jnp.bfloat16)
    context_b, grad_rows = lax.optimization_barrier((context_b, grad_rows))
    attn_out = tp_scatter_sum(
        jnp.dot(context_b, out_w, preferred_element_type=jnp.float32), tp_size, jnp.bfloat16
    )
    residual = tokens_f + attn_out
    ffn_in = rms_norm(residual, gain_ffn).astype(jnp.bfloat16)
    ffn_rows = tp_gather(ffn_in, tp_size)
    expert_count = gate_w.shape[0]
    chosen = routes[:, :, None] == lax.iota(jnp.int32, expert_count)[None, None, :]
    share = jnp.sum(jnp.where(chosen, route_weights[:, :, None], 0.0), axis=1)
    gate_val = jnp.einsum("td,edf->tef", ffn_rows, gate_w, preferred_element_type=jnp.float32)
    up_val = jnp.einsum("td,edf->tef", ffn_rows, up_w, preferred_element_type=jnp.float32)
    sigma = jax.nn.sigmoid(gate_val)
    active = gate_val * sigma
    hidden = (active * up_val).astype(jnp.bfloat16)
    hidden_share = (hidden.astype(jnp.float32) * share[:, :, None]).astype(jnp.bfloat16)
    mixture = jnp.einsum(
        "tef,efd->td", hidden_share, down_w, preferred_element_type=jnp.float32
    )
    mixture_own = tp_scatter_sum(mixture, tp_size, jnp.bfloat16)
    grad_out = out_grad.astype(jnp.float32)
    hidden_grad = (
        jnp.einsum("td,efd->tef", grad_rows, down_w, preferred_element_type=jnp.float32)
        * share[:, :, None]
    )
    gate_back = (hidden_grad * up_val * sigma * (1.0 + gate_val * (1.0 - sigma))).astype(
        jnp.bfloat16
    )
    up_back = (hidden_grad * active).astype(jnp.bfloat16)
    ffn_in_grad = jnp.einsum(
        "tef,edf->td", gate_back, gate_w, preferred_element_type=jnp.float32
    ) + jnp.einsum("tef,edf->td", up_back, up_w, preferred_element_type=jnp.float32)
    gate_part = jnp.einsum("td,tef->edf", ffn_rows, gate_back, preferred_element_type=jnp.float32)
    up_part = jnp.einsum("td,tef->edf", ffn_rows, up_back, preferred_element_type=jnp.float32)
    down_part = jnp.einsum(
        "tef,td->efd", hidden_share, grad_rows, preferred_element_type=jnp.float32
    )
    ffn_in_own = tp_scatter_sum(ffn_in_grad, tp_size, jnp.bfloat16)
    _, second_back = jax.vjp(rms_norm, residual, gain_ffn)
    residual_norm_grad, ffn_gain_part = second_back(ffn_in_own)
    residual_grad = grad_out + residual_norm_grad
    residual_grad, mixture_own = lax.optimization_barrier((residual_grad, mixture_own))
    gate_grad, up_grad, down_grad = (
        lax.psum_scatter(
            part.astype(jnp.bfloat16), "fsdp", scatter_dimension=0, tiled=True
        ).astype(jnp.float32)
        for part in (gate_part, up_part, down_part)
    )
    layer_out = (residual + mixture_own).astype(jnp.bfloat16)
    attn_out_grad = tp_gather(residual_grad.astype(jnp.bfloat16), tp_size)
    output_part = jnp.einsum(
        "gq,gd->qd", context_b, attn_out_grad, preferred_element_type=jnp.float32
    )
    context_grad = (
        jnp.einsum("gd,qd->gq", attn_out_grad, out_w, preferred_element_type=jnp.float32)
        .astype(jnp.bfloat16)
        .reshape(seq_count, SEQ, per_dev, HD)
    )

    def attend_back(operands):
        queries, keys_b, values_b, attn_probs, ctx_grad = operands
        value_grad = jnp.einsum(
            "hqk,qhd->kd",
            attn_probs.astype(jnp.bfloat16),
            ctx_grad,
            preferred_element_type=jnp.float32,
        )
        probs_grad = jnp.einsum(
            "qhd,kd->hqk", ctx_grad, values_b, preferred_element_type=jnp.float32
        )
        scores_grad = (
            attn_probs * (probs_grad - jnp.sum(attn_probs * probs_grad, axis=-1, keepdims=True))
        ).astype(jnp.bfloat16)
        query_grad = (
            jnp.einsum("hqk,kd->qhd", scores_grad, keys_b, preferred_element_type=jnp.float32)
            * factor
        )
        key_grad = (
            jnp.einsum("hqk,qhd->kd", scores_grad, queries, preferred_element_type=jnp.float32)
            * factor
        )
        return (query_grad, key_grad, value_grad)

    query_norm_grad, key_norm_grad, value_grad = lax.map(
        attend_back, (query_seq, key_seq, value_seq, probs_all, context_grad)
    )
    query_raw_grad, key_raw_grad, query_gain_part, key_gain_part = prepare_back(
        (query_norm_grad.reshape(group_rows, per_dev, HD), key_norm_grad.reshape(group_rows, HD))
    )
    query_back = query_raw_grad.astype(jnp.bfloat16)
    key_back = key_raw_grad.astype(jnp.bfloat16)
    value_back = value_grad.reshape(group_rows, HD).astype(jnp.bfloat16)
    result = jnp.einsum("gq,dq->gd", query_back, query_w, preferred_element_type=jnp.float32)
    result = result + jnp.einsum("gk,dk->gd", key_back, key_w, preferred_element_type=jnp.float32)
    attn_in_part = result + jnp.einsum(
        "gk,dk->gd", value_back, value_w, preferred_element_type=jnp.float32
    )
    attn_in_part, down_grad, gate_grad, up_grad = lax.optimization_barrier(
        (attn_in_part, down_grad, gate_grad, up_grad)
    )
    attn_in_grad = tp_scatter_sum(attn_in_part, tp_size, jnp.bfloat16)
    query_part = jnp.einsum("gd,gq->dq", attn_rows, query_back, preferred_element_type=jnp.float32)
    key_head_part = jnp.einsum("gd,gk->dk", attn_rows, key_back, preferred_element_type=jnp.float32)
    value_head_part = jnp.einsum(
        "gd,gk->dk", attn_rows, value_back, preferred_element_type=jnp.float32
    )
    _, first_back = jax.vjp(rms_norm, tokens_f, gain_attn)
    input_norm_grad, _ = first_back(attn_in_grad)
    _, rows_back = jax.vjp(
        lambda weight: rms_norm(layer_rows.astype(jnp.float32), weight), gain_attn
    )
    (attn_gain_part,) = rows_back(attn_in_part)
    in_grad = residual_grad + input_norm_grad
    fsdp_size = lax.axis_size("fsdp")
    query_proj_grad = jnp.sum(
        lax.all_to_all(
            query_part.astype(jnp.bfloat16).reshape(fsdp_size, -1, query_part.shape[1]),
            "fsdp",
            split_axis=0,
            concat_axis=0,
            tiled=True,
        ).astype(jnp.float32),
        axis=0,
    )
    output_proj_grad = jnp.sum(
        lax.all_to_all(
            output_part.astype(jnp.bfloat16)
            .reshape(output_part.shape[0], fsdp_size, -1)
            .transpose(1, 0, 2),
            "fsdp",
            split_axis=0,
            concat_axis=0,
            tiled=True,
        ).astype(jnp.float32),
        axis=0,
    )
    device_count = fsdp_size * tp_size
    gain_parts = (attn_gain_part, query_gain_part, key_gain_part, ffn_gain_part)
    gain_table = jnp.concatenate(
        [part.reshape(device_count, -1) for part in gain_parts], axis=1
    )
    gain_width = gain_table.shape[1]
    kv_full = jnp.concatenate([key_head_part, value_head_part], axis=1)
    block_rows = kv_full.shape[0] // fsdp_size
    sub_rows = block_rows // tp_size
    gain_rows = -(-(tp_size * gain_width) // (8 * 2 * HD)) * 8
    gain_block = jnp.pad(
        gain_table.reshape(fsdp_size, tp_size * gain_width),
        ((0, 0), (0, gain_rows * 2 * HD - tp_size * gain_width)),
    ).reshape(fsdp_size, gain_rows, 2 * HD)
    combined = jnp.concatenate(
        [kv_full.reshape(fsdp_size, block_rows, 2 * HD), gain_block], axis=1
    ).reshape(fsdp_size * (block_rows + gain_rows), 2 * HD)
    summed = lax.psum_scatter(combined, "fsdp", scatter_dimension=0, tiled=True)
    summed = jnp.concatenate(
        [
            summed[:block_rows].reshape(-1),
            summed[block_rows:].reshape(-1)[: tp_size * gain_width],
        ]
    )
    kv_local = summed[: block_rows * 2 * HD].reshape(tp_size, sub_rows * 2 * HD)
    gain_local = summed[block_rows * 2 * HD :].reshape(tp_size, gain_width)
    got = lax.all_to_all(
        jnp.concatenate([kv_local, gain_local], axis=1),
        "tp",
        split_axis=0,
        concat_axis=0,
        tiled=True,
    )
    kv_got = got[:, : sub_rows * 2 * HD].reshape(tp_size, sub_rows, 2 * HD)
    kv_got = jnp.sum(kv_got.reshape(HK, tp_size // HK, sub_rows, 2 * HD), axis=1)
    key_proj_grad = kv_got[:, :, :HD].transpose(1, 0, 2).reshape(sub_rows, HK * HD)
    value_proj_grad = kv_got[:, :, HD:].transpose(1, 0, 2).reshape(sub_rows, HK * HD)
    gain_sum = jnp.sum(got[:, sub_rows * 2 * HD :], axis=0)
    gain_grads = []
    offset = 0
    for part in gain_parts:
        size = part.shape[0] // device_count
        gain_grads.append(gain_sum[offset : offset + size])
        offset += size
    attn_gain_grad, query_gain_grad, key_gain_grad, ffn_gain_grad = gain_grads
    return (
        layer_out,
        in_grad,
        query_proj_grad,
        key_proj_grad,
        value_proj_grad,
        output_proj_grad,
        attn_gain_grad,
        query_gain_grad,
        key_gain_grad,
        ffn_gain_grad,
        gate_grad,
        up_grad,
        down_grad,
    )


def solution(mesh):
    in_specs = (
        P(("fsdp", "tp"), None),
        P("fsdp", "tp"),
        P(("fsdp", "tp"), None),
        P(("fsdp", "tp"), None),
        P("tp", "fsdp"),
        P(("fsdp", "tp")),
        P(("fsdp", "tp")),
        P(("fsdp", "tp")),
        P(("fsdp", "tp")),
        P("fsdp", None, "tp"),
        P("fsdp", None, "tp"),
        P("fsdp", "tp", None),
        P("fsdp", None),
        P("fsdp", None),
        P("fsdp"),
        P(("fsdp", "tp"), None),
    )
    out_specs = (
        P(("fsdp", "tp"), None),
        P(("fsdp", "tp"), None),
        P("fsdp", "tp"),
        P(("fsdp", "tp"), None),
        P(("fsdp", "tp"), None),
        P("tp", "fsdp"),
        P(("fsdp", "tp")),
        P(("fsdp", "tp")),
        P(("fsdp", "tp")),
        P(("fsdp", "tp")),
        P("fsdp", None, "tp"),
        P("fsdp", None, "tp"),
        P("fsdp", "tp", None),
    )
    return jax.shard_map(body, mesh=mesh, in_specs=in_specs, out_specs=out_specs, check_vma=False)
```

```python
import math

import jax
import jax.numpy as jnp
from jax import lax
from jax.sharding import PartitionSpec as P

HQ = 32
HK = 4
HD = 128
TOP = 8
SEQ = 1024


EPSILON = 1e-06


def rms_norm(values, weight):
    return values * lax.rsqrt(jnp.mean(values * values, axis=-1, keepdims=True) + EPSILON) * weight


def rotate(values, cosine, sine):
    half_width = values.shape[-1] // 2
    first_half = values[..., :half_width]
    second_half = values[..., half_width:]
    return jnp.concatenate(
        [first_half * cosine - second_half * sine, second_half * cosine + first_half * sine],
        axis=-1,
    )


def rotary_tables(positions, width):
    half_width = width // 2
    inverse = jnp.exp(
        -math.log(1000000.0) * 2.0 * jnp.arange(half_width, dtype=jnp.float32) / width
    )
    angles = positions[:, None] * inverse[None, :]
    return (jnp.cos(angles), jnp.sin(angles))


def masked_scores(queries, keys_b, prefix_end, factor):
    scores = jnp.einsum("qhd,kd->hqk", queries, keys_b, preferred_element_type=jnp.float32) * factor
    position = lax.iota(jnp.int32, queries.shape[0])
    allowed = (position[None, :] <= position[:, None]) | (position[None, :] < prefix_end)
    return jnp.where(allowed[None], scores, -1e30)


def tp_gather(block, count):
    place = lax.axis_index("tp")
    from_left = []
    from_right = []
    going_right = block
    going_left = block
    for step in range(1, count):
        going_right = lax.ppermute(
            going_right, "tp", [(i, i + 1) for i in range(step - 1, count - 1)]
        )
        going_left = lax.ppermute(going_left, "tp", [(i + 1, i) for i in range(0, count - step)])
        from_left.append(going_right)
        from_right.append(going_left)
    stacked = jnp.stack(from_left[::-1] + [block] + from_right, axis=0)
    picked = lax.dynamic_slice_in_dim(stacked, count - 1 - place, count, 0)
    return picked.reshape((count * block.shape[0],) + block.shape[1:])


def tp_scatter_sum(partial, count, send_type):
    place = lax.axis_index("tp")
    rows = partial.shape[0] // count
    pieces = partial.reshape((count, rows) + partial.shape[1:])

    def piece(target):
        return lax.dynamic_index_in_dim(pieces, jnp.clip(target, 0, count - 1), 0, keepdims=False)

    left_sum = None
    right_sum = None
    for step in range(1, count):
        outgoing = piece(place + count - step)
        if left_sum is not None:
            outgoing = outgoing + left_sum.astype(outgoing.dtype)
        left_sum = lax.ppermute(
            outgoing.astype(send_type), "tp", [(i, i + 1) for i in range(step)]
        )
        outgoing = piece(place - count + step)
        if right_sum is not None:
            outgoing = outgoing + right_sum.astype(outgoing.dtype)
        right_sum = lax.ppermute(
            outgoing.astype(send_type), "tp", [(i, i - 1) for i in range(count - step, count)]
        )
    own = piece(place)
    if left_sum is not None:
        own = own + left_sum.astype(own.dtype) + right_sum.astype(own.dtype)
    return own


def body(
    layer_in,
    query_proj,
    key_proj,
    value_proj,
    output_proj,
    attn_gain,
    query_gain,
    key_gain,
    ffn_gain,
    expert_gate,
    expert_up,
    expert_down,
    routes,
    route_weights,
    prefix_len,
    out_grad,
):
    tok_rows = layer_in.shape[0]
    width = layer_in.shape[1]
    group_rows = tok_rows * lax.axis_size("tp")
    seq_count = group_rows // SEQ
    factor = 1.0 / math.sqrt(HD)
    gain_sizes = (attn_gain.shape[0], query_gain.shape[0], key_gain.shape[0], ffn_gain.shape[0])
    kv_rows, kv_width = key_proj.shape
    gain_row = jnp.concatenate([attn_gain, query_gain, key_gain, ffn_gain])
    gain_block = jnp.zeros((8, 2 * kv_width), jnp.bfloat16).at[0, : gain_row.shape[0]].set(gain_row)
    packed = jnp.concatenate(
        [jnp.concatenate([key_proj, value_proj], axis=1), gain_block], axis=0
    )
    packed_all = lax.all_gather(packed, ("fsdp", "tp"), axis=0, tiled=False)
    kv_all = packed_all[:, :kv_rows].reshape(-1, 2 * kv_width)
    key_all = kv_all[:, :kv_width]
    value_all = kv_all[:, kv_width:]
    gain_all = packed_all[:, kv_rows]
    gains = []
    offset = 0
    for size in gain_sizes:
        gains.append(gain_all[:, offset : offset + size].reshape(-1))
        offset += size
    gain_attn, gain_query, gain_key, gain_ffn = gains
    gain_attn = gain_attn.astype(jnp.float32)
    gain_query = gain_query.astype(jnp.float32)
    gain_key = gain_key.astype(jnp.float32)
    gain_ffn = gain_ffn.astype(jnp.float32)
    query_w, out_w, gate_w, up_w, down_w = (
        lax.all_gather(query_proj, "fsdp", axis=0, tiled=True),
        lax.all_gather(output_proj, "fsdp", axis=1, tiled=True),
        lax.all_gather(expert_gate, "fsdp", axis=0, tiled=True),
        lax.all_gather(expert_up, "fsdp", axis=0, tiled=True),
        lax.all_gather(expert_down, "fsdp", axis=0, tiled=True),
    )
    per_dev = query_w.shape[1] // HD
    kv_head = lax.axis_index("tp") * per_dev // (HQ // HK)
    key_w = lax.dynamic_slice_in_dim(key_all, kv_head * HD, HD, 1)
    value_w = lax.dynamic_slice_in_dim(value_all, kv_head * HD, HD, 1)
    tokens_f = layer_in.astype(jnp.float32)
    tp_size = lax.axis_size("tp")
    layer_rows = tp_gather(layer_in, tp_size)
    attn_rows = rms_norm(layer_rows.astype(jnp.float32), gain_attn).astype(jnp.bfloat16)
    out_grad, attn_rows = lax.optimization_barrier((out_grad, attn_rows))
    grad_rows = tp_gather(out_grad, tp_size)
    query_raw = jnp.dot(attn_rows, query_w, preferred_element_type=jnp.float32)
    key_raw = jnp.dot(attn_rows, key_w, preferred_element_type=jnp.float32)
    value_rows = jnp.dot(attn_rows, value_w, preferred_element_type=jnp.float32).astype(
        jnp.bfloat16
    )
    cosine, sine = rotary_tables((lax.iota(jnp.int32, group_rows) % SEQ).astype(jnp.float32), HD)

    def prepare(query_in, key_in, weight_query, weight_key):
        query_heads = rms_norm(query_in.reshape(group_rows, per_dev, HD), weight_query)
        return (
            rotate(query_heads, cosine[:, None, :], sine[:, None, :]),
            rotate(rms_norm(key_in, weight_key), cosine, sine),
        )

    (query_norm, key_norm), prepare_back = jax.vjp(
        prepare, query_raw, key_raw, gain_query, gain_key
    )
    query_seq = query_norm.astype(jnp.bfloat16).reshape(seq_count, SEQ, per_dev, HD)
    key_seq = key_norm.astype(jnp.bfloat16).reshape(seq_count, SEQ, HD)
    value_seq = value_rows.reshape(seq_count, SEQ, HD)

    def attend(operands):
        queries, keys_b, values_b, prefix_end = operands
        scores = masked_scores(queries, keys_b, prefix_end, factor)
        highest = jnp.max(scores, axis=-1, keepdims=True)
        expo = jnp.exp(scores - highest)
        denom = jnp.sum(expo, axis=-1, keepdims=True)
        probs_full = expo / denom
        context = jnp.einsum(
            "hqk,kd->qhd",
            probs_full.astype(jnp.bfloat16),
            values_b,
            preferred_element_type=jnp.float32,
        )
        return (context, probs_full)

    forward_parts = [
        attend((query_seq[index], key_seq[index], value_seq[index], prefix_len[index]))
        for index in range(seq_count)
    ]
    context_all = jnp.stack([part[0] for part in forward_parts])
    probs_all = [part[1] for part in forward_parts]
    context_b = context_all.reshape(group_rows, per_dev * HD).astype(jnp.bfloat16)
    context_b, grad_rows = lax.optimization_barrier((context_b, grad_rows))
    attn_out = tp_scatter_sum(
        jnp.dot(context_b, out_w, preferred_element_type=jnp.float32), tp_size, jnp.bfloat16
    )
    residual = tokens_f + attn_out
    ffn_in = rms_norm(residual, gain_ffn).astype(jnp.bfloat16)
    ffn_rows = tp_gather(ffn_in, tp_size)
    expert_count = gate_w.shape[0]
    chosen = routes[:, :, None] == lax.iota(jnp.int32, expert_count)[None, None, :]
    share = jnp.sum(jnp.where(chosen, route_weights[:, :, None], 0.0), axis=1)
    gate_val = jnp.einsum("td,edf->tef", ffn_rows, gate_w, preferred_element_type=jnp.float32)
    up_val = jnp.einsum("td,edf->tef", ffn_rows, up_w, preferred_element_type=jnp.float32)
    sigma = jax.nn.sigmoid(gate_val)
    active = gate_val * sigma
    hidden = (active * up_val).astype(jnp.bfloat16)
    hidden_share = (hidden.astype(jnp.float32) * share[:, :, None]).astype(jnp.bfloat16)
    mixture = jnp.einsum(
        "tef,efd->td", hidden_share, down_w, preferred_element_type=jnp.float32
    )
    mixture_own = tp_scatter_sum(mixture, tp_size, jnp.bfloat16)
    grad_out = out_grad.astype(jnp.float32)
    hidden_grad = (
        jnp.einsum("td,efd->tef", grad_rows, down_w, preferred_element_type=jnp.float32)
        * share[:, :, None]
    )
    gate_back = (hidden_grad * up_val * sigma * (1.0 + gate_val * (1.0 - sigma))).astype(
        jnp.bfloat16
    )
    up_back = (hidden_grad * active).astype(jnp.bfloat16)
    ffn_in_grad = jnp.einsum(
        "tef,edf->td", gate_back, gate_w, preferred_element_type=jnp.float32
    ) + jnp.einsum("tef,edf->td", up_back, up_w, preferred_element_type=jnp.float32)
    gate_part = jnp.einsum("td,tef->edf", ffn_rows, gate_back, preferred_element_type=jnp.float32)
    up_part = jnp.einsum("td,tef->edf", ffn_rows, up_back, preferred_element_type=jnp.float32)
    down_part = jnp.einsum(
        "tef,td->efd", hidden_share, grad_rows, preferred_element_type=jnp.float32
    )
    ffn_in_own = tp_scatter_sum(ffn_in_grad, tp_size, jnp.bfloat16)
    _, second_back = jax.vjp(rms_norm, residual, gain_ffn)
    residual_norm_grad, ffn_gain_part = second_back(ffn_in_own)
    residual_grad = grad_out + residual_norm_grad
    residual_grad, mixture_own = lax.optimization_barrier((residual_grad, mixture_own))
    gate_grad, up_grad, down_grad = (
        lax.psum_scatter(
            part.astype(jnp.bfloat16), "fsdp", scatter_dimension=0, tiled=True
        ).astype(jnp.float32)
        for part in (gate_part, up_part, down_part)
    )
    layer_out = (residual + mixture_own).astype(jnp.bfloat16)
    attn_out_grad = tp_gather(residual_grad.astype(jnp.bfloat16), tp_size)
    output_part = jnp.einsum(
        "gq,gd->qd", context_b, attn_out_grad, preferred_element_type=jnp.float32
    )
    context_grad = (
        jnp.einsum("gd,qd->gq", attn_out_grad, out_w, preferred_element_type=jnp.float32)
        .astype(jnp.bfloat16)
        .reshape(seq_count, SEQ, per_dev, HD)
    )

    def attend_back(operands):
        queries, keys_b, values_b, attn_probs, ctx_grad = operands
        value_grad = jnp.einsum(
            "hqk,qhd->kd",
            attn_probs.astype(jnp.bfloat16),
            ctx_grad,
            preferred_element_type=jnp.float32,
        )
        probs_grad = jnp.einsum(
            "qhd,kd->hqk", ctx_grad, values_b, preferred_element_type=jnp.float32
        )
        scores_grad = (
            attn_probs * (probs_grad - jnp.sum(attn_probs * probs_grad, axis=-1, keepdims=True))
        ).astype(jnp.bfloat16)
        query_grad = (
            jnp.einsum("hqk,kd->qhd", scores_grad, keys_b, preferred_element_type=jnp.float32)
            * factor
        )
        key_grad = (
            jnp.einsum("hqk,qhd->kd", scores_grad, queries, preferred_element_type=jnp.float32)
            * factor
        )
        return (query_grad, key_grad, value_grad)

    backward_parts = [
        attend_back(
            (
                query_seq[index],
                key_seq[index],
                value_seq[index],
                probs_all[index],
                context_grad[index],
            )
        )
        for index in range(seq_count)
    ]
    query_norm_grad, key_norm_grad, value_grad = (
        jnp.stack([part[slot] for part in backward_parts]) for slot in range(3)
    )
    query_raw_grad, key_raw_grad, query_gain_part, key_gain_part = prepare_back(
        (query_norm_grad.reshape(group_rows, per_dev, HD), key_norm_grad.reshape(group_rows, HD))
    )
    query_back = query_raw_grad.astype(jnp.bfloat16)
    key_back = key_raw_grad.astype(jnp.bfloat16)
    value_back = value_grad.reshape(group_rows, HD).astype(jnp.bfloat16)
    result = jnp.einsum("gq,dq->gd", query_back, query_w, preferred_element_type=jnp.float32)
    result = result + jnp.einsum("gk,dk->gd", key_back, key_w, preferred_element_type=jnp.float32)
    attn_in_part = result + jnp.einsum(
        "gk,dk->gd", value_back, value_w, preferred_element_type=jnp.float32
    )
    attn_in_part, down_grad, gate_grad, up_grad = lax.optimization_barrier(
        (attn_in_part, down_grad, gate_grad, up_grad)
    )
    attn_in_grad = tp_scatter_sum(attn_in_part, tp_size, jnp.bfloat16)
    query_part = jnp.einsum("gd,gq->dq", attn_rows, query_back, preferred_element_type=jnp.float32)
    key_head_part = jnp.einsum("gd,gk->dk", attn_rows, key_back, preferred_element_type=jnp.float32)
    value_head_part = jnp.einsum(
        "gd,gk->dk", attn_rows, value_back, preferred_element_type=jnp.float32
    )
    _, first_back = jax.vjp(rms_norm, tokens_f, gain_attn)
    input_norm_grad, _ = first_back(attn_in_grad)
    _, rows_back = jax.vjp(
        lambda weight: rms_norm(layer_rows.astype(jnp.float32), weight), gain_attn
    )
    (attn_gain_part,) = rows_back(attn_in_part)
    in_grad = residual_grad + input_norm_grad
    fsdp_size = lax.axis_size("fsdp")
    query_proj_grad = jnp.sum(
        lax.all_to_all(
            query_part.astype(jnp.bfloat16).reshape(fsdp_size, -1, query_part.shape[1]),
            "fsdp",
            split_axis=0,
            concat_axis=0,
            tiled=True,
        ).astype(jnp.float32),
        axis=0,
    )
    output_proj_grad = jnp.sum(
        lax.all_to_all(
            output_part.astype(jnp.bfloat16)
            .reshape(output_part.shape[0], fsdp_size, -1)
            .transpose(1, 0, 2),
            "fsdp",
            split_axis=0,
            concat_axis=0,
            tiled=True,
        ).astype(jnp.float32),
        axis=0,
    )
    device_count = fsdp_size * tp_size
    gain_parts = (attn_gain_part, query_gain_part, key_gain_part, ffn_gain_part)
    gain_table = jnp.concatenate(
        [part.reshape(device_count, -1) for part in gain_parts], axis=1
    )
    gain_width = gain_table.shape[1]
    kv_full = jnp.concatenate([key_head_part, value_head_part], axis=1)
    block_rows = kv_full.shape[0] // fsdp_size
    sub_rows = block_rows // tp_size
    gain_rows = -(-(tp_size * gain_width) // (8 * 2 * HD)) * 8
    gain_block = jnp.pad(
        gain_table.reshape(fsdp_size, tp_size * gain_width),
        ((0, 0), (0, gain_rows * 2 * HD - tp_size * gain_width)),
    ).reshape(fsdp_size, gain_rows, 2 * HD)
    combined = jnp.concatenate(
        [kv_full.reshape(fsdp_size, block_rows, 2 * HD), gain_block], axis=1
    ).reshape(fsdp_size * (block_rows + gain_rows), 2 * HD)
    summed = lax.psum_scatter(combined, "fsdp", scatter_dimension=0, tiled=True)
    summed = jnp.concatenate(
        [
            summed[:block_rows].reshape(-1),
            summed[block_rows:].reshape(-1)[: tp_size * gain_width],
        ]
    )
    kv_local = summed[: block_rows * 2 * HD].reshape(tp_size, sub_rows * 2 * HD)
    gain_local = summed[block_rows * 2 * HD :].reshape(tp_size, gain_width)
    got = lax.all_to_all(
        jnp.concatenate([kv_local, gain_local], axis=1),
        "tp",
        split_axis=0,
        concat_axis=0,
        tiled=True,
    )
    kv_got = got[:, : sub_rows * 2 * HD].reshape(tp_size, sub_rows, 2 * HD)
    kv_got = jnp.sum(kv_got.reshape(HK, tp_size // HK, sub_rows, 2 * HD), axis=1)
    key_proj_grad = kv_got[:, :, :HD].transpose(1, 0, 2).reshape(sub_rows, HK * HD)
    value_proj_grad = kv_got[:, :, HD:].transpose(1, 0, 2).reshape(sub_rows, HK * HD)
    gain_sum = jnp.sum(got[:, sub_rows * 2 * HD :], axis=0)
    gain_grads = []
    offset = 0
    for part in gain_parts:
        size = part.shape[0] // device_count
        gain_grads.append(gain_sum[offset : offset + size])
        offset += size
    attn_gain_grad, query_gain_grad, key_gain_grad, ffn_gain_grad = gain_grads
    return (
        layer_out,
        in_grad,
        query_proj_grad,
        key_proj_grad,
        value_proj_grad,
        output_proj_grad,
        attn_gain_grad,
        query_gain_grad,
        key_gain_grad,
        ffn_gain_grad,
        gate_grad,
        up_grad,
        down_grad,
    )


def solution(mesh):
    in_specs = (
        P(("fsdp", "tp"), None),
        P("fsdp", "tp"),
        P(("fsdp", "tp"), None),
        P(("fsdp", "tp"), None),
        P("tp", "fsdp"),
        P(("fsdp", "tp")),
        P(("fsdp", "tp")),
        P(("fsdp", "tp")),
        P(("fsdp", "tp")),
        P("fsdp", None, "tp"),
        P("fsdp", None, "tp"),
        P("fsdp", "tp", None),
        P("fsdp", None),
        P("fsdp", None),
        P("fsdp"),
        P(("fsdp", "tp"), None),
    )
    out_specs = (
        P(("fsdp", "tp"), None),
        P(("fsdp", "tp"), None),
        P("fsdp", "tp"),
        P(("fsdp", "tp"), None),
        P(("fsdp", "tp"), None),
        P("tp", "fsdp"),
        P(("fsdp", "tp")),
        P(("fsdp", "tp")),
        P(("fsdp", "tp")),
        P(("fsdp", "tp")),
        P("fsdp", None, "tp"),
        P("fsdp", None, "tp"),
        P("fsdp", "tp", None),
    )
    return jax.shard_map(body, mesh=mesh, in_specs=in_specs, out_specs=out_specs, check_vma=False)
```

```python
import math

import jax
import jax.numpy as jnp
from jax import lax
from jax.sharding import PartitionSpec as P

HQ = 32
HK = 4
HD = 128
TOP = 8
SEQ = 1024


EPSILON = 1e-06


def rms_norm(values, weight):
    return values * lax.rsqrt(jnp.mean(values * values, axis=-1, keepdims=True) + EPSILON) * weight


def rotate(values, cosine, sine):
    half_width = values.shape[-1] // 2
    first_half = values[..., :half_width]
    second_half = values[..., half_width:]
    return jnp.concatenate(
        [first_half * cosine - second_half * sine, second_half * cosine + first_half * sine],
        axis=-1,
    )


def rotary_tables(positions, width):
    half_width = width // 2
    inverse = jnp.exp(
        -math.log(1000000.0) * 2.0 * jnp.arange(half_width, dtype=jnp.float32) / width
    )
    angles = positions[:, None] * inverse[None, :]
    return (jnp.cos(angles), jnp.sin(angles))


def masked_scores(queries, keys_b, prefix_end, factor):
    scores = jnp.einsum("qhd,kd->hqk", queries, keys_b, preferred_element_type=jnp.float32) * factor
    position = lax.iota(jnp.int32, queries.shape[0])
    allowed = (position[None, :] <= position[:, None]) | (position[None, :] < prefix_end)
    return jnp.where(allowed[None], scores, -1e30)


def tp_gather(block, count):
    place = lax.axis_index("tp")
    from_left = []
    from_right = []
    going_right = block
    going_left = block
    for step in range(1, count):
        going_right = lax.ppermute(
            going_right, "tp", [(i, i + 1) for i in range(step - 1, count - 1)]
        )
        going_left = lax.ppermute(going_left, "tp", [(i + 1, i) for i in range(0, count - step)])
        from_left.append(going_right)
        from_right.append(going_left)
    stacked = jnp.stack(from_left[::-1] + [block] + from_right, axis=0)
    picked = lax.dynamic_slice_in_dim(stacked, count - 1 - place, count, 0)
    return picked.reshape((count * block.shape[0],) + block.shape[1:])


def tp_scatter_sum(partial, count, send_type):
    place = lax.axis_index("tp")
    rows = partial.shape[0] // count
    pieces = partial.reshape((count, rows) + partial.shape[1:])

    def piece(target):
        return lax.dynamic_index_in_dim(pieces, jnp.clip(target, 0, count - 1), 0, keepdims=False)

    left_sum = None
    right_sum = None
    for step in range(1, count):
        outgoing = piece(place + count - step)
        if left_sum is not None:
            outgoing = outgoing + left_sum.astype(outgoing.dtype)
        left_sum = lax.ppermute(
            outgoing.astype(send_type), "tp", [(i, i + 1) for i in range(step)]
        )
        outgoing = piece(place - count + step)
        if right_sum is not None:
            outgoing = outgoing + right_sum.astype(outgoing.dtype)
        right_sum = lax.ppermute(
            outgoing.astype(send_type), "tp", [(i, i - 1) for i in range(count - step, count)]
        )
    own = piece(place)
    if left_sum is not None:
        own = own + left_sum.astype(own.dtype) + right_sum.astype(own.dtype)
    return own


def body(
    layer_in,
    query_proj,
    key_proj,
    value_proj,
    output_proj,
    attn_gain,
    query_gain,
    key_gain,
    ffn_gain,
    expert_gate,
    expert_up,
    expert_down,
    routes,
    route_weights,
    prefix_len,
    out_grad,
):
    tok_rows = layer_in.shape[0]
    width = layer_in.shape[1]
    group_rows = tok_rows * lax.axis_size("tp")
    seq_count = group_rows // SEQ
    factor = 1.0 / math.sqrt(HD)
    gain_sizes = (attn_gain.shape[0], query_gain.shape[0], key_gain.shape[0], ffn_gain.shape[0])
    kv_rows, kv_width = key_proj.shape
    gain_row = jnp.concatenate([attn_gain, query_gain, key_gain, ffn_gain])
    gain_block = jnp.zeros((8, 2 * kv_width), jnp.bfloat16).at[0, : gain_row.shape[0]].set(gain_row)
    packed = jnp.concatenate(
        [jnp.concatenate([key_proj, value_proj], axis=1), gain_block], axis=0
    )
    packed_all = lax.all_gather(packed, ("fsdp", "tp"), axis=0, tiled=False)
    kv_all = packed_all[:, :kv_rows].reshape(-1, 2 * kv_width)
    key_all = kv_all[:, :kv_width]
    value_all = kv_all[:, kv_width:]
    gain_all = packed_all[:, kv_rows]
    gains = []
    offset = 0
    for size in gain_sizes:
        gains.append(gain_all[:, offset : offset + size].reshape(-1))
        offset += size
    gain_attn, gain_query, gain_key, gain_ffn = gains
    gain_attn = gain_attn.astype(jnp.float32)
    gain_query = gain_query.astype(jnp.float32)
    gain_key = gain_key.astype(jnp.float32)
    gain_ffn = gain_ffn.astype(jnp.float32)
    query_w, out_w, gate_w, up_w, down_w = (
        lax.all_gather(query_proj, "fsdp", axis=0, tiled=True),
        lax.all_gather(output_proj, "fsdp", axis=1, tiled=True),
        lax.all_gather(expert_gate, "fsdp", axis=0, tiled=True),
        lax.all_gather(expert_up, "fsdp", axis=0, tiled=True),
        lax.all_gather(expert_down, "fsdp", axis=0, tiled=True),
    )
    per_dev = query_w.shape[1] // HD
    kv_head = lax.axis_index("tp") * per_dev // (HQ // HK)
    key_w = lax.dynamic_slice_in_dim(key_all, kv_head * HD, HD, 1)
    value_w = lax.dynamic_slice_in_dim(value_all, kv_head * HD, HD, 1)
    tokens_f = layer_in.astype(jnp.float32)
    tp_size = lax.axis_size("tp")
    layer_rows = tp_gather(layer_in, tp_size)
    attn_rows = rms_norm(layer_rows.astype(jnp.float32), gain_attn).astype(jnp.bfloat16)
    out_grad, attn_rows = lax.optimization_barrier((out_grad, attn_rows))
    grad_rows = tp_gather(out_grad, tp_size)
    query_raw = jnp.dot(attn_rows, query_w, preferred_element_type=jnp.float32)
    key_raw = jnp.dot(attn_rows, key_w, preferred_element_type=jnp.float32)
    value_rows = jnp.dot(attn_rows, value_w, preferred_element_type=jnp.float32).astype(
        jnp.bfloat16
    )
    cosine, sine = rotary_tables((lax.iota(jnp.int32, group_rows) % SEQ).astype(jnp.float32), HD)

    def prepare(query_in, key_in, weight_query, weight_key):
        query_heads = rms_norm(query_in.reshape(group_rows, per_dev, HD), weight_query)
        return (
            rotate(query_heads, cosine[:, None, :], sine[:, None, :]),
            rotate(rms_norm(key_in, weight_key), cosine, sine),
        )

    (query_norm, key_norm), prepare_back = jax.vjp(
        prepare, query_raw, key_raw, gain_query, gain_key
    )
    query_seq = query_norm.astype(jnp.bfloat16).reshape(seq_count, SEQ, per_dev, HD)
    key_seq = key_norm.astype(jnp.bfloat16).reshape(seq_count, SEQ, HD)
    value_seq = value_rows.reshape(seq_count, SEQ, HD)

    def attend(operands):
        queries, keys_b, values_b, prefix_end = operands
        scores = masked_scores(queries, keys_b, prefix_end, factor)
        highest = jnp.max(scores, axis=-1, keepdims=True)
        expo = jnp.exp(scores - highest)
        denom = jnp.sum(expo, axis=-1, keepdims=True)
        probs_full = expo / denom
        context = jnp.einsum(
            "hqk,kd->qhd",
            probs_full.astype(jnp.bfloat16),
            values_b,
            preferred_element_type=jnp.float32,
        )
        return (context, probs_full)

    context_all, probs_all = lax.map(attend, (query_seq, key_seq, value_seq, prefix_len))
    context_b = context_all.reshape(group_rows, per_dev * HD).astype(jnp.bfloat16)
    context_b, grad_rows = lax.optimization_barrier((context_b, grad_rows))
    attn_out = tp_scatter_sum(
        jnp.dot(context_b, out_w, preferred_element_type=jnp.float32), tp_size, jnp.bfloat16
    )
    residual = tokens_f + attn_out
    ffn_in = rms_norm(residual, gain_ffn).astype(jnp.bfloat16)
    ffn_rows = tp_gather(ffn_in, tp_size)
    expert_count = gate_w.shape[0]
    chosen = routes[:, :, None] == lax.iota(jnp.int32, expert_count)[None, None, :]
    share = jnp.sum(jnp.where(chosen, route_weights[:, :, None], 0.0), axis=1)
    gate_val = jnp.einsum("td,edf->tef", ffn_rows, gate_w, preferred_element_type=jnp.float32)
    up_val = jnp.einsum("td,edf->tef", ffn_rows, up_w, preferred_element_type=jnp.float32)
    sigma = jax.nn.sigmoid(gate_val)
    active = gate_val * sigma
    hidden = (active * up_val).astype(jnp.bfloat16)
    hidden_share = (hidden.astype(jnp.float32) * share[:, :, None]).astype(jnp.bfloat16)
    mixture = jnp.einsum(
        "tef,efd->td", hidden_share, down_w, preferred_element_type=jnp.float32
    )
    grad_out = out_grad.astype(jnp.float32)
    hidden_grad = (
        jnp.einsum("td,efd->tef", grad_rows, down_w, preferred_element_type=jnp.float32)
        * share[:, :, None]
    )
    gate_back = (hidden_grad * up_val * sigma * (1.0 + gate_val * (1.0 - sigma))).astype(
        jnp.bfloat16
    )
    up_back = (hidden_grad * active).astype(jnp.bfloat16)
    ffn_in_grad = jnp.einsum(
        "tef,edf->td", gate_back, gate_w, preferred_element_type=jnp.float32
    ) + jnp.einsum("tef,edf->td", up_back, up_w, preferred_element_type=jnp.float32)
    gate_part = jnp.einsum("td,tef->edf", ffn_rows, gate_back, preferred_element_type=jnp.float32)
    up_part = jnp.einsum("td,tef->edf", ffn_rows, up_back, preferred_element_type=jnp.float32)
    down_part = jnp.einsum(
        "tef,td->efd", hidden_share, grad_rows, preferred_element_type=jnp.float32
    )
    ffn_in_own = tp_scatter_sum(ffn_in_grad, tp_size, jnp.bfloat16)
    _, second_back = jax.vjp(rms_norm, residual, gain_ffn)
    residual_norm_grad, ffn_gain_part = second_back(ffn_in_own)
    residual_grad = grad_out + residual_norm_grad
    gate_grad, up_grad, down_grad = (
        lax.psum_scatter(
            part.astype(jnp.bfloat16), "fsdp", scatter_dimension=0, tiled=True
        ).astype(jnp.float32)
        for part in (gate_part, up_part, down_part)
    )
    attn_out_grad = tp_gather(residual_grad.astype(jnp.bfloat16), tp_size)
    attn_out_grad, mixture = lax.optimization_barrier((attn_out_grad, mixture))
    mixture_own = tp_scatter_sum(mixture, tp_size, jnp.bfloat16)
    layer_out = (residual + mixture_own).astype(jnp.bfloat16)
    output_part = jnp.einsum(
        "gq,gd->qd", context_b, attn_out_grad, preferred_element_type=jnp.float32
    )
    context_grad = (
        jnp.einsum("gd,qd->gq", attn_out_grad, out_w, preferred_element_type=jnp.float32)
        .astype(jnp.bfloat16)
        .reshape(seq_count, SEQ, per_dev, HD)
    )

    def attend_back(operands):
        queries, keys_b, values_b, attn_probs, ctx_grad = operands
        value_grad = jnp.einsum(
            "hqk,qhd->kd",
            attn_probs.astype(jnp.bfloat16),
            ctx_grad,
            preferred_element_type=jnp.float32,
        )
        probs_grad = jnp.einsum(
            "qhd,kd->hqk", ctx_grad, values_b, preferred_element_type=jnp.float32
        )
        scores_grad = (
            attn_probs * (probs_grad - jnp.sum(attn_probs * probs_grad, axis=-1, keepdims=True))
        ).astype(jnp.bfloat16)
        query_grad = (
            jnp.einsum("hqk,kd->qhd", scores_grad, keys_b, preferred_element_type=jnp.float32)
            * factor
        )
        key_grad = (
            jnp.einsum("hqk,qhd->kd", scores_grad, queries, preferred_element_type=jnp.float32)
            * factor
        )
        return (query_grad, key_grad, value_grad)

    query_norm_grad, key_norm_grad, value_grad = lax.map(
        attend_back, (query_seq, key_seq, value_seq, probs_all, context_grad)
    )
    query_raw_grad, key_raw_grad, query_gain_part, key_gain_part = prepare_back(
        (query_norm_grad.reshape(group_rows, per_dev, HD), key_norm_grad.reshape(group_rows, HD))
    )
    query_back = query_raw_grad.astype(jnp.bfloat16)
    key_back = key_raw_grad.astype(jnp.bfloat16)
    value_back = value_grad.reshape(group_rows, HD).astype(jnp.bfloat16)
    result = jnp.einsum("gq,dq->gd", query_back, query_w, preferred_element_type=jnp.float32)
    result = result + jnp.einsum("gk,dk->gd", key_back, key_w, preferred_element_type=jnp.float32)
    attn_in_part = result + jnp.einsum(
        "gk,dk->gd", value_back, value_w, preferred_element_type=jnp.float32
    )
    attn_in_part, down_grad, gate_grad, up_grad = lax.optimization_barrier(
        (attn_in_part, down_grad, gate_grad, up_grad)
    )
    attn_in_grad = tp_scatter_sum(attn_in_part, tp_size, jnp.bfloat16)
    query_part = jnp.einsum("gd,gq->dq", attn_rows, query_back, preferred_element_type=jnp.float32)
    key_head_part = jnp.einsum("gd,gk->dk", attn_rows, key_back, preferred_element_type=jnp.float32)
    value_head_part = jnp.einsum(
        "gd,gk->dk", attn_rows, value_back, preferred_element_type=jnp.float32
    )
    _, first_back = jax.vjp(rms_norm, tokens_f, gain_attn)
    input_norm_grad, _ = first_back(attn_in_grad)
    _, rows_back = jax.vjp(
        lambda weight: rms_norm(layer_rows.astype(jnp.float32), weight), gain_attn
    )
    (attn_gain_part,) = rows_back(attn_in_part)
    in_grad = residual_grad + input_norm_grad
    fsdp_size = lax.axis_size("fsdp")
    query_proj_grad = jnp.sum(
        lax.all_to_all(
            query_part.astype(jnp.bfloat16).reshape(fsdp_size, -1, query_part.shape[1]),
            "fsdp",
            split_axis=0,
            concat_axis=0,
            tiled=True,
        ).astype(jnp.float32),
        axis=0,
    )
    output_proj_grad = jnp.sum(
        lax.all_to_all(
            output_part.astype(jnp.bfloat16)
            .reshape(output_part.shape[0], fsdp_size, -1)
            .transpose(1, 0, 2),
            "fsdp",
            split_axis=0,
            concat_axis=0,
            tiled=True,
        ).astype(jnp.float32),
        axis=0,
    )
    device_count = fsdp_size * tp_size
    gain_parts = (attn_gain_part, query_gain_part, key_gain_part, ffn_gain_part)
    gain_table = jnp.concatenate(
        [part.reshape(device_count, -1) for part in gain_parts], axis=1
    )
    gain_width = gain_table.shape[1]
    kv_full = jnp.concatenate([key_head_part, value_head_part], axis=1)
    block_rows = kv_full.shape[0] // fsdp_size
    sub_rows = block_rows // tp_size
    gain_rows = -(-(tp_size * gain_width) // (8 * 2 * HD)) * 8
    gain_block = jnp.pad(
        gain_table.reshape(fsdp_size, tp_size * gain_width),
        ((0, 0), (0, gain_rows * 2 * HD - tp_size * gain_width)),
    ).reshape(fsdp_size, gain_rows, 2 * HD)
    combined = jnp.concatenate(
        [kv_full.reshape(fsdp_size, block_rows, 2 * HD), gain_block], axis=1
    ).reshape(fsdp_size * (block_rows + gain_rows), 2 * HD)
    summed = lax.psum_scatter(combined, "fsdp", scatter_dimension=0, tiled=True)
    summed = jnp.concatenate(
        [
            summed[:block_rows].reshape(-1),
            summed[block_rows:].reshape(-1)[: tp_size * gain_width],
        ]
    )
    kv_local = summed[: block_rows * 2 * HD].reshape(tp_size, sub_rows * 2 * HD)
    gain_local = summed[block_rows * 2 * HD :].reshape(tp_size, gain_width)
    got = lax.all_to_all(
        jnp.concatenate([kv_local, gain_local], axis=1),
        "tp",
        split_axis=0,
        concat_axis=0,
        tiled=True,
    )
    kv_got = got[:, : sub_rows * 2 * HD].reshape(tp_size, sub_rows, 2 * HD)
    kv_got = jnp.sum(kv_got.reshape(HK, tp_size // HK, sub_rows, 2 * HD), axis=1)
    key_proj_grad = kv_got[:, :, :HD].transpose(1, 0, 2).reshape(sub_rows, HK * HD)
    value_proj_grad = kv_got[:, :, HD:].transpose(1, 0, 2).reshape(sub_rows, HK * HD)
    gain_sum = jnp.sum(got[:, sub_rows * 2 * HD :], axis=0)
    gain_grads = []
    offset = 0
    for part in gain_parts:
        size = part.shape[0] // device_count
        gain_grads.append(gain_sum[offset : offset + size])
        offset += size
    attn_gain_grad, query_gain_grad, key_gain_grad, ffn_gain_grad = gain_grads
    return (
        layer_out,
        in_grad,
        query_proj_grad,
        key_proj_grad,
        value_proj_grad,
        output_proj_grad,
        attn_gain_grad,
        query_gain_grad,
        key_gain_grad,
        ffn_gain_grad,
        gate_grad,
        up_grad,
        down_grad,
    )


def solution(mesh):
    in_specs = (
        P(("fsdp", "tp"), None),
        P("fsdp", "tp"),
        P(("fsdp", "tp"), None),
        P(("fsdp", "tp"), None),
        P("tp", "fsdp"),
        P(("fsdp", "tp")),
        P(("fsdp", "tp")),
        P(("fsdp", "tp")),
        P(("fsdp", "tp")),
        P("fsdp", None, "tp"),
        P("fsdp", None, "tp"),
        P("fsdp", "tp", None),
        P("fsdp", None),
        P("fsdp", None),
        P("fsdp"),
        P(("fsdp", "tp"), None),
    )
    out_specs = (
        P(("fsdp", "tp"), None),
        P(("fsdp", "tp"), None),
        P("fsdp", "tp"),
        P(("fsdp", "tp"), None),
        P(("fsdp", "tp"), None),
        P("tp", "fsdp"),
        P(("fsdp", "tp")),
        P(("fsdp", "tp")),
        P(("fsdp", "tp")),
        P(("fsdp", "tp")),
        P("fsdp", None, "tp"),
        P("fsdp", None, "tp"),
        P("fsdp", "tp", None),
    )
    return jax.shard_map(body, mesh=mesh, in_specs=in_specs, out_specs=out_specs, check_vma=False)
```

```python
import math

import jax
import jax.numpy as jnp
from jax import lax
from jax.sharding import PartitionSpec as P

HQ = 32
HK = 4
HD = 128
TOP = 8
SEQ = 1024


EPSILON = 1e-06


def rms_norm(values, weight):
    return values * lax.rsqrt(jnp.mean(values * values, axis=-1, keepdims=True) + EPSILON) * weight


def rotate(values, cosine, sine):
    half_width = values.shape[-1] // 2
    first_half = values[..., :half_width]
    second_half = values[..., half_width:]
    return jnp.concatenate(
        [first_half * cosine - second_half * sine, second_half * cosine + first_half * sine],
        axis=-1,
    )


def rotary_tables(positions, width):
    half_width = width // 2
    inverse = jnp.exp(
        -math.log(1000000.0) * 2.0 * jnp.arange(half_width, dtype=jnp.float32) / width
    )
    angles = positions[:, None] * inverse[None, :]
    return (jnp.cos(angles), jnp.sin(angles))


def masked_scores(queries, keys_b, prefix_end, factor):
    scores = jnp.einsum("qhd,kd->hqk", queries, keys_b, preferred_element_type=jnp.float32) * factor
    position = lax.iota(jnp.int32, queries.shape[0])
    allowed = (position[None, :] <= position[:, None]) | (position[None, :] < prefix_end)
    return jnp.where(allowed[None], scores, -1e30)


def tp_gather(block, count):
    place = lax.axis_index("tp")
    from_left = []
    from_right = []
    going_right = block
    going_left = block
    for step in range(1, count):
        going_right = lax.ppermute(
            going_right, "tp", [(i, i + 1) for i in range(step - 1, count - 1)]
        )
        going_left = lax.ppermute(going_left, "tp", [(i + 1, i) for i in range(0, count - step)])
        from_left.append(going_right)
        from_right.append(going_left)
    stacked = jnp.stack(from_left[::-1] + [block] + from_right, axis=0)
    picked = lax.dynamic_slice_in_dim(stacked, count - 1 - place, count, 0)
    return picked.reshape((count * block.shape[0],) + block.shape[1:])


def tp_scatter_sum(partial, count, send_type):
    place = lax.axis_index("tp")
    rows = partial.shape[0] // count
    pieces = partial.reshape((count, rows) + partial.shape[1:])

    def piece(target):
        return lax.dynamic_index_in_dim(pieces, jnp.clip(target, 0, count - 1), 0, keepdims=False)

    left_sum = None
    right_sum = None
    for step in range(1, count):
        outgoing = piece(place + count - step)
        if left_sum is not None:
            outgoing = outgoing + left_sum.astype(outgoing.dtype)
        left_sum = lax.ppermute(
            outgoing.astype(send_type), "tp", [(i, i + 1) for i in range(step)]
        )
        outgoing = piece(place - count + step)
        if right_sum is not None:
            outgoing = outgoing + right_sum.astype(outgoing.dtype)
        right_sum = lax.ppermute(
            outgoing.astype(send_type), "tp", [(i, i - 1) for i in range(count - step, count)]
        )
    own = piece(place)
    if left_sum is not None:
        own = own + left_sum.astype(own.dtype) + right_sum.astype(own.dtype)
    return own


def body(
    layer_in,
    query_proj,
    key_proj,
    value_proj,
    output_proj,
    attn_gain,
    query_gain,
    key_gain,
    ffn_gain,
    expert_gate,
    expert_up,
    expert_down,
    routes,
    route_weights,
    prefix_len,
    out_grad,
):
    tok_rows = layer_in.shape[0]
    width = layer_in.shape[1]
    group_rows = tok_rows * lax.axis_size("tp")
    seq_count = group_rows // SEQ
    factor = 1.0 / math.sqrt(HD)
    gain_sizes = (attn_gain.shape[0], query_gain.shape[0], key_gain.shape[0], ffn_gain.shape[0])
    kv_rows, kv_width = key_proj.shape
    gain_row = jnp.concatenate([attn_gain, query_gain, key_gain, ffn_gain])
    gain_block = jnp.zeros((8, 2 * kv_width), jnp.bfloat16).at[0, : gain_row.shape[0]].set(gain_row)
    packed = jnp.concatenate(
        [jnp.concatenate([key_proj, value_proj], axis=1), gain_block], axis=0
    )
    packed_all = lax.all_gather(packed, ("fsdp", "tp"), axis=0, tiled=False)
    kv_all = packed_all[:, :kv_rows].reshape(-1, 2 * kv_width)
    key_all = kv_all[:, :kv_width]
    value_all = kv_all[:, kv_width:]
    gain_all = packed_all[:, kv_rows]
    gains = []
    offset = 0
    for size in gain_sizes:
        gains.append(gain_all[:, offset : offset + size].reshape(-1))
        offset += size
    gain_attn, gain_query, gain_key, gain_ffn = gains
    gain_attn = gain_attn.astype(jnp.float32)
    gain_query = gain_query.astype(jnp.float32)
    gain_key = gain_key.astype(jnp.float32)
    gain_ffn = gain_ffn.astype(jnp.float32)
    query_w, out_w, gate_w, up_w, down_w = (
        lax.all_gather(query_proj, "fsdp", axis=0, tiled=True),
        lax.all_gather(output_proj, "fsdp", axis=1, tiled=True),
        lax.all_gather(expert_gate, "fsdp", axis=0, tiled=True),
        lax.all_gather(expert_up, "fsdp", axis=0, tiled=True),
        lax.all_gather(expert_down, "fsdp", axis=0, tiled=True),
    )
    per_dev = query_w.shape[1] // HD
    kv_head = lax.axis_index("tp") * per_dev // (HQ // HK)
    key_w = lax.dynamic_slice_in_dim(key_all, kv_head * HD, HD, 1)
    value_w = lax.dynamic_slice_in_dim(value_all, kv_head * HD, HD, 1)
    tokens_f = layer_in.astype(jnp.float32)
    tp_size = lax.axis_size("tp")
    layer_rows = tp_gather(layer_in, tp_size)
    attn_rows = rms_norm(layer_rows.astype(jnp.float32), gain_attn).astype(jnp.bfloat16)
    out_grad, attn_rows = lax.optimization_barrier((out_grad, attn_rows))
    grad_rows = tp_gather(out_grad, tp_size)
    query_raw = jnp.dot(attn_rows, query_w, preferred_element_type=jnp.float32)
    key_raw = jnp.dot(attn_rows, key_w, preferred_element_type=jnp.float32)
    value_rows = jnp.dot(attn_rows, value_w, preferred_element_type=jnp.float32).astype(
        jnp.bfloat16
    )
    cosine, sine = rotary_tables((lax.iota(jnp.int32, group_rows) % SEQ).astype(jnp.float32), HD)

    def prepare(query_in, key_in, weight_query, weight_key):
        query_heads = rms_norm(query_in.reshape(group_rows, per_dev, HD), weight_query)
        return (
            rotate(query_heads, cosine[:, None, :], sine[:, None, :]),
            rotate(rms_norm(key_in, weight_key), cosine, sine),
        )

    (query_norm, key_norm), prepare_back = jax.vjp(
        prepare, query_raw, key_raw, gain_query, gain_key
    )
    query_seq = query_norm.astype(jnp.bfloat16).reshape(seq_count, SEQ, per_dev, HD)
    key_seq = key_norm.astype(jnp.bfloat16).reshape(seq_count, SEQ, HD)
    value_seq = value_rows.reshape(seq_count, SEQ, HD)

    def attend(operands):
        queries, keys_b, values_b, prefix_end = operands
        scores = masked_scores(queries, keys_b, prefix_end, factor)
        highest = jnp.max(scores, axis=-1, keepdims=True)
        expo = jnp.exp(scores - highest)
        denom = jnp.sum(expo, axis=-1, keepdims=True)
        probs_full = expo / denom
        context = jnp.einsum(
            "hqk,kd->qhd",
            probs_full.astype(jnp.bfloat16),
            values_b,
            preferred_element_type=jnp.float32,
        )
        return (context, probs_full)

    context_all, probs_all = lax.map(attend, (query_seq, key_seq, value_seq, prefix_len))
    context_b = context_all.reshape(group_rows, per_dev * HD).astype(jnp.bfloat16)
    attn_out = tp_scatter_sum(
        jnp.dot(context_b, out_w, preferred_element_type=jnp.float32), tp_size, jnp.bfloat16
    )
    residual = tokens_f + attn_out
    ffn_in = rms_norm(residual, gain_ffn).astype(jnp.bfloat16)
    ffn_rows = tp_gather(ffn_in, tp_size)
    expert_count = gate_w.shape[0]
    chosen = routes[:, :, None] == lax.iota(jnp.int32, expert_count)[None, None, :]
    share = jnp.sum(jnp.where(chosen, route_weights[:, :, None], 0.0), axis=1)
    gate_val = jnp.einsum("td,edf->tef", ffn_rows, gate_w, preferred_element_type=jnp.float32)
    up_val = jnp.einsum("td,edf->tef", ffn_rows, up_w, preferred_element_type=jnp.float32)
    sigma = jax.nn.sigmoid(gate_val)
    active = gate_val * sigma
    hidden = (active * up_val).astype(jnp.bfloat16)
    hidden_share = (hidden.astype(jnp.float32) * share[:, :, None]).astype(jnp.bfloat16)
    mixture = jnp.einsum(
        "tef,efd->td", hidden_share, down_w, preferred_element_type=jnp.float32
    )
    grad_out = out_grad.astype(jnp.float32)
    hidden_grad = (
        jnp.einsum("td,efd->tef", grad_rows, down_w, preferred_element_type=jnp.float32)
        * share[:, :, None]
    )
    gate_back = (hidden_grad * up_val * sigma * (1.0 + gate_val * (1.0 - sigma))).astype(
        jnp.bfloat16
    )
    up_back = (hidden_grad * active).astype(jnp.bfloat16)
    ffn_in_grad = jnp.einsum(
        "tef,edf->td", gate_back, gate_w, preferred_element_type=jnp.float32
    ) + jnp.einsum("tef,edf->td", up_back, up_w, preferred_element_type=jnp.float32)
    gate_part = jnp.einsum("td,tef->edf", ffn_rows, gate_back, preferred_element_type=jnp.float32)
    up_part = jnp.einsum("td,tef->edf", ffn_rows, up_back, preferred_element_type=jnp.float32)
    down_part = jnp.einsum(
        "tef,td->efd", hidden_share, grad_rows, preferred_element_type=jnp.float32
    )
    ffn_in_own = tp_scatter_sum(ffn_in_grad, tp_size, jnp.bfloat16)
    _, second_back = jax.vjp(rms_norm, residual, gain_ffn)
    residual_norm_grad, ffn_gain_part = second_back(ffn_in_own)
    residual_grad = grad_out + residual_norm_grad
    gate_grad, up_grad, down_grad = (
        lax.psum_scatter(
            part.astype(jnp.bfloat16), "fsdp", scatter_dimension=0, tiled=True
        ).astype(jnp.float32)
        for part in (gate_part, up_part, down_part)
    )
    attn_out_grad = tp_gather(residual_grad.astype(jnp.bfloat16), tp_size)
    attn_out_grad, mixture = lax.optimization_barrier((attn_out_grad, mixture))
    mixture_own = tp_scatter_sum(mixture, tp_size, jnp.bfloat16)
    layer_out = (residual + mixture_own).astype(jnp.bfloat16)
    output_part = jnp.einsum(
        "gq,gd->qd", context_b, attn_out_grad, preferred_element_type=jnp.float32
    )
    context_grad = (
        jnp.einsum("gd,qd->gq", attn_out_grad, out_w, preferred_element_type=jnp.float32)
        .astype(jnp.bfloat16)
        .reshape(seq_count, SEQ, per_dev, HD)
    )

    def attend_back(operands):
        queries, keys_b, values_b, attn_probs, ctx_grad = operands
        value_grad = jnp.einsum(
            "hqk,qhd->kd",
            attn_probs.astype(jnp.bfloat16),
            ctx_grad,
            preferred_element_type=jnp.float32,
        )
        probs_grad = jnp.einsum(
            "qhd,kd->hqk", ctx_grad, values_b, preferred_element_type=jnp.float32
        )
        scores_grad = (
            attn_probs * (probs_grad - jnp.sum(attn_probs * probs_grad, axis=-1, keepdims=True))
        ).astype(jnp.bfloat16)
        query_grad = (
            jnp.einsum("hqk,kd->qhd", scores_grad, keys_b, preferred_element_type=jnp.float32)
            * factor
        )
        key_grad = (
            jnp.einsum("hqk,qhd->kd", scores_grad, queries, preferred_element_type=jnp.float32)
            * factor
        )
        return (query_grad, key_grad, value_grad)

    query_norm_grad, key_norm_grad, value_grad = lax.map(
        attend_back, (query_seq, key_seq, value_seq, probs_all, context_grad)
    )
    query_raw_grad, key_raw_grad, query_gain_part, key_gain_part = prepare_back(
        (query_norm_grad.reshape(group_rows, per_dev, HD), key_norm_grad.reshape(group_rows, HD))
    )
    query_back = query_raw_grad.astype(jnp.bfloat16)
    key_back = key_raw_grad.astype(jnp.bfloat16)
    value_back = value_grad.reshape(group_rows, HD).astype(jnp.bfloat16)
    result = jnp.einsum("gq,dq->gd", query_back, query_w, preferred_element_type=jnp.float32)
    result = result + jnp.einsum("gk,dk->gd", key_back, key_w, preferred_element_type=jnp.float32)
    attn_in_part = result + jnp.einsum(
        "gk,dk->gd", value_back, value_w, preferred_element_type=jnp.float32
    )
    attn_in_part, down_grad, gate_grad, up_grad = lax.optimization_barrier(
        (attn_in_part, down_grad, gate_grad, up_grad)
    )
    attn_in_grad = tp_scatter_sum(attn_in_part, tp_size, jnp.bfloat16)
    query_part = jnp.einsum("gd,gq->dq", attn_rows, query_back, preferred_element_type=jnp.float32)
    key_head_part = jnp.einsum("gd,gk->dk", attn_rows, key_back, preferred_element_type=jnp.float32)
    value_head_part = jnp.einsum(
        "gd,gk->dk", attn_rows, value_back, preferred_element_type=jnp.float32
    )
    _, first_back = jax.vjp(rms_norm, tokens_f, gain_attn)
    input_norm_grad, _ = first_back(attn_in_grad)
    _, rows_back = jax.vjp(
        lambda weight: rms_norm(layer_rows.astype(jnp.float32), weight), gain_attn
    )
    (attn_gain_part,) = rows_back(attn_in_part)
    in_grad = residual_grad + input_norm_grad
    fsdp_size = lax.axis_size("fsdp")
    query_proj_grad = jnp.sum(
        lax.all_to_all(
            query_part.astype(jnp.bfloat16).reshape(fsdp_size, -1, query_part.shape[1]),
            "fsdp",
            split_axis=0,
            concat_axis=0,
            tiled=True,
        ).astype(jnp.float32),
        axis=0,
    )
    output_proj_grad = jnp.sum(
        lax.all_to_all(
            output_part.astype(jnp.bfloat16)
            .reshape(output_part.shape[0], fsdp_size, -1)
            .transpose(1, 0, 2),
            "fsdp",
            split_axis=0,
            concat_axis=0,
            tiled=True,
        ).astype(jnp.float32),
        axis=0,
    )
    device_count = fsdp_size * tp_size
    gain_parts = (attn_gain_part, query_gain_part, key_gain_part, ffn_gain_part)
    gain_table = jnp.concatenate(
        [part.reshape(device_count, -1) for part in gain_parts], axis=1
    )
    gain_width = gain_table.shape[1]
    kv_full = jnp.concatenate([key_head_part, value_head_part], axis=1)
    block_rows = kv_full.shape[0] // fsdp_size
    sub_rows = block_rows // tp_size
    gain_rows = -(-(tp_size * gain_width) // (8 * 2 * HD)) * 8
    gain_block = jnp.pad(
        gain_table.reshape(fsdp_size, tp_size * gain_width),
        ((0, 0), (0, gain_rows * 2 * HD - tp_size * gain_width)),
    ).reshape(fsdp_size, gain_rows, 2 * HD)
    combined = jnp.concatenate(
        [kv_full.reshape(fsdp_size, block_rows, 2 * HD), gain_block], axis=1
    ).reshape(fsdp_size * (block_rows + gain_rows), 2 * HD)
    summed = lax.psum_scatter(combined, "fsdp", scatter_dimension=0, tiled=True)
    summed = jnp.concatenate(
        [
            summed[:block_rows].reshape(-1),
            summed[block_rows:].reshape(-1)[: tp_size * gain_width],
        ]
    )
    kv_local = summed[: block_rows * 2 * HD].reshape(tp_size, sub_rows * 2 * HD)
    gain_local = summed[block_rows * 2 * HD :].reshape(tp_size, gain_width)
    got = lax.all_to_all(
        jnp.concatenate([kv_local, gain_local], axis=1),
        "tp",
        split_axis=0,
        concat_axis=0,
        tiled=True,
    )
    kv_got = got[:, : sub_rows * 2 * HD].reshape(tp_size, sub_rows, 2 * HD)
    kv_got = jnp.sum(kv_got.reshape(HK, tp_size // HK, sub_rows, 2 * HD), axis=1)
    key_proj_grad = kv_got[:, :, :HD].transpose(1, 0, 2).reshape(sub_rows, HK * HD)
    value_proj_grad = kv_got[:, :, HD:].transpose(1, 0, 2).reshape(sub_rows, HK * HD)
    gain_sum = jnp.sum(got[:, sub_rows * 2 * HD :], axis=0)
    gain_grads = []
    offset = 0
    for part in gain_parts:
        size = part.shape[0] // device_count
        gain_grads.append(gain_sum[offset : offset + size])
        offset += size
    attn_gain_grad, query_gain_grad, key_gain_grad, ffn_gain_grad = gain_grads
    return (
        layer_out,
        in_grad,
        query_proj_grad,
        key_proj_grad,
        value_proj_grad,
        output_proj_grad,
        attn_gain_grad,
        query_gain_grad,
        key_gain_grad,
        ffn_gain_grad,
        gate_grad,
        up_grad,
        down_grad,
    )


def solution(mesh):
    in_specs = (
        P(("fsdp", "tp"), None),
        P("fsdp", "tp"),
        P(("fsdp", "tp"), None),
        P(("fsdp", "tp"), None),
        P("tp", "fsdp"),
        P(("fsdp", "tp")),
        P(("fsdp", "tp")),
        P(("fsdp", "tp")),
        P(("fsdp", "tp")),
        P("fsdp", None, "tp"),
        P("fsdp", None, "tp"),
        P("fsdp", "tp", None),
        P("fsdp", None),
        P("fsdp", None),
        P("fsdp"),
        P(("fsdp", "tp"), None),
    )
    out_specs = (
        P(("fsdp", "tp"), None),
        P(("fsdp", "tp"), None),
        P("fsdp", "tp"),
        P(("fsdp", "tp"), None),
        P(("fsdp", "tp"), None),
        P("tp", "fsdp"),
        P(("fsdp", "tp")),
        P(("fsdp", "tp")),
        P(("fsdp", "tp")),
        P(("fsdp", "tp")),
        P("fsdp", None, "tp"),
        P("fsdp", None, "tp"),
        P("fsdp", "tp", None),
    )
    return jax.shard_map(body, mesh=mesh, in_specs=in_specs, out_specs=out_specs, check_vma=False)
```

```python
import math

import jax
import jax.numpy as jnp
from jax import lax
from jax.sharding import PartitionSpec as P

HQ = 32
HK = 4
HD = 128
TOP = 8
SEQ = 1024


EPSILON = 1e-06


def rms_norm(values, weight):
    return values * lax.rsqrt(jnp.mean(values * values, axis=-1, keepdims=True) + EPSILON) * weight


def rotate(values, cosine, sine):
    half_width = values.shape[-1] // 2
    first_half = values[..., :half_width]
    second_half = values[..., half_width:]
    return jnp.concatenate(
        [first_half * cosine - second_half * sine, second_half * cosine + first_half * sine],
        axis=-1,
    )


def rotary_tables(positions, width):
    half_width = width // 2
    inverse = jnp.exp(
        -math.log(1000000.0) * 2.0 * jnp.arange(half_width, dtype=jnp.float32) / width
    )
    angles = positions[:, None] * inverse[None, :]
    return (jnp.cos(angles), jnp.sin(angles))


def masked_scores(queries, keys_b, prefix_end, factor):
    scores = jnp.einsum("qhd,kd->hqk", queries, keys_b, preferred_element_type=jnp.float32) * factor
    position = lax.iota(jnp.int32, queries.shape[0])
    allowed = (position[None, :] <= position[:, None]) | (position[None, :] < prefix_end)
    return jnp.where(allowed[None], scores, -1e30)


def tp_gather(block, count):
    place = lax.axis_index("tp")
    from_left = []
    from_right = []
    going_right = block
    going_left = block
    for step in range(1, count):
        going_right = lax.ppermute(
            going_right, "tp", [(i, i + 1) for i in range(step - 1, count - 1)]
        )
        going_left = lax.ppermute(going_left, "tp", [(i + 1, i) for i in range(0, count - step)])
        from_left.append(going_right)
        from_right.append(going_left)
    stacked = jnp.stack(from_left[::-1] + [block] + from_right, axis=0)
    picked = lax.dynamic_slice_in_dim(stacked, count - 1 - place, count, 0)
    return picked.reshape((count * block.shape[0],) + block.shape[1:])


def tp_scatter_sum(partial, count, send_type):
    place = lax.axis_index("tp")
    rows = partial.shape[0] // count
    pieces = partial.reshape((count, rows) + partial.shape[1:])

    def piece(target):
        return lax.dynamic_index_in_dim(pieces, jnp.clip(target, 0, count - 1), 0, keepdims=False)

    left_sum = None
    right_sum = None
    for step in range(1, count):
        outgoing = piece(place + count - step)
        if left_sum is not None:
            outgoing = outgoing + left_sum.astype(outgoing.dtype)
        left_sum = lax.ppermute(
            outgoing.astype(send_type), "tp", [(i, i + 1) for i in range(step)]
        )
        outgoing = piece(place - count + step)
        if right_sum is not None:
            outgoing = outgoing + right_sum.astype(outgoing.dtype)
        right_sum = lax.ppermute(
            outgoing.astype(send_type), "tp", [(i, i - 1) for i in range(count - step, count)]
        )
    own = piece(place)
    if left_sum is not None:
        own = own + left_sum.astype(own.dtype) + right_sum.astype(own.dtype)
    return own


def body(
    layer_in,
    query_proj,
    key_proj,
    value_proj,
    output_proj,
    attn_gain,
    query_gain,
    key_gain,
    ffn_gain,
    expert_gate,
    expert_up,
    expert_down,
    routes,
    route_weights,
    prefix_len,
    out_grad,
):
    tok_rows = layer_in.shape[0]
    width = layer_in.shape[1]
    group_rows = tok_rows * lax.axis_size("tp")
    seq_count = group_rows // SEQ
    factor = 1.0 / math.sqrt(HD)
    gain_sizes = (attn_gain.shape[0], query_gain.shape[0], key_gain.shape[0], ffn_gain.shape[0])
    kv_rows, kv_width = key_proj.shape
    gain_row = jnp.concatenate([attn_gain, query_gain, key_gain, ffn_gain])
    gain_block = jnp.zeros((8, 2 * kv_width), jnp.bfloat16).at[0, : gain_row.shape[0]].set(gain_row)
    packed = jnp.concatenate(
        [jnp.concatenate([key_proj, value_proj], axis=1), gain_block], axis=0
    )
    packed_all = lax.all_gather(packed, ("fsdp", "tp"), axis=0, tiled=False)
    kv_all = packed_all[:, :kv_rows].reshape(-1, 2 * kv_width)
    key_all = kv_all[:, :kv_width]
    value_all = kv_all[:, kv_width:]
    gain_all = packed_all[:, kv_rows]
    gains = []
    offset = 0
    for size in gain_sizes:
        gains.append(gain_all[:, offset : offset + size].reshape(-1))
        offset += size
    gain_attn, gain_query, gain_key, gain_ffn = gains
    gain_attn = gain_attn.astype(jnp.float32)
    gain_query = gain_query.astype(jnp.float32)
    gain_key = gain_key.astype(jnp.float32)
    gain_ffn = gain_ffn.astype(jnp.float32)
    query_w, out_w, gate_w, up_w, down_w = (
        lax.all_gather(query_proj, "fsdp", axis=0, tiled=True),
        lax.all_gather(output_proj, "fsdp", axis=1, tiled=True),
        lax.all_gather(expert_gate, "fsdp", axis=0, tiled=True),
        lax.all_gather(expert_up, "fsdp", axis=0, tiled=True),
        lax.all_gather(expert_down, "fsdp", axis=0, tiled=True),
    )
    per_dev = query_w.shape[1] // HD
    kv_head = lax.axis_index("tp") * per_dev // (HQ // HK)
    key_w = lax.dynamic_slice_in_dim(key_all, kv_head * HD, HD, 1)
    value_w = lax.dynamic_slice_in_dim(value_all, kv_head * HD, HD, 1)
    tokens_f = layer_in.astype(jnp.float32)
    tp_size = lax.axis_size("tp")
    layer_rows = tp_gather(layer_in, tp_size)
    attn_rows = rms_norm(layer_rows.astype(jnp.float32), gain_attn).astype(jnp.bfloat16)
    out_grad, attn_rows = lax.optimization_barrier((out_grad, attn_rows))
    grad_rows = tp_gather(out_grad, tp_size)
    query_raw = jnp.dot(attn_rows, query_w, preferred_element_type=jnp.float32)
    key_raw = jnp.dot(attn_rows, key_w, preferred_element_type=jnp.float32)
    value_rows = jnp.dot(attn_rows, value_w, preferred_element_type=jnp.float32).astype(
        jnp.bfloat16
    )
    cosine, sine = rotary_tables((lax.iota(jnp.int32, group_rows) % SEQ).astype(jnp.float32), HD)

    def prepare(query_in, key_in, weight_query, weight_key):
        query_heads = rms_norm(query_in.reshape(group_rows, per_dev, HD), weight_query)
        return (
            rotate(query_heads, cosine[:, None, :], sine[:, None, :]),
            rotate(rms_norm(key_in, weight_key), cosine, sine),
        )

    (query_norm, key_norm), prepare_back = jax.vjp(
        prepare, query_raw, key_raw, gain_query, gain_key
    )
    query_seq = query_norm.astype(jnp.bfloat16).reshape(seq_count, SEQ, per_dev, HD)
    key_seq = key_norm.astype(jnp.bfloat16).reshape(seq_count, SEQ, HD)
    value_seq = value_rows.reshape(seq_count, SEQ, HD)

    def attend(operands):
        queries, keys_b, values_b, prefix_end = operands
        scores = masked_scores(queries, keys_b, prefix_end, factor)
        highest = jnp.max(scores, axis=-1, keepdims=True)
        expo = jnp.exp(scores - highest)
        denom = jnp.sum(expo, axis=-1, keepdims=True)
        probs_full = expo / denom
        context = jnp.einsum(
            "hqk,kd->qhd",
            probs_full.astype(jnp.bfloat16),
            values_b,
            preferred_element_type=jnp.float32,
        )
        return (context, probs_full)

    context_all, probs_all = lax.map(attend, (query_seq, key_seq, value_seq, prefix_len))
    context_b = context_all.reshape(group_rows, per_dev * HD).astype(jnp.bfloat16)
    context_b, grad_rows = lax.optimization_barrier((context_b, grad_rows))
    attn_out = tp_scatter_sum(
        jnp.dot(context_b, out_w, preferred_element_type=jnp.float32), tp_size, jnp.bfloat16
    )
    residual = tokens_f + attn_out
    ffn_in = rms_norm(residual, gain_ffn).astype(jnp.bfloat16)
    ffn_rows = tp_gather(ffn_in, tp_size)
    expert_count = gate_w.shape[0]
    chosen = routes[:, :, None] == lax.iota(jnp.int32, expert_count)[None, None, :]
    share = jnp.sum(jnp.where(chosen, route_weights[:, :, None], 0.0), axis=1)
    gate_val = jnp.einsum("td,edf->tef", ffn_rows, gate_w, preferred_element_type=jnp.float32)
    up_val = jnp.einsum("td,edf->tef", ffn_rows, up_w, preferred_element_type=jnp.float32)
    sigma = jax.nn.sigmoid(gate_val)
    active = gate_val * sigma
    hidden = (active * up_val).astype(jnp.bfloat16)
    hidden_share = (hidden.astype(jnp.float32) * share[:, :, None]).astype(jnp.bfloat16)
    mixture = jnp.einsum(
        "tef,efd->td", hidden_share, down_w, preferred_element_type=jnp.float32
    )
    grad_out = out_grad.astype(jnp.float32)
    hidden_grad = (
        jnp.einsum("td,efd->tef", grad_rows, down_w, preferred_element_type=jnp.float32)
        * share[:, :, None]
    )
    gate_back = (hidden_grad * up_val * sigma * (1.0 + gate_val * (1.0 - sigma))).astype(
        jnp.bfloat16
    )
    up_back = (hidden_grad * active).astype(jnp.bfloat16)
    ffn_in_grad = jnp.einsum(
        "tef,edf->td", gate_back, gate_w, preferred_element_type=jnp.float32
    ) + jnp.einsum("tef,edf->td", up_back, up_w, preferred_element_type=jnp.float32)
    gate_part = jnp.einsum("td,tef->edf", ffn_rows, gate_back, preferred_element_type=jnp.float32)
    up_part = jnp.einsum("td,tef->edf", ffn_rows, up_back, preferred_element_type=jnp.float32)
    down_part = jnp.einsum(
        "tef,td->efd", hidden_share, grad_rows, preferred_element_type=jnp.float32
    )
    ffn_in_own = tp_scatter_sum(ffn_in_grad, tp_size, jnp.bfloat16)
    _, second_back = jax.vjp(rms_norm, residual, gain_ffn)
    residual_norm_grad, ffn_gain_part = second_back(ffn_in_own)
    residual_grad = grad_out + residual_norm_grad
    gate_grad, up_grad, down_grad = (
        lax.psum_scatter(
            part.astype(jnp.bfloat16), "fsdp", scatter_dimension=0, tiled=True
        ).astype(jnp.float32)
        for part in (gate_part, up_part, down_part)
    )
    attn_out_grad = tp_gather(residual_grad.astype(jnp.bfloat16), tp_size)
    attn_out_grad, mixture = lax.optimization_barrier((attn_out_grad, mixture))
    mixture_own = tp_scatter_sum(mixture, tp_size, jnp.bfloat16)
    layer_out = (residual + mixture_own).astype(jnp.bfloat16)
    output_part = jnp.einsum(
        "gq,gd->qd", context_b, attn_out_grad, preferred_element_type=jnp.float32
    )
    context_grad = (
        jnp.einsum("gd,qd->gq", attn_out_grad, out_w, preferred_element_type=jnp.float32)
        .astype(jnp.bfloat16)
        .reshape(seq_count, SEQ, per_dev, HD)
    )

    def attend_back(operands):
        queries, keys_b, values_b, attn_probs, ctx_grad = operands
        value_grad = jnp.einsum(
            "hqk,qhd->kd",
            attn_probs.astype(jnp.bfloat16),
            ctx_grad,
            preferred_element_type=jnp.float32,
        )
        probs_grad = jnp.einsum(
            "qhd,kd->hqk", ctx_grad, values_b, preferred_element_type=jnp.float32
        )
        scores_grad = (
            attn_probs * (probs_grad - jnp.sum(attn_probs * probs_grad, axis=-1, keepdims=True))
        ).astype(jnp.bfloat16)
        query_grad = (
            jnp.einsum("hqk,kd->qhd", scores_grad, keys_b, preferred_element_type=jnp.float32)
            * factor
        )
        key_grad = (
            jnp.einsum("hqk,qhd->kd", scores_grad, queries, preferred_element_type=jnp.float32)
            * factor
        )
        return (query_grad, key_grad, value_grad)

    query_norm_grad, key_norm_grad, value_grad = lax.map(
        attend_back, (query_seq, key_seq, value_seq, probs_all, context_grad)
    )
    query_raw_grad, key_raw_grad, query_gain_part, key_gain_part = prepare_back(
        (query_norm_grad.reshape(group_rows, per_dev, HD), key_norm_grad.reshape(group_rows, HD))
    )
    query_back = query_raw_grad.astype(jnp.bfloat16)
    key_back = key_raw_grad.astype(jnp.bfloat16)
    value_back = value_grad.reshape(group_rows, HD).astype(jnp.bfloat16)
    result = jnp.einsum("gq,dq->gd", query_back, query_w, preferred_element_type=jnp.float32)
    result = result + jnp.einsum("gk,dk->gd", key_back, key_w, preferred_element_type=jnp.float32)
    attn_in_part = result + jnp.einsum(
        "gk,dk->gd", value_back, value_w, preferred_element_type=jnp.float32
    )
    attn_in_part, down_grad, gate_grad, up_grad = lax.optimization_barrier(
        (attn_in_part, down_grad, gate_grad, up_grad)
    )
    attn_in_grad = tp_scatter_sum(attn_in_part, tp_size, jnp.bfloat16)
    query_part = jnp.einsum("gd,gq->dq", attn_rows, query_back, preferred_element_type=jnp.float32)
    key_head_part = jnp.einsum("gd,gk->dk", attn_rows, key_back, preferred_element_type=jnp.float32)
    value_head_part = jnp.einsum(
        "gd,gk->dk", attn_rows, value_back, preferred_element_type=jnp.float32
    )
    _, first_back = jax.vjp(rms_norm, tokens_f, gain_attn)
    input_norm_grad, _ = first_back(attn_in_grad)
    _, rows_back = jax.vjp(
        lambda weight: rms_norm(layer_rows.astype(jnp.float32), weight), gain_attn
    )
    (attn_gain_part,) = rows_back(attn_in_part)
    in_grad = residual_grad + input_norm_grad
    fsdp_size = lax.axis_size("fsdp")
    query_proj_grad = lax.psum_scatter(
        query_part.astype(jnp.bfloat16), "fsdp", scatter_dimension=0, tiled=True
    ).astype(jnp.float32)
    output_proj_grad = jnp.sum(
        lax.all_to_all(
            output_part.astype(jnp.bfloat16)
            .reshape(output_part.shape[0], fsdp_size, -1)
            .transpose(1, 0, 2),
            "fsdp",
            split_axis=0,
            concat_axis=0,
            tiled=True,
        ).astype(jnp.float32),
        axis=0,
    )
    device_count = fsdp_size * tp_size
    gain_parts = (attn_gain_part, query_gain_part, key_gain_part, ffn_gain_part)
    gain_table = jnp.concatenate(
        [part.reshape(device_count, -1) for part in gain_parts], axis=1
    )
    gain_width = gain_table.shape[1]
    kv_full = jnp.concatenate([key_head_part, value_head_part], axis=1)
    block_rows = kv_full.shape[0] // fsdp_size
    sub_rows = block_rows // tp_size
    gain_rows = -(-(tp_size * gain_width) // (8 * 2 * HD)) * 8
    gain_block = jnp.pad(
        gain_table.reshape(fsdp_size, tp_size * gain_width),
        ((0, 0), (0, gain_rows * 2 * HD - tp_size * gain_width)),
    ).reshape(fsdp_size, gain_rows, 2 * HD)
    combined = jnp.concatenate(
        [kv_full.reshape(fsdp_size, block_rows, 2 * HD), gain_block], axis=1
    ).reshape(fsdp_size * (block_rows + gain_rows), 2 * HD)
    summed = lax.psum_scatter(combined, "fsdp", scatter_dimension=0, tiled=True)
    summed = jnp.concatenate(
        [
            summed[:block_rows].reshape(-1),
            summed[block_rows:].reshape(-1)[: tp_size * gain_width],
        ]
    )
    kv_local = summed[: block_rows * 2 * HD].reshape(tp_size, sub_rows * 2 * HD)
    gain_local = summed[block_rows * 2 * HD :].reshape(tp_size, gain_width)
    got = lax.all_to_all(
        jnp.concatenate([kv_local, gain_local], axis=1),
        "tp",
        split_axis=0,
        concat_axis=0,
        tiled=True,
    )
    kv_got = got[:, : sub_rows * 2 * HD].reshape(tp_size, sub_rows, 2 * HD)
    kv_got = jnp.sum(kv_got.reshape(HK, tp_size // HK, sub_rows, 2 * HD), axis=1)
    key_proj_grad = kv_got[:, :, :HD].transpose(1, 0, 2).reshape(sub_rows, HK * HD)
    value_proj_grad = kv_got[:, :, HD:].transpose(1, 0, 2).reshape(sub_rows, HK * HD)
    gain_sum = jnp.sum(got[:, sub_rows * 2 * HD :], axis=0)
    gain_grads = []
    offset = 0
    for part in gain_parts:
        size = part.shape[0] // device_count
        gain_grads.append(gain_sum[offset : offset + size])
        offset += size
    attn_gain_grad, query_gain_grad, key_gain_grad, ffn_gain_grad = gain_grads
    return (
        layer_out,
        in_grad,
        query_proj_grad,
        key_proj_grad,
        value_proj_grad,
        output_proj_grad,
        attn_gain_grad,
        query_gain_grad,
        key_gain_grad,
        ffn_gain_grad,
        gate_grad,
        up_grad,
        down_grad,
    )


def solution(mesh):
    in_specs = (
        P(("fsdp", "tp"), None),
        P("fsdp", "tp"),
        P(("fsdp", "tp"), None),
        P(("fsdp", "tp"), None),
        P("tp", "fsdp"),
        P(("fsdp", "tp")),
        P(("fsdp", "tp")),
        P(("fsdp", "tp")),
        P(("fsdp", "tp")),
        P("fsdp", None, "tp"),
        P("fsdp", None, "tp"),
        P("fsdp", "tp", None),
        P("fsdp", None),
        P("fsdp", None),
        P("fsdp"),
        P(("fsdp", "tp"), None),
    )
    out_specs = (
        P(("fsdp", "tp"), None),
        P(("fsdp", "tp"), None),
        P("fsdp", "tp"),
        P(("fsdp", "tp"), None),
        P(("fsdp", "tp"), None),
        P("tp", "fsdp"),
        P(("fsdp", "tp")),
        P(("fsdp", "tp")),
        P(("fsdp", "tp")),
        P(("fsdp", "tp")),
        P("fsdp", None, "tp"),
        P("fsdp", None, "tp"),
        P("fsdp", "tp", None),
    )
    return jax.shard_map(body, mesh=mesh, in_specs=in_specs, out_specs=out_specs, check_vma=False)
```
